128 devices in a mesh: dp: 32 (over x, z, core), fsdp: 4 (over y).
Axes of the slice: x: 4, y: 4, z: 4, core: 2. Of those that a mesh axis runs over, the one named last changes fastest.
Arguments:
- latents: bfloat16 [2816, 8, 8, 320], P(('dp', 'fsdp')), may hold values from -6 to 6
- noise_draw: bfloat16 [2816, 8, 8, 320], P(('dp', 'fsdp')), may hold values from -6 to 6
- timesteps: int32 [2816], P(('dp', 'fsdp')), may hold values from 0 to 999
- buckets: int32 [2816], P(('dp', 'fsdp')), may hold values from 0 to 2
- owners: int32 [2816], P(('dp', 'fsdp')), may hold values from 0 to 31, as said below
- adv_grad: bfloat16 [2816, 8, 8, 320], P(('dp', 'fsdp')), may hold values from -6 to 6
- w_down: bfloat16 [2880, 640], P('fsdp'), may hold values from -0.109375 to 0.109375
- w_up: bfloat16 [5760, 320], P('fsdp'), may hold values from -0.078125 to 0.078125
- t_down: bfloat16 [2880, 640], P('fsdp'), may hold values from -0.109375 to 0.109375
- t_up: bfloat16 [5760, 320], P('fsdp'), may hold values from -0.078125 to 0.078125
Outputs:
- student_out: bfloat16 [2816, 8, 8, 320], P(('dp', 'fsdp'))
- grad_down: float32 [2880, 640], P('fsdp')
- grad_up: float32 [5760, 320], P('fsdp')
The draws below stay inside these ranges and needn't reach their ends.
Inputs may be any that keep to these rules, and one draw needn't show every extreme that they name: `owners`: within one index of fsdp every owner receives exactly 22 tiles; at most 2 of one device's tiles name the same owner, and on every device some owner is named exactly 2 times.
All inputs are finite; a program needn't handle non-finite values.
Results may differ from the reference program's by a relative error of at most 0.015.
Values may be sent and summed in bfloat16 or wider, within the bound.
No kernel may reach another device: no remote copies, remote signals or barrier semaphores. Data moves between devices by JAX's collectives and lax.ppermute only.
A program may use at most 320 MiB of HBM per device.

```python
import jax
import jax.numpy as jnp
from jax import lax

C1 = 320
C2 = 640
GROUPS = 32
TILE = 8
TSTEPS = 1000
TILE_DEV = 22
PEER_CAP = 2
TILES = 2816
N_DP = 32
N_FSDP = 4


def draw_owners(key, part):

    def one_group(group_key):
        key_list = jax.random.split(group_key, 4)
        order = jax.random.permutation(key_list[0], N_DP)
        offsets = order[jnp.arange(TILE_DEV) // PEER_CAP]
        offsets = offsets[jax.random.permutation(key_list[1], TILE_DEV)]
        shuffle_src = jax.random.permutation(key_list[2], N_DP)
        shuffle_dst = jax.random.permutation(key_list[3], N_DP)
        return shuffle_dst[(shuffle_src[:, None] + offsets[None, :]) % N_DP]
    groups = jax.vmap(one_group)(jax.random.split(jax.random.fold_in(key, 7), N_FSDP))
    return jnp.transpose(groups, (1, 0, 2)).reshape(N_DP * N_FSDP * TILE_DEV).astype(jnp.int32)


def plant(drawn, stream_key, low, top_value):
    longest = drawn.shape.index(max(drawn.shape))
    spots = []
    for shift in (0, 1):
        where = [jax.random.randint(jax.random.fold_in(stream_key, axis), (), 0, length) for axis, length in enumerate(drawn.shape)]
        where[longest] = (where[longest] + shift) % drawn.shape[longest]
        spots.append(tuple(where))
    return drawn.at[spots[0]].set(low).at[spots[1]].set(top_value)


def levels(key, shape, shards, low, largest):
    gain = 1.0
    for axis_at, shards_of in shards:
        steps = jax.random.uniform(jax.random.fold_in(jax.random.fold_in(key, 6), axis_at), (shards_of,), jnp.float32, low / len(shards), largest / len(shards))
        gain = gain * jnp.repeat(jnp.exp(steps), shape[axis_at] // shards_of).reshape((-1,) + (1,) * (len(shape) - 1 - axis_at))
    return gain


def gaussian(stream_key, shape, scale, limit, pieces=(), kind=jnp.bfloat16):
    loudness = levels(stream_key, shape, pieces, -0.22, 0.18) if pieces else 1.0
    values = jax.random.normal(stream_key, shape, jnp.float32) * scale * loudness
    return jnp.minimum(jnp.maximum(values, -limit), limit).astype(kind)


def setup_inputs(seed: int = 0) -> dict:
    arg_keys = jax.random.split(jax.random.key(seed), 11)
    return {
        "latents": gaussian(arg_keys[0], (TILES, TILE, TILE, C1), 1.0, 6.0, ((0, 128),)),
        "noise_draw": gaussian(arg_keys[1], (TILES, TILE, TILE, C1), 1.0, 6.0, ((0, 128),)),
        "timesteps": plant(jax.random.randint(arg_keys[2], (TILES,), 0, TSTEPS), jax.random.fold_in(arg_keys[2], 1), 0, TSTEPS - 1).astype(jnp.int32),
        "buckets": plant(jax.random.randint(arg_keys[3], (TILES,), 0, 3), jax.random.fold_in(arg_keys[3], 1), 0, 2).astype(jnp.int32),
        "owners": draw_owners(jax.random.fold_in(arg_keys[10], 71), 0),
        "adv_grad": gaussian(arg_keys[5], (TILES, TILE, TILE, C1), 1.0, 6.0, ((0, 128),)),
        "w_down": gaussian(arg_keys[6], (9 * C1, C2), (9 * C1) ** -0.5, 0.109375, ((0, 4),)),
        "w_up": gaussian(arg_keys[7], (9 * C2, C1), (9 * C2) ** -0.5, 0.078125, ((0, 4),)),
        "t_down": gaussian(arg_keys[8], (9 * C1, C2), (9 * C1) ** -0.5, 0.109375, ((0, 4),)),
        "t_up": gaussian(arg_keys[9], (9 * C2, C1), (9 * C2) ** -0.5, 0.078125, ((0, 4),)),
    }


distill_weight = 2.5
norm_epsilon = 1e-05

def tap_columns(volume, stride):
    tile_count, tile_side, _, channels = volume.shape
    out_side = tile_side // stride
    padded = jnp.pad(volume, ((0, 0), (1, 1), (1, 1), (0, 0)))
    tap_list = []
    for row_shift in range(3):
        for col_shift in range(3):
            tap_list.append(lax.slice(padded, (0, row_shift, col_shift, 0), (tile_count, row_shift + tile_side, col_shift + tile_side, channels), (1, stride, stride, 1)))
    return jnp.concatenate(tap_list, axis=3).reshape(tile_count * out_side * out_side, 9 * channels)

def width_masks(buckets, tile_side):
    half_side = tile_side // 2
    tile_count = buckets.shape[0]
    columns = jnp.arange(tile_side, dtype=jnp.int32)
    full_mask = (columns[None, None, :, None] < (tile_side - 2 * buckets)[:, None, None, None]).astype(jnp.float32)
    full_mask = jnp.broadcast_to(full_mask, (tile_count, tile_side, tile_side, 1))
    half_cols = jnp.arange(half_side, dtype=jnp.int32)
    half_mask = (half_cols[None, None, :, None] < (half_side - buckets)[:, None, None, None]).astype(jnp.float32)
    half_mask = jnp.broadcast_to(half_mask, (tile_count, half_side, half_side, 1))
    return (full_mask, half_mask)

def group_stats(hidden, half_mask):
    tile_count, height, breadth, channels = hidden.shape
    grouped = hidden.reshape(tile_count, height * breadth, GROUPS, channels // GROUPS)
    live_weight = half_mask.reshape(tile_count, height * breadth, 1, 1)
    population = lax.optimization_barrier(jnp.sum(live_weight, axis=(1, 3), keepdims=True)) * (channels // GROUPS)
    center = lax.optimization_barrier(jnp.sum(grouped * live_weight, axis=(1, 3), keepdims=True)) / population
    spread = lax.optimization_barrier(jnp.sum(jnp.square(grouped - center) * live_weight, axis=(1, 3), keepdims=True)) / population
    inverse = lax.rsqrt(spread + norm_epsilon)
    normed = ((grouped - center) * inverse).reshape(hidden.shape)
    return (normed, inverse, population)

def group_back(d_norm, normed, inverse, population, half_mask):
    tile_count, height, breadth, channels = d_norm.shape
    grouped_d = d_norm.reshape(tile_count, height * breadth, GROUPS, channels // GROUPS)
    grouped_n = normed.reshape(tile_count, height * breadth, GROUPS, channels // GROUPS)
    live_weight = half_mask.reshape(tile_count, height * breadth, 1, 1)
    mean_first = lax.optimization_barrier(jnp.sum(grouped_d, axis=(1, 3), keepdims=True)) / population
    mean_second = lax.optimization_barrier(jnp.sum(grouped_d * grouped_n, axis=(1, 3), keepdims=True)) / population
    result = live_weight * inverse * (grouped_d - mean_first - grouped_n * mean_second)
    return result.reshape(d_norm.shape)

def upsample(activated):
    return jnp.repeat(jnp.repeat(activated, 2, axis=1), 2, axis=2)

def network(noisy, full_mask, half_mask, down_weight, up_weight):
    tile_count, tile_side = (noisy.shape[0], noisy.shape[1])
    half_side = tile_side // 2
    down_cols = tap_columns(noisy, 2)
    hidden = jnp.dot(down_cols, down_weight, preferred_element_type=jnp.float32).reshape(tile_count, half_side, half_side, -1)
    normed, inverse, population = group_stats(hidden, half_mask)
    activated = (half_mask * jax.nn.silu(normed)).astype(jnp.bfloat16)
    up_cols = tap_columns(upsample(activated), 1)
    output = jnp.dot(up_cols, up_weight, preferred_element_type=jnp.float32).reshape(tile_count, tile_side, tile_side, -1)
    student = (full_mask * (noisy.astype(jnp.float32) + output)).astype(jnp.bfloat16)
    return (student, (down_cols, normed, inverse, population, activated, up_cols))

def flip_kernel(up_weight):
    up_chan = up_weight.shape[0] // 9
    out_chan = up_weight.shape[1]
    return up_weight.reshape(3, 3, up_chan, out_chan)[::-1, ::-1].transpose(0, 1, 3, 2).reshape(9 * out_chan, up_chan)

def cotangents(student, target, adversarial, full_mask, half_mask, flipped, cached, loss_scale):
    down_cols, normed, inverse, population, activated, up_cols = cached
    tile_count, tile_side = (student.shape[0], student.shape[1])
    half_side = tile_side // 2
    d_out = (full_mask * (distill_weight * (student.astype(jnp.float32) - target.astype(jnp.float32)) + adversarial.astype(jnp.float32)) * loss_scale).astype(jnp.bfloat16)
    d_up = jnp.dot(tap_columns(d_out, 1), flipped, preferred_element_type=jnp.float32)
    d_up = d_up.reshape(tile_count, half_side, 2, half_side, 2, flipped.shape[1])
    d_act = lax.optimization_barrier(jnp.sum(d_up, axis=(2, 4)))
    sigmoid_n = jax.nn.sigmoid(normed)
    d_norm = half_mask * d_act * sigmoid_n * (1.0 + normed * (1.0 - sigmoid_n))
    d_hidden = group_back(d_norm, normed, inverse, population, half_mask).astype(jnp.bfloat16)
    return (d_out, d_hidden)

def transposed(left_side, right_side):
    return lax.dot_general(left_side, right_side, (((0,), (0,)), ((), ())), preferred_element_type=jnp.float32)

def reference(latents, noise_draw, timesteps, buckets, owners, adv_grad, w_down, w_up, t_down, t_up):
    tile_index = jnp.arange(TILES, dtype=jnp.int32)
    fsdp_index = tile_index // TILE_DEV % N_FSDP
    group_key = fsdp_index * N_DP + owners
    hit_table = (group_key[:, None] == jnp.arange(N_FSDP * N_DP, dtype=jnp.int32)[None, :]).astype(jnp.int32)
    before = (jnp.cumsum(hit_table, axis=0) - hit_table).astype(jnp.int32)
    rank_in = lax.optimization_barrier(jnp.sum(before * hit_table, axis=1)).astype(jnp.int32)
    owner_place = ((owners * N_FSDP + fsdp_index) * TILE_DEV + rank_in).astype(jnp.int32)
    tile_side = latents.shape[1]
    full_mask, half_mask = width_masks(buckets, tile_side)
    alpha_bar = jnp.square(jnp.cos(0.5 * jnp.pi * (timesteps.astype(jnp.float32) + 0.5) / TSTEPS))
    noisy = (full_mask * (jnp.sqrt(alpha_bar)[:, None, None, None] * latents.astype(jnp.float32) + jnp.sqrt(1.0 - alpha_bar)[:, None, None, None] * noise_draw.astype(jnp.float32))).astype(jnp.bfloat16)
    adversarial = adv_grad[owner_place]
    flipped = flip_kernel(w_up)
    loss_scale = jnp.float32(1.0 / TILES)
    block_size = TILES // N_DP

    def regroup(array):
        return array.reshape((N_DP, block_size) + array.shape[1:])

    def visit_block(totals, block_items):
        noisy_b, full_b, half_b, adv_b = block_items
        student, cached = network(noisy_b, full_b, half_b, w_down, w_up)
        target, _ = network(noisy_b, full_b, half_b, t_down, t_up)
        d_out, d_hidden = cotangents(student, target, adv_b, full_b, half_b, flipped, cached, loss_scale)
        new_down = totals[0] + transposed(cached[0], d_hidden.reshape(-1, d_hidden.shape[3]))
        new_up = totals[1] + transposed(cached[5], d_out.reshape(-1, d_out.shape[3]))
        return ((new_down, new_up), student)
    initial = (jnp.zeros(w_down.shape, jnp.float32), jnp.zeros(w_up.shape, jnp.float32))
    (grad_down, grad_up), students = lax.scan(visit_block, initial, (regroup(noisy), regroup(full_mask), regroup(half_mask), regroup(adversarial)))
    student_out = jnp.zeros_like(latents).at[owner_place].set(students.reshape(latents.shape))
    return (student_out, grad_down, grad_up)
```

```python
import jax
import jax.numpy as jnp
from jax import lax
from jax.sharding import PartitionSpec as P

GROUPS = 32
TSTEPS = 1000


distill_weight = 2.5
norm_epsilon = 1e-05


def conv_forward(volume, kernel_rows, stride):
    in_chan = volume.shape[3]
    kernel = kernel_rows.reshape(3, 3, in_chan, kernel_rows.shape[1])
    return lax.conv_general_dilated(
        volume,
        kernel,
        (stride, stride),
        ((1, 1), (1, 1)),
        dimension_numbers=("NHWC", "HWIO", "NHWC"),
        preferred_element_type=jnp.float32,
    )


def kernel_grad(volume, cotangent, stride):
    pad_upper = 1 if stride == 1 else 0
    result_grad = lax.conv_general_dilated(
        volume,
        cotangent,
        (1, 1),
        ((1, pad_upper), (1, pad_upper)),
        rhs_dilation=(stride, stride),
        dimension_numbers=("CHWN", "IHWO", "HWNC"),
        preferred_element_type=jnp.float32,
    )
    return result_grad.reshape(9 * volume.shape[3], cotangent.shape[3])


def width_masks(buckets, tile_side):
    half_side = tile_side // 2
    tile_count = buckets.shape[0]
    columns = jnp.arange(tile_side, dtype=jnp.int32)
    full_mask = (
        columns[None, None, :, None] < (tile_side - 2 * buckets)[:, None, None, None]
    ).astype(jnp.float32)
    full_mask = jnp.broadcast_to(full_mask, (tile_count, tile_side, tile_side, 1))
    half_cols = jnp.arange(half_side, dtype=jnp.int32)
    half_mask = (
        half_cols[None, None, :, None] < (half_side - buckets)[:, None, None, None]
    ).astype(jnp.float32)
    half_mask = jnp.broadcast_to(half_mask, (tile_count, half_side, half_side, 1))
    return (full_mask, half_mask)


def group_stats(hidden, half_mask):
    tile_count, height, breadth, channels = hidden.shape
    grouped = hidden.reshape(tile_count, height * breadth, GROUPS, channels // GROUPS)
    live_weight = half_mask.reshape(tile_count, height * breadth, 1, 1)
    population = jnp.sum(live_weight, axis=(1, 3), keepdims=True) * (channels // GROUPS)
    center = jnp.sum(grouped * live_weight, axis=(1, 3), keepdims=True) / population
    spread = (
        jnp.sum(jnp.square(grouped - center) * live_weight, axis=(1, 3), keepdims=True) / population
    )
    inverse = lax.rsqrt(spread + norm_epsilon)
    normed = ((grouped - center) * inverse).reshape(hidden.shape)
    return (normed, inverse, population)


def group_back(d_norm, normed, inverse, population, half_mask):
    tile_count, height, breadth, channels = d_norm.shape
    grouped_d = d_norm.reshape(tile_count, height * breadth, GROUPS, channels // GROUPS)
    grouped_n = normed.reshape(tile_count, height * breadth, GROUPS, channels // GROUPS)
    live_weight = half_mask.reshape(tile_count, height * breadth, 1, 1)
    mean_first = jnp.sum(grouped_d, axis=(1, 3), keepdims=True) / population
    mean_second = jnp.sum(grouped_d * grouped_n, axis=(1, 3), keepdims=True) / population
    result = live_weight * inverse * (grouped_d - mean_first - grouped_n * mean_second)
    return result.reshape(d_norm.shape)


def upsample(activated):
    return jnp.repeat(jnp.repeat(activated, 2, axis=1), 2, axis=2)


def network(noisy, full_mask, half_mask, down_weight, up_weight):
    hidden = conv_forward(noisy, down_weight, 2)
    normed, inverse, population = group_stats(hidden, half_mask)
    activated = (half_mask * jax.nn.silu(normed)).astype(jnp.bfloat16)
    enlarged = upsample(activated)
    output = conv_forward(enlarged, up_weight, 1)
    student = (full_mask * (noisy.astype(jnp.float32) + output)).astype(jnp.bfloat16)
    return (student, (noisy, normed, inverse, population, activated, enlarged))


def flip_kernel(up_weight):
    up_chan = up_weight.shape[0] // 9
    out_chan = up_weight.shape[1]
    return (
        up_weight.reshape(3, 3, up_chan, out_chan)[::-1, ::-1]
        .transpose(0, 1, 3, 2)
        .reshape(9 * out_chan, up_chan)
    )


def cotangents(student, target, adversarial, full_mask, half_mask, flipped, cached, loss_scale):
    source_in, normed, inverse, population, activated, enlarged = cached
    tile_count, tile_side = (student.shape[0], student.shape[1])
    half_side = tile_side // 2
    d_out = (
        full_mask
        * (
            distill_weight * (student.astype(jnp.float32) - target.astype(jnp.float32))
            + adversarial.astype(jnp.float32)
        )
        * loss_scale
    ).astype(jnp.bfloat16)
    d_up = conv_forward(d_out, flipped, 1)
    d_up = d_up.reshape(tile_count, half_side, 2, half_side, 2, flipped.shape[1])
    d_act = jnp.sum(d_up, axis=(2, 4))
    sigmoid_n = jax.nn.sigmoid(normed)
    d_norm = half_mask * d_act * sigmoid_n * (1.0 + normed * (1.0 - sigmoid_n))
    d_hidden = group_back(d_norm, normed, inverse, population, half_mask).astype(jnp.bfloat16)
    return (d_out, d_hidden)


def ring_gather(own, dp_count, fsdp_count):
    n = own.shape[0]
    half = n // 2
    fsdp_at = lax.axis_index("fsdp")
    core = lax.axis_index("dp") % 2

    def lin(d, f):
        return d * fsdp_count + f

    ring_pairs = []
    for d in range(dp_count):
        step = -1 if d % 2 == 0 else 1
        for f in range(fsdp_count):
            ring_pairs.append((lin(d, f), lin(d, (f + step) % fsdp_count)))
    first = lax.ppermute(own, ("dp", "fsdp"), ring_pairs)
    forward = jnp.where(core == 0, first[:half], first[half:])
    second = lax.ppermute(forward, ("dp", "fsdp"), ring_pairs)
    swap_pairs = [(d, d ^ 1) for d in range(dp_count)]
    other_first, other_second = lax.ppermute((first, second), "dp", swap_pairs)
    is_even = core == 0
    next_one = jnp.where(is_even, first, other_first)
    far = jnp.where(is_even, jnp.concatenate([second, other_second]), jnp.concatenate([other_second, second]))
    prev_one = jnp.where(is_even, other_first, first)
    relative = jnp.stack([own, next_one, far, prev_one])
    doubled = jnp.concatenate([relative, relative])
    return lax.dynamic_slice_in_dim(doubled, fsdp_count - fsdp_at, fsdp_count, axis=0)


def gather_pair(down_rows, up_rows, dp_count, fsdp_count):
    down_size = down_rows.size
    if fsdp_count != 4 or dp_count % 2:
        return (
            lax.all_gather(down_rows, "fsdp", axis=0, tiled=True),
            lax.all_gather(up_rows, "fsdp", axis=0, tiled=True),
        )
    own = jnp.concatenate([down_rows.reshape(-1), up_rows.reshape(-1)])
    full = ring_gather(own, dp_count, fsdp_count)
    down_full = full[:, :down_size].reshape(fsdp_count * down_rows.shape[0], down_rows.shape[1])
    up_full = full[:, down_size:].reshape(fsdp_count * up_rows.shape[0], up_rows.shape[1])
    return (down_full, up_full)


def on_device(
    latents, noise_draw, timesteps, buckets, owners, adv_grad, w_down, w_up, t_down, t_up
):
    tile_count, tile_side = (latents.shape[0], latents.shape[1])
    dp_count = lax.axis_size("dp")
    fsdp_count = lax.axis_size("fsdp")
    full_mask, half_mask = width_masks(buckets, tile_side)
    alpha_bar = jnp.square(jnp.cos(0.5 * jnp.pi * (timesteps.astype(jnp.float32) + 0.5) / TSTEPS))
    noisy = (
        full_mask
        * (
            jnp.sqrt(alpha_bar)[:, None, None, None] * latents.astype(jnp.float32)
            + jnp.sqrt(1.0 - alpha_bar)[:, None, None, None] * noise_draw.astype(jnp.float32)
        )
    ).astype(jnp.bfloat16)
    peer_cap = max(2, (tile_count + dp_count - 1) // dp_count)
    slot_count = dp_count * peer_cap
    hit_table = (owners[:, None] == jnp.arange(dp_count, dtype=jnp.int32)[None, :]).astype(
        jnp.int32
    )
    before = jnp.cumsum(hit_table, axis=0) - hit_table
    slot_of = owners * peer_cap + jnp.sum(before * hit_table, axis=1)
    slot_hits = slot_of[None, :] == jnp.arange(slot_count, dtype=jnp.int32)[:, None]
    spread_matrix = slot_hits.astype(jnp.bfloat16)
    send_noisy = (
        jnp.dot(spread_matrix, noisy.reshape(tile_count, -1), preferred_element_type=jnp.float32)
        .astype(jnp.bfloat16)
        .reshape(dp_count, peer_cap, -1)
    )
    send_code = jnp.sum(jnp.where(slot_hits, buckets[None, :] + 1, 0), axis=1).reshape(
        dp_count, peer_cap
    )
    teacher_down, teacher_up = gather_pair(t_down, t_up, dp_count, fsdp_count)
    recv_noisy, recv_code = (
        lax.all_to_all(send_noisy, "dp", split_axis=0, concat_axis=0, tiled=True),
        lax.all_to_all(send_code, "dp", split_axis=0, concat_axis=0, tiled=True),
    )
    flat_code = recv_code.reshape(slot_count)
    live_slot = (flat_code > 0).astype(jnp.int32)
    position = jnp.cumsum(live_slot) - live_slot
    pick_hits = (live_slot[None, :] == 1) & (
        position[None, :] == jnp.arange(tile_count, dtype=jnp.int32)[:, None]
    )
    pick_matrix = pick_hits.astype(jnp.bfloat16)
    own_noisy = (
        jnp.dot(pick_matrix, recv_noisy.reshape(slot_count, -1), preferred_element_type=jnp.float32)
        .astype(jnp.bfloat16)
        .reshape(latents.shape)
    )
    own_buckets = jnp.sum(jnp.where(pick_hits, flat_code[None, :] - 1, 0), axis=1).astype(jnp.int32)
    own_full, own_half = width_masks(own_buckets, tile_side)
    student_down, student_up = gather_pair(w_down, w_up, dp_count, fsdp_count)
    student, cached = network(own_noisy, own_full, own_half, student_down, student_up)
    target, _ = network(own_noisy, own_full, own_half, teacher_down, teacher_up)
    loss_scale = jnp.float32(1.0 / (tile_count * dp_count * fsdp_count))
    flipped = flip_kernel(student_up)
    d_out, d_hidden = cotangents(
        student, target, adv_grad, own_full, own_half, flipped, cached, loss_scale
    )
    local_down = kernel_grad(cached[0], d_hidden, 2)
    local_up = kernel_grad(cached[5], d_out, 1)
    shard_down, shard_up = (
        lax.psum_scatter(
            local_down.astype(jnp.bfloat16), "fsdp", scatter_dimension=0, tiled=True
        ).astype(jnp.float32),
        lax.psum_scatter(
            local_up.astype(jnp.bfloat16), "fsdp", scatter_dimension=0, tiled=True
        ).astype(jnp.float32),
    )
    grad_down, grad_up = (
        lax.psum(shard_down.astype(jnp.bfloat16), "dp").astype(jnp.float32),
        lax.psum(shard_up.astype(jnp.bfloat16), "dp").astype(jnp.float32),
    )
    return (student, grad_down, grad_up)


def solution(mesh):
    return jax.shard_map(
        on_device,
        mesh=mesh,
        in_specs=(
            P(("dp", "fsdp"), None, None, None),
            P(("dp", "fsdp"), None, None, None),
            P(("dp", "fsdp")),
            P(("dp", "fsdp")),
            P(("dp", "fsdp")),
            P(("dp", "fsdp"), None, None, None),
            P("fsdp", None),
            P("fsdp", None),
            P("fsdp", None),
            P("fsdp", None),
        ),
        out_specs=(P(("dp", "fsdp"), None, None, None), P("fsdp", None), P("fsdp", None)),
        check_vma=False,
    )
```

```python
import jax
import jax.numpy as jnp
from jax import lax
from jax.sharding import PartitionSpec as P

GROUPS = 32
TSTEPS = 1000


distill_weight = 2.5
norm_epsilon = 1e-05


def conv_forward(volume, kernel_rows, stride):
    in_chan = volume.shape[3]
    kernel = kernel_rows.reshape(3, 3, in_chan, kernel_rows.shape[1])
    return lax.conv_general_dilated(
        volume,
        kernel,
        (stride, stride),
        ((1, 1), (1, 1)),
        dimension_numbers=("NHWC", "HWIO", "NHWC"),
        preferred_element_type=jnp.float32,
    )


def kernel_grad(volume, cotangent, stride):
    pad_upper = 1 if stride == 1 else 0
    result_grad = lax.conv_general_dilated(
        volume,
        cotangent,
        (1, 1),
        ((1, pad_upper), (1, pad_upper)),
        rhs_dilation=(stride, stride),
        dimension_numbers=("CHWN", "IHWO", "HWNC"),
        preferred_element_type=jnp.float32,
    )
    return result_grad.reshape(9 * volume.shape[3], cotangent.shape[3])


def width_masks(buckets, tile_side):
    half_side = tile_side // 2
    tile_count = buckets.shape[0]
    columns = jnp.arange(tile_side, dtype=jnp.int32)
    full_mask = (
        columns[None, None, :, None] < (tile_side - 2 * buckets)[:, None, None, None]
    ).astype(jnp.float32)
    full_mask = jnp.broadcast_to(full_mask, (tile_count, tile_side, tile_side, 1))
    half_cols = jnp.arange(half_side, dtype=jnp.int32)
    half_mask = (
        half_cols[None, None, :, None] < (half_side - buckets)[:, None, None, None]
    ).astype(jnp.float32)
    half_mask = jnp.broadcast_to(half_mask, (tile_count, half_side, half_side, 1))
    return (full_mask, half_mask)


def group_stats(hidden, half_mask):
    tile_count, height, breadth, channels = hidden.shape
    grouped = hidden.reshape(tile_count, height * breadth, GROUPS, channels // GROUPS)
    live_weight = half_mask.reshape(tile_count, height * breadth, 1, 1)
    population = jnp.sum(live_weight, axis=(1, 3), keepdims=True) * (channels // GROUPS)
    center = jnp.sum(grouped * live_weight, axis=(1, 3), keepdims=True) / population
    spread = (
        jnp.sum(jnp.square(grouped - center) * live_weight, axis=(1, 3), keepdims=True) / population
    )
    inverse = lax.rsqrt(spread + norm_epsilon)
    normed = ((grouped - center) * inverse).reshape(hidden.shape)
    return (normed, inverse, population)


def group_back(d_norm, normed, inverse, population, half_mask):
    tile_count, height, breadth, channels = d_norm.shape
    grouped_d = d_norm.reshape(tile_count, height * breadth, GROUPS, channels // GROUPS)
    grouped_n = normed.reshape(tile_count, height * breadth, GROUPS, channels // GROUPS)
    live_weight = half_mask.reshape(tile_count, height * breadth, 1, 1)
    mean_first = jnp.sum(grouped_d, axis=(1, 3), keepdims=True) / population
    mean_second = jnp.sum(grouped_d * grouped_n, axis=(1, 3), keepdims=True) / population
    result = live_weight * inverse * (grouped_d - mean_first - grouped_n * mean_second)
    return result.reshape(d_norm.shape)


def upsample(activated):
    return jnp.repeat(jnp.repeat(activated, 2, axis=1), 2, axis=2)


def network(noisy, full_mask, half_mask, down_weight, up_weight):
    hidden = conv_forward(noisy, down_weight, 2)
    normed, inverse, population = group_stats(hidden, half_mask)
    activated = (half_mask * jax.nn.silu(normed)).astype(jnp.bfloat16)
    enlarged = upsample(activated)
    output = conv_forward(enlarged, up_weight, 1)
    student = (full_mask * (noisy.astype(jnp.float32) + output)).astype(jnp.bfloat16)
    return (student, (noisy, normed, inverse, population, activated, enlarged))


def flip_kernel(up_weight):
    up_chan = up_weight.shape[0] // 9
    out_chan = up_weight.shape[1]
    return (
        up_weight.reshape(3, 3, up_chan, out_chan)[::-1, ::-1]
        .transpose(0, 1, 3, 2)
        .reshape(9 * out_chan, up_chan)
    )


def cotangents(student, target, adversarial, full_mask, half_mask, flipped, cached, loss_scale):
    source_in, normed, inverse, population, activated, enlarged = cached
    tile_count, tile_side = (student.shape[0], student.shape[1])
    half_side = tile_side // 2
    d_out = (
        full_mask
        * (
            distill_weight * (student.astype(jnp.float32) - target.astype(jnp.float32))
            + adversarial.astype(jnp.float32)
        )
        * loss_scale
    ).astype(jnp.bfloat16)
    d_up = conv_forward(d_out, flipped, 1)
    d_up = d_up.reshape(tile_count, half_side, 2, half_side, 2, flipped.shape[1])
    d_act = jnp.sum(d_up, axis=(2, 4))
    sigmoid_n = jax.nn.sigmoid(normed)
    d_norm = half_mask * d_act * sigmoid_n * (1.0 + normed * (1.0 - sigmoid_n))
    d_hidden = group_back(d_norm, normed, inverse, population, half_mask).astype(jnp.bfloat16)
    return (d_out, d_hidden)


def ring_gather(shards, dp_count, fsdp_count):
    fsdp_at = lax.axis_index("fsdp")
    core = lax.axis_index("dp") % 2
    step = 1 - 2 * core

    def lin(d, f):
        return d * fsdp_count + f

    ring_pairs = []
    for d in range(dp_count):
        toward = -1 if d % 2 == 0 else 1
        for f in range(fsdp_count):
            ring_pairs.append((lin(d, f), lin(d, (f + toward) % fsdp_count)))
    first = lax.ppermute(shards, ("dp", "fsdp"), ring_pairs)
    halves = tuple(
        lax.dynamic_slice_in_dim(piece, core * (piece.shape[0] // 2), piece.shape[0] // 2, axis=0)
        for piece in first
    )
    second = lax.ppermute(halves, ("dp", "fsdp"), ring_pairs)
    swap_pairs = [(d, d ^ 1) for d in range(dp_count)]
    other_first, other_second = lax.ppermute((first, second), "dp", swap_pairs)
    near = (fsdp_at + step + fsdp_count) % fsdp_count
    behind = (fsdp_at - step + fsdp_count) % fsdp_count
    far = (fsdp_at + 2) % fsdp_count
    gathered = []
    for own, got, got_other, half, half_other in zip(shards, first, other_first, second, other_second):
        rows = own.shape[0]
        full = jnp.zeros((fsdp_count * rows,) + own.shape[1:], own.dtype)
        full = lax.dynamic_update_slice_in_dim(full, own, fsdp_at * rows, axis=0)
        full = lax.dynamic_update_slice_in_dim(full, got, near * rows, axis=0)
        full = lax.dynamic_update_slice_in_dim(full, got_other, behind * rows, axis=0)
        full = lax.dynamic_update_slice_in_dim(full, half, far * rows + core * (rows // 2), axis=0)
        full = lax.dynamic_update_slice_in_dim(
            full, half_other, far * rows + (1 - core) * (rows // 2), axis=0
        )
        gathered.append(full)
    return tuple(gathered)


def gather_pair(down_rows, up_rows, dp_count, fsdp_count):
    if fsdp_count != 4 or dp_count % 2 or down_rows.shape[0] % 2 or up_rows.shape[0] % 2:
        return (
            lax.all_gather(down_rows, "fsdp", axis=0, tiled=True),
            lax.all_gather(up_rows, "fsdp", axis=0, tiled=True),
        )
    return ring_gather((down_rows, up_rows), dp_count, fsdp_count)


def on_device(
    latents, noise_draw, timesteps, buckets, owners, adv_grad, w_down, w_up, t_down, t_up
):
    tile_count, tile_side = (latents.shape[0], latents.shape[1])
    dp_count = lax.axis_size("dp")
    fsdp_count = lax.axis_size("fsdp")
    full_mask, half_mask = width_masks(buckets, tile_side)
    alpha_bar = jnp.square(jnp.cos(0.5 * jnp.pi * (timesteps.astype(jnp.float32) + 0.5) / TSTEPS))
    noisy = (
        full_mask
        * (
            jnp.sqrt(alpha_bar)[:, None, None, None] * latents.astype(jnp.float32)
            + jnp.sqrt(1.0 - alpha_bar)[:, None, None, None] * noise_draw.astype(jnp.float32)
        )
    ).astype(jnp.bfloat16)
    peer_cap = max(2, (tile_count + dp_count - 1) // dp_count)
    slot_count = dp_count * peer_cap
    hit_table = (owners[:, None] == jnp.arange(dp_count, dtype=jnp.int32)[None, :]).astype(
        jnp.int32
    )
    before = jnp.cumsum(hit_table, axis=0) - hit_table
    slot_of = owners * peer_cap + jnp.sum(before * hit_table, axis=1)
    slot_hits = slot_of[None, :] == jnp.arange(slot_count, dtype=jnp.int32)[:, None]
    spread_matrix = slot_hits.astype(jnp.bfloat16)
    send_noisy = (
        jnp.dot(spread_matrix, noisy.reshape(tile_count, -1), preferred_element_type=jnp.float32)
        .astype(jnp.bfloat16)
        .reshape(dp_count, peer_cap, -1)
    )
    send_code = jnp.sum(jnp.where(slot_hits, buckets[None, :] + 1, 0), axis=1).reshape(
        dp_count, peer_cap
    )
    teacher_down, teacher_up = gather_pair(t_down, t_up, dp_count, fsdp_count)
    recv_noisy, recv_code = (
        lax.all_to_all(send_noisy, "dp", split_axis=0, concat_axis=0, tiled=True),
        lax.all_to_all(send_code, "dp", split_axis=0, concat_axis=0, tiled=True),
    )
    flat_code = recv_code.reshape(slot_count)
    live_slot = (flat_code > 0).astype(jnp.int32)
    position = jnp.cumsum(live_slot) - live_slot
    pick_hits = (live_slot[None, :] == 1) & (
        position[None, :] == jnp.arange(tile_count, dtype=jnp.int32)[:, None]
    )
    pick_matrix = pick_hits.astype(jnp.bfloat16)
    own_noisy = (
        jnp.dot(pick_matrix, recv_noisy.reshape(slot_count, -1), preferred_element_type=jnp.float32)
        .astype(jnp.bfloat16)
        .reshape(latents.shape)
    )
    own_buckets = jnp.sum(jnp.where(pick_hits, flat_code[None, :] - 1, 0), axis=1).astype(jnp.int32)
    own_full, own_half = width_masks(own_buckets, tile_side)
    student_down, student_up = gather_pair(w_down, w_up, dp_count, fsdp_count)
    student, cached = network(own_noisy, own_full, own_half, student_down, student_up)
    target, _ = network(own_noisy, own_full, own_half, teacher_down, teacher_up)
    loss_scale = jnp.float32(1.0 / (tile_count * dp_count * fsdp_count))
    flipped = flip_kernel(student_up)
    d_out, d_hidden = cotangents(
        student, target, adv_grad, own_full, own_half, flipped, cached, loss_scale
    )
    local_down = kernel_grad(cached[0], d_hidden, 2)
    local_up = kernel_grad(cached[5], d_out, 1)
    shard_down, shard_up = (
        lax.psum_scatter(
            local_down.astype(jnp.bfloat16), "fsdp", scatter_dimension=0, tiled=True
        ).astype(jnp.float32),
        lax.psum_scatter(
            local_up.astype(jnp.bfloat16), "fsdp", scatter_dimension=0, tiled=True
        ).astype(jnp.float32),
    )
    grad_down, grad_up = (
        lax.psum(shard_down.astype(jnp.bfloat16), "dp").astype(jnp.float32),
        lax.psum(shard_up.astype(jnp.bfloat16), "dp").astype(jnp.float32),
    )
    return (student, grad_down, grad_up)


def solution(mesh):
    return jax.shard_map(
        on_device,
        mesh=mesh,
        in_specs=(
            P(("dp", "fsdp"), None, None, None),
            P(("dp", "fsdp"), None, None, None),
            P(("dp", "fsdp")),
            P(("dp", "fsdp")),
            P(("dp", "fsdp")),
            P(("dp", "fsdp"), None, None, None),
            P("fsdp", None),
            P("fsdp", None),
            P("fsdp", None),
            P("fsdp", None),
        ),
        out_specs=(P(("dp", "fsdp"), None, None, None), P("fsdp", None), P("fsdp", None)),
        check_vma=False,
    )
```

```python
import jax
import jax.numpy as jnp
from jax import lax
from jax.sharding import PartitionSpec as P

GROUPS = 32
TSTEPS = 1000


distill_weight = 2.5
norm_epsilon = 1e-05


def conv_forward(volume, kernel_rows, stride):
    in_chan = volume.shape[3]
    kernel = kernel_rows.reshape(3, 3, in_chan, kernel_rows.shape[1])
    return lax.conv_general_dilated(
        volume,
        kernel,
        (stride, stride),
        ((1, 1), (1, 1)),
        dimension_numbers=("NHWC", "HWIO", "NHWC"),
        preferred_element_type=jnp.float32,
    )


def kernel_grad(volume, cotangent, stride):
    pad_upper = 1 if stride == 1 else 0
    result_grad = lax.conv_general_dilated(
        volume,
        cotangent,
        (1, 1),
        ((1, pad_upper), (1, pad_upper)),
        rhs_dilation=(stride, stride),
        dimension_numbers=("CHWN", "IHWO", "HWNC"),
        preferred_element_type=jnp.float32,
    )
    return result_grad.reshape(9 * volume.shape[3], cotangent.shape[3])


def width_masks(buckets, tile_side):
    half_side = tile_side // 2
    tile_count = buckets.shape[0]
    columns = jnp.arange(tile_side, dtype=jnp.int32)
    full_mask = (
        columns[None, None, :, None] < (tile_side - 2 * buckets)[:, None, None, None]
    ).astype(jnp.float32)
    full_mask = jnp.broadcast_to(full_mask, (tile_count, tile_side, tile_side, 1))
    half_cols = jnp.arange(half_side, dtype=jnp.int32)
    half_mask = (
        half_cols[None, None, :, None] < (half_side - buckets)[:, None, None, None]
    ).astype(jnp.float32)
    half_mask = jnp.broadcast_to(half_mask, (tile_count, half_side, half_side, 1))
    return (full_mask, half_mask)


def group_stats(hidden, half_mask):
    tile_count, height, breadth, channels = hidden.shape
    grouped = hidden.reshape(tile_count, height * breadth, GROUPS, channels // GROUPS)
    live_weight = half_mask.reshape(tile_count, height * breadth, 1, 1)
    population = jnp.sum(live_weight, axis=(1, 3), keepdims=True) * (channels // GROUPS)
    center = jnp.sum(grouped * live_weight, axis=(1, 3), keepdims=True) / population
    spread = (
        jnp.sum(jnp.square(grouped - center) * live_weight, axis=(1, 3), keepdims=True) / population
    )
    inverse = lax.rsqrt(spread + norm_epsilon)
    normed = ((grouped - center) * inverse).reshape(hidden.shape)
    return (normed, inverse, population)


def group_back(d_norm, normed, inverse, population, half_mask):
    tile_count, height, breadth, channels = d_norm.shape
    grouped_d = d_norm.reshape(tile_count, height * breadth, GROUPS, channels // GROUPS)
    grouped_n = normed.reshape(tile_count, height * breadth, GROUPS, channels // GROUPS)
    live_weight = half_mask.reshape(tile_count, height * breadth, 1, 1)
    mean_first = jnp.sum(grouped_d, axis=(1, 3), keepdims=True) / population
    mean_second = jnp.sum(grouped_d * grouped_n, axis=(1, 3), keepdims=True) / population
    result = live_weight * inverse * (grouped_d - mean_first - grouped_n * mean_second)
    return result.reshape(d_norm.shape)


def upsample(activated):
    return jnp.repeat(jnp.repeat(activated, 2, axis=1), 2, axis=2)


def network(noisy, full_mask, half_mask, down_weight, up_weight):
    hidden = conv_forward(noisy, down_weight, 2)
    normed, inverse, population = group_stats(hidden, half_mask)
    activated = (half_mask * jax.nn.silu(normed)).astype(jnp.bfloat16)
    enlarged = upsample(activated)
    output = conv_forward(enlarged, up_weight, 1)
    student = (full_mask * (noisy.astype(jnp.float32) + output)).astype(jnp.bfloat16)
    return (student, (noisy, normed, inverse, population, activated, enlarged))


def flip_kernel(up_weight):
    up_chan = up_weight.shape[0] // 9
    out_chan = up_weight.shape[1]
    return (
        up_weight.reshape(3, 3, up_chan, out_chan)[::-1, ::-1]
        .transpose(0, 1, 3, 2)
        .reshape(9 * out_chan, up_chan)
    )


def cotangents(student, target, adversarial, full_mask, half_mask, flipped, cached, loss_scale):
    source_in, normed, inverse, population, activated, enlarged = cached
    tile_count, tile_side = (student.shape[0], student.shape[1])
    half_side = tile_side // 2
    d_out = (
        full_mask
        * (
            distill_weight * (student.astype(jnp.float32) - target.astype(jnp.float32))
            + adversarial.astype(jnp.float32)
        )
        * loss_scale
    ).astype(jnp.bfloat16)
    d_up = conv_forward(d_out, flipped, 1)
    d_up = d_up.reshape(tile_count, half_side, 2, half_side, 2, flipped.shape[1])
    d_act = jnp.sum(d_up, axis=(2, 4))
    sigmoid_n = jax.nn.sigmoid(normed)
    d_norm = half_mask * d_act * sigmoid_n * (1.0 + normed * (1.0 - sigmoid_n))
    d_hidden = group_back(d_norm, normed, inverse, population, half_mask).astype(jnp.bfloat16)
    return (d_out, d_hidden)


def ring_gather(shards, dp_count, fsdp_count):
    fsdp_at = lax.axis_index("fsdp")
    core = lax.axis_index("dp") % 2
    step = 1 - 2 * core

    def lin(d, f):
        return d * fsdp_count + f

    ring_pairs = []
    for d in range(dp_count):
        toward = -1 if d % 2 == 0 else 1
        for f in range(fsdp_count):
            ring_pairs.append((lin(d, f), lin(d, (f + toward) % fsdp_count)))
    first = lax.ppermute(shards, ("dp", "fsdp"), ring_pairs)
    halves = tuple(
        lax.dynamic_slice_in_dim(piece, core * (piece.shape[0] // 2), piece.shape[0] // 2, axis=0)
        for piece in first
    )
    second = lax.ppermute(halves, ("dp", "fsdp"), ring_pairs)
    swap_pairs = [(d, d ^ 1) for d in range(dp_count)]
    other_first, other_second = lax.ppermute((first, second), "dp", swap_pairs)
    near = (fsdp_at + step + fsdp_count) % fsdp_count
    behind = (fsdp_at - step + fsdp_count) % fsdp_count
    far = (fsdp_at + 2) % fsdp_count
    gathered = []
    for own, got, got_other, half, half_other in zip(shards, first, other_first, second, other_second):
        rows = own.shape[0]
        full = jnp.zeros((fsdp_count * rows,) + own.shape[1:], own.dtype)
        full = lax.dynamic_update_slice_in_dim(full, own, fsdp_at * rows, axis=0)
        full = lax.dynamic_update_slice_in_dim(full, got, near * rows, axis=0)
        full = lax.dynamic_update_slice_in_dim(full, got_other, behind * rows, axis=0)
        full = lax.dynamic_update_slice_in_dim(full, half, far * rows + core * (rows // 2), axis=0)
        full = lax.dynamic_update_slice_in_dim(
            full, half_other, far * rows + (1 - core) * (rows // 2), axis=0
        )
        gathered.append(full)
    return tuple(gathered)


def gather_pair(down_rows, up_rows, dp_count, fsdp_count):
    if fsdp_count != 4 or dp_count % 2 or down_rows.shape[0] % 2 or up_rows.shape[0] % 2:
        return (
            lax.all_gather(down_rows, "fsdp", axis=0, tiled=True),
            lax.all_gather(up_rows, "fsdp", axis=0, tiled=True),
        )
    return ring_gather((down_rows, up_rows), dp_count, fsdp_count)


def coordinate_pairs(dp_count, fsdp_count, moved, shift):
    sizes = {"x": dp_count // 8, "z": 4, "core": 2, "y": fsdp_count}
    pairs = []
    for d in range(dp_count):
        for f in range(fsdp_count):
            place = {"x": d // 8, "z": (d // 2) % 4, "core": d % 2, "y": f}
            place[moved] = (place[moved] + shift) % sizes[moved]
            target = (place["x"] * 8 + place["z"] * 2 + place["core"]) * fsdp_count + place["y"]
            pairs.append((d * fsdp_count + f, target))
    return pairs


def scatter_sum(parts, at, count, pairs_of):
    total = lax.dynamic_index_in_dim(parts, at, axis=0, keepdims=False)
    for k in range(1, count):
        sent = lax.dynamic_index_in_dim(parts, (at + k) % count, axis=0, keepdims=False)
        got = lax.ppermute(sent.astype(jnp.bfloat16), ("dp", "fsdp"), pairs_of(k))
        total = total + got.astype(jnp.float32)
    return total


def gather_blocks(block, at, count, pairs_of):
    full = jnp.zeros((count,) + block.shape, block.dtype)
    full = lax.dynamic_update_index_in_dim(full, block, at, axis=0)
    for k in range(1, count):
        got = lax.ppermute(block, ("dp", "fsdp"), pairs_of(k))
        full = lax.dynamic_update_index_in_dim(full, got, (at - k + count) % count, axis=0)
    return full


def reduce_gradients(local_down, local_up, dp_count, fsdp_count):
    if dp_count != 32 or fsdp_count != 4:
        shard_down = lax.psum_scatter(local_down.astype(jnp.bfloat16), "fsdp", scatter_dimension=0, tiled=True)
        shard_up = lax.psum_scatter(local_up.astype(jnp.bfloat16), "fsdp", scatter_dimension=0, tiled=True)
        return (
            lax.psum(shard_down, "dp").astype(jnp.float32),
            lax.psum(shard_up, "dp").astype(jnp.float32),
        )
    d = lax.axis_index("dp")
    at = {"x": d // 8, "z": (d // 2) % 4, "core": d % 2, "y": lax.axis_index("fsdp")}
    sizes = {"x": dp_count // 8, "z": 4, "core": 2, "y": fsdp_count}
    down_size = local_down.size // fsdp_count
    chunk = 2 * down_size // (2 * sizes["x"] * sizes["z"])
    table = jnp.concatenate(
        [local_down.reshape(fsdp_count, down_size), local_up.reshape(fsdp_count, down_size)], axis=1
    ).reshape(fsdp_count, 2, sizes["x"], sizes["z"], chunk)

    def pairs(moved):
        return lambda k: coordinate_pairs(dp_count, fsdp_count, moved, k)

    halves = jnp.moveaxis(table, 1, 0)
    part = scatter_sum(halves, at["core"], 2, pairs("core"))
    part = scatter_sum(part, at["y"], fsdp_count, pairs("y"))
    part = scatter_sum(part, at["x"], sizes["x"], pairs("x"))
    part = scatter_sum(part, at["z"], sizes["z"], pairs("z"))
    part = gather_blocks(part.astype(jnp.bfloat16), at["z"], sizes["z"], pairs("z"))
    part = gather_blocks(part, at["x"], sizes["x"], pairs("x"))
    part = gather_blocks(part, at["core"], 2, pairs("core"))
    flat = part.reshape(-1).astype(jnp.float32)
    return (
        flat[:down_size].reshape(local_down.shape[0] // fsdp_count, local_down.shape[1]),
        flat[down_size:].reshape(local_up.shape[0] // fsdp_count, local_up.shape[1]),
    )


def on_device(
    latents, noise_draw, timesteps, buckets, owners, adv_grad, w_down, w_up, t_down, t_up
):
    tile_count, tile_side = (latents.shape[0], latents.shape[1])
    dp_count = lax.axis_size("dp")
    fsdp_count = lax.axis_size("fsdp")
    full_mask, half_mask = width_masks(buckets, tile_side)
    alpha_bar = jnp.square(jnp.cos(0.5 * jnp.pi * (timesteps.astype(jnp.float32) + 0.5) / TSTEPS))
    noisy = (
        full_mask
        * (
            jnp.sqrt(alpha_bar)[:, None, None, None] * latents.astype(jnp.float32)
            + jnp.sqrt(1.0 - alpha_bar)[:, None, None, None] * noise_draw.astype(jnp.float32)
        )
    ).astype(jnp.bfloat16)
    peer_cap = max(2, (tile_count + dp_count - 1) // dp_count)
    slot_count = dp_count * peer_cap
    hit_table = (owners[:, None] == jnp.arange(dp_count, dtype=jnp.int32)[None, :]).astype(
        jnp.int32
    )
    before = jnp.cumsum(hit_table, axis=0) - hit_table
    slot_of = owners * peer_cap + jnp.sum(before * hit_table, axis=1)
    slot_hits = slot_of[None, :] == jnp.arange(slot_count, dtype=jnp.int32)[:, None]
    spread_matrix = slot_hits.astype(jnp.bfloat16)
    send_noisy = (
        jnp.dot(spread_matrix, noisy.reshape(tile_count, -1), preferred_element_type=jnp.float32)
        .astype(jnp.bfloat16)
        .reshape(dp_count, peer_cap, -1)
    )
    send_code = jnp.sum(jnp.where(slot_hits, buckets[None, :] + 1, 0), axis=1).reshape(
        dp_count, peer_cap
    )
    teacher_down, teacher_up = gather_pair(t_down, t_up, dp_count, fsdp_count)
    recv_noisy, recv_code = (
        lax.all_to_all(send_noisy, "dp", split_axis=0, concat_axis=0, tiled=True),
        lax.all_to_all(send_code, "dp", split_axis=0, concat_axis=0, tiled=True),
    )
    flat_code = recv_code.reshape(slot_count)
    live_slot = (flat_code > 0).astype(jnp.int32)
    position = jnp.cumsum(live_slot) - live_slot
    pick_hits = (live_slot[None, :] == 1) & (
        position[None, :] == jnp.arange(tile_count, dtype=jnp.int32)[:, None]
    )
    pick_matrix = pick_hits.astype(jnp.bfloat16)
    own_noisy = (
        jnp.dot(pick_matrix, recv_noisy.reshape(slot_count, -1), preferred_element_type=jnp.float32)
        .astype(jnp.bfloat16)
        .reshape(latents.shape)
    )
    own_buckets = jnp.sum(jnp.where(pick_hits, flat_code[None, :] - 1, 0), axis=1).astype(jnp.int32)
    own_full, own_half = width_masks(own_buckets, tile_side)
    student_down, student_up = gather_pair(w_down, w_up, dp_count, fsdp_count)
    student, cached = network(own_noisy, own_full, own_half, student_down, student_up)
    target, _ = network(own_noisy, own_full, own_half, teacher_down, teacher_up)
    loss_scale = jnp.float32(1.0 / (tile_count * dp_count * fsdp_count))
    flipped = flip_kernel(student_up)
    d_out, d_hidden = cotangents(
        student, target, adv_grad, own_full, own_half, flipped, cached, loss_scale
    )
    local_down = kernel_grad(cached[0], d_hidden, 2)
    local_up = kernel_grad(cached[5], d_out, 1)
    grad_down, grad_up = reduce_gradients(local_down, local_up, dp_count, fsdp_count)
    return (student, grad_down, grad_up)


def solution(mesh):
    return jax.shard_map(
        on_device,
        mesh=mesh,
        in_specs=(
            P(("dp", "fsdp"), None, None, None),
            P(("dp", "fsdp"), None, None, None),
            P(("dp", "fsdp")),
            P(("dp", "fsdp")),
            P(("dp", "fsdp")),
            P(("dp", "fsdp"), None, None, None),
            P("fsdp", None),
            P("fsdp", None),
            P("fsdp", None),
            P("fsdp", None),
        ),
        out_specs=(P(("dp", "fsdp"), None, None, None), P("fsdp", None), P("fsdp", None)),
        check_vma=False,
    )
```

```python
import jax
import jax.numpy as jnp
from jax import lax
from jax.sharding import PartitionSpec as P

GROUPS = 32
TSTEPS = 1000


distill_weight = 2.5
norm_epsilon = 1e-05


def conv_forward(volume, kernel_rows, stride):
    in_chan = volume.shape[3]
    kernel = kernel_rows.reshape(3, 3, in_chan, kernel_rows.shape[1])
    return lax.conv_general_dilated(
        volume,
        kernel,
        (stride, stride),
        ((1, 1), (1, 1)),
        dimension_numbers=("NHWC", "HWIO", "NHWC"),
        preferred_element_type=jnp.float32,
    )


def kernel_grad(volume, cotangent, stride):
    pad_upper = 1 if stride == 1 else 0
    result_grad = lax.conv_general_dilated(
        volume,
        cotangent,
        (1, 1),
        ((1, pad_upper), (1, pad_upper)),
        rhs_dilation=(stride, stride),
        dimension_numbers=("CHWN", "IHWO", "HWNC"),
        preferred_element_type=jnp.float32,
    )
    return result_grad.reshape(9 * volume.shape[3], cotangent.shape[3])


def width_masks(buckets, tile_side):
    half_side = tile_side // 2
    tile_count = buckets.shape[0]
    columns = jnp.arange(tile_side, dtype=jnp.int32)
    full_mask = (
        columns[None, None, :, None] < (tile_side - 2 * buckets)[:, None, None, None]
    ).astype(jnp.float32)
    full_mask = jnp.broadcast_to(full_mask, (tile_count, tile_side, tile_side, 1))
    half_cols = jnp.arange(half_side, dtype=jnp.int32)
    half_mask = (
        half_cols[None, None, :, None] < (half_side - buckets)[:, None, None, None]
    ).astype(jnp.float32)
    half_mask = jnp.broadcast_to(half_mask, (tile_count, half_side, half_side, 1))
    return (full_mask, half_mask)


def group_stats(hidden, half_mask):
    tile_count, height, breadth, channels = hidden.shape
    grouped = hidden.reshape(tile_count, height * breadth, GROUPS, channels // GROUPS)
    live_weight = half_mask.reshape(tile_count, height * breadth, 1, 1)
    population = jnp.sum(live_weight, axis=(1, 3), keepdims=True) * (channels // GROUPS)
    center = jnp.sum(grouped * live_weight, axis=(1, 3), keepdims=True) / population
    spread = (
        jnp.sum(jnp.square(grouped - center) * live_weight, axis=(1, 3), keepdims=True) / population
    )
    inverse = lax.rsqrt(spread + norm_epsilon)
    normed = ((grouped - center) * inverse).reshape(hidden.shape)
    return (normed, inverse, population)


def group_back(d_norm, normed, inverse, population, half_mask):
    tile_count, height, breadth, channels = d_norm.shape
    grouped_d = d_norm.reshape(tile_count, height * breadth, GROUPS, channels // GROUPS)
    grouped_n = normed.reshape(tile_count, height * breadth, GROUPS, channels // GROUPS)
    live_weight = half_mask.reshape(tile_count, height * breadth, 1, 1)
    mean_first = jnp.sum(grouped_d, axis=(1, 3), keepdims=True) / population
    mean_second = jnp.sum(grouped_d * grouped_n, axis=(1, 3), keepdims=True) / population
    result = live_weight * inverse * (grouped_d - mean_first - grouped_n * mean_second)
    return result.reshape(d_norm.shape)


def upsample(activated):
    return jnp.repeat(jnp.repeat(activated, 2, axis=1), 2, axis=2)


def network(noisy, full_mask, half_mask, down_weight, up_weight):
    hidden = conv_forward(noisy, down_weight, 2)
    normed, inverse, population = group_stats(hidden, half_mask)
    activated = (half_mask * jax.nn.silu(normed)).astype(jnp.bfloat16)
    enlarged = upsample(activated)
    output = conv_forward(enlarged, up_weight, 1)
    student = (full_mask * (noisy.astype(jnp.float32) + output)).astype(jnp.bfloat16)
    return (student, (noisy, normed, inverse, population, activated, enlarged))


def flip_kernel(up_weight):
    up_chan = up_weight.shape[0] // 9
    out_chan = up_weight.shape[1]
    return (
        up_weight.reshape(3, 3, up_chan, out_chan)[::-1, ::-1]
        .transpose(0, 1, 3, 2)
        .reshape(9 * out_chan, up_chan)
    )


def cotangents(student, target, adversarial, full_mask, half_mask, flipped, cached, loss_scale):
    source_in, normed, inverse, population, activated, enlarged = cached
    tile_count, tile_side = (student.shape[0], student.shape[1])
    half_side = tile_side // 2
    d_out = (
        full_mask
        * (
            distill_weight * (student.astype(jnp.float32) - target.astype(jnp.float32))
            + adversarial.astype(jnp.float32)
        )
        * loss_scale
    ).astype(jnp.bfloat16)
    d_up = conv_forward(d_out, flipped, 1)
    d_up = d_up.reshape(tile_count, half_side, 2, half_side, 2, flipped.shape[1])
    d_act = jnp.sum(d_up, axis=(2, 4))
    sigmoid_n = jax.nn.sigmoid(normed)
    d_norm = half_mask * d_act * sigmoid_n * (1.0 + normed * (1.0 - sigmoid_n))
    d_hidden = group_back(d_norm, normed, inverse, population, half_mask).astype(jnp.bfloat16)
    return (d_out, d_hidden)


def ring_gather(shards, dp_count, fsdp_count):
    fsdp_at = lax.axis_index("fsdp")
    core = lax.axis_index("dp") % 2
    step = 1 - 2 * core

    def lin(d, f):
        return d * fsdp_count + f

    ring_pairs = []
    for d in range(dp_count):
        toward = -1 if d % 2 == 0 else 1
        for f in range(fsdp_count):
            ring_pairs.append((lin(d, f), lin(d, (f + toward) % fsdp_count)))
    first = lax.ppermute(shards, ("dp", "fsdp"), ring_pairs)
    halves = tuple(
        lax.dynamic_slice_in_dim(piece, core * (piece.shape[0] // 2), piece.shape[0] // 2, axis=0)
        for piece in first
    )
    second = lax.ppermute(halves, ("dp", "fsdp"), ring_pairs)
    swap_pairs = [(d, d ^ 1) for d in range(dp_count)]
    other_first, other_second = lax.ppermute((first, second), "dp", swap_pairs)
    near = (fsdp_at + step + fsdp_count) % fsdp_count
    behind = (fsdp_at - step + fsdp_count) % fsdp_count
    far = (fsdp_at + 2) % fsdp_count
    gathered = []
    for own, got, got_other, half, half_other in zip(shards, first, other_first, second, other_second):
        rows = own.shape[0]
        full = jnp.zeros((fsdp_count * rows,) + own.shape[1:], own.dtype)
        full = lax.dynamic_update_slice_in_dim(full, own, fsdp_at * rows, axis=0)
        full = lax.dynamic_update_slice_in_dim(full, got, near * rows, axis=0)
        full = lax.dynamic_update_slice_in_dim(full, got_other, behind * rows, axis=0)
        full = lax.dynamic_update_slice_in_dim(full, half, far * rows + core * (rows // 2), axis=0)
        full = lax.dynamic_update_slice_in_dim(
            full, half_other, far * rows + (1 - core) * (rows // 2), axis=0
        )
        gathered.append(full)
    return tuple(gathered)


def gather_pair(down_rows, up_rows, dp_count, fsdp_count):
    if fsdp_count != 4 or dp_count % 2 or down_rows.shape[0] % 2 or up_rows.shape[0] % 2:
        return (
            lax.all_gather(down_rows, "fsdp", axis=0, tiled=True),
            lax.all_gather(up_rows, "fsdp", axis=0, tiled=True),
        )
    return ring_gather((down_rows, up_rows), dp_count, fsdp_count)


def coordinate_pairs(dp_count, fsdp_count, moved, shift):
    sizes = {"x": dp_count // 8, "z": 4, "core": 2, "y": fsdp_count}
    pairs = []
    for d in range(dp_count):
        for f in range(fsdp_count):
            place = {"x": d // 8, "z": (d // 2) % 4, "core": d % 2, "y": f}
            place[moved] = (place[moved] + shift) % sizes[moved]
            target = (place["x"] * 8 + place["z"] * 2 + place["core"]) * fsdp_count + place["y"]
            pairs.append((d * fsdp_count + f, target))
    return pairs


def scatter_sum(parts, at, count, pairs_of, axis=0):
    total = lax.dynamic_index_in_dim(parts, at, axis=axis, keepdims=False)
    for k in range(1, count):
        sent = lax.dynamic_index_in_dim(parts, (at + k) % count, axis=axis, keepdims=False)
        got = lax.ppermute(sent.astype(jnp.bfloat16), ("dp", "fsdp"), pairs_of(k))
        total = total + got.astype(jnp.float32)
    return total


def gather_blocks(block, at, count, pairs_of):
    full = jnp.zeros((count,) + block.shape, block.dtype)
    full = lax.dynamic_update_index_in_dim(full, block, at, axis=0)
    for k in range(1, count):
        got = lax.ppermute(block, ("dp", "fsdp"), pairs_of(k))
        full = lax.dynamic_update_index_in_dim(full, got, (at - k + count) % count, axis=0)
    return full


def reduce_gradients(local_down, local_up, dp_count, fsdp_count):
    d = lax.axis_index("dp")
    at = {"x": d // 8, "z": (d // 2) % 4, "core": d % 2, "y": lax.axis_index("fsdp")}
    sizes = {"x": dp_count // 8, "z": 4, "core": 2, "y": fsdp_count}
    down_size = local_down.size // fsdp_count
    chunk = 2 * down_size // (2 * sizes["x"] * sizes["z"])
    if dp_count != 32 or fsdp_count != 4 or chunk % 3:
        shard_down = lax.psum_scatter(local_down.astype(jnp.bfloat16), "fsdp", scatter_dimension=0, tiled=True)
        shard_up = lax.psum_scatter(local_up.astype(jnp.bfloat16), "fsdp", scatter_dimension=0, tiled=True)
        return (
            lax.psum(shard_down, "dp").astype(jnp.float32),
            lax.psum(shard_up, "dp").astype(jnp.float32),
        )
    table = jnp.concatenate(
        [local_down.reshape(fsdp_count, down_size), local_up.reshape(fsdp_count, down_size)], axis=1
    ).reshape(fsdp_count, 2, sizes["x"], sizes["z"], chunk)

    def pairs(moved):
        return lambda k: coordinate_pairs(dp_count, fsdp_count, moved, k)

    halves = jnp.moveaxis(table, 1, 0)
    part = scatter_sum(halves, at["core"], 2, pairs("core"))
    colour = chunk // 3
    axes = ("y", "x", "z")
    done = []
    for c, order in enumerate((("y", "x", "z"), ("x", "z", "y"), ("z", "y", "x"))):
        piece = part[..., c * colour:(c + 1) * colour]
        left = list(axes)
        for name in order:
            piece = scatter_sum(piece, at[name], sizes[name], pairs(name), axis=left.index(name))
            left.remove(name)
        if c == 1:
            piece = gather_blocks(piece.astype(jnp.bfloat16), at["x"], sizes["x"], pairs("x"))
            piece = gather_blocks(piece, at["z"], sizes["z"], pairs("z"))
            piece = jnp.swapaxes(piece, 0, 1)
        else:
            piece = gather_blocks(piece.astype(jnp.bfloat16), at["z"], sizes["z"], pairs("z"))
            piece = gather_blocks(piece, at["x"], sizes["x"], pairs("x"))
        done.append(piece)
    part = jnp.concatenate(done, axis=-1)
    part = gather_blocks(part, at["core"], 2, pairs("core"))
    flat = part.reshape(-1).astype(jnp.float32)
    return (
        flat[:down_size].reshape(local_down.shape[0] // fsdp_count, local_down.shape[1]),
        flat[down_size:].reshape(local_up.shape[0] // fsdp_count, local_up.shape[1]),
    )


def on_device(
    latents, noise_draw, timesteps, buckets, owners, adv_grad, w_down, w_up, t_down, t_up
):
    tile_count, tile_side = (latents.shape[0], latents.shape[1])
    dp_count = lax.axis_size("dp")
    fsdp_count = lax.axis_size("fsdp")
    full_mask, half_mask = width_masks(buckets, tile_side)
    alpha_bar = jnp.square(jnp.cos(0.5 * jnp.pi * (timesteps.astype(jnp.float32) + 0.5) / TSTEPS))
    noisy = (
        full_mask
        * (
            jnp.sqrt(alpha_bar)[:, None, None, None] * latents.astype(jnp.float32)
            + jnp.sqrt(1.0 - alpha_bar)[:, None, None, None] * noise_draw.astype(jnp.float32)
        )
    ).astype(jnp.bfloat16)
    peer_cap = max(2, (tile_count + dp_count - 1) // dp_count)
    slot_count = dp_count * peer_cap
    hit_table = (owners[:, None] == jnp.arange(dp_count, dtype=jnp.int32)[None, :]).astype(
        jnp.int32
    )
    before = jnp.cumsum(hit_table, axis=0) - hit_table
    slot_of = owners * peer_cap + jnp.sum(before * hit_table, axis=1)
    slot_hits = slot_of[None, :] == jnp.arange(slot_count, dtype=jnp.int32)[:, None]
    spread_matrix = slot_hits.astype(jnp.bfloat16)
    send_noisy = (
        jnp.dot(spread_matrix, noisy.reshape(tile_count, -1), preferred_element_type=jnp.float32)
        .astype(jnp.bfloat16)
        .reshape(dp_count, peer_cap, -1)
    )
    send_code = jnp.sum(jnp.where(slot_hits, buckets[None, :] + 1, 0), axis=1).reshape(
        dp_count, peer_cap
    )
    teacher_down, teacher_up = gather_pair(t_down, t_up, dp_count, fsdp_count)
    recv_noisy, recv_code = (
        lax.all_to_all(send_noisy, "dp", split_axis=0, concat_axis=0, tiled=True),
        lax.all_to_all(send_code, "dp", split_axis=0, concat_axis=0, tiled=True),
    )
    flat_code = recv_code.reshape(slot_count)
    live_slot = (flat_code > 0).astype(jnp.int32)
    position = jnp.cumsum(live_slot) - live_slot
    pick_hits = (live_slot[None, :] == 1) & (
        position[None, :] == jnp.arange(tile_count, dtype=jnp.int32)[:, None]
    )
    pick_matrix = pick_hits.astype(jnp.bfloat16)
    own_noisy = (
        jnp.dot(pick_matrix, recv_noisy.reshape(slot_count, -1), preferred_element_type=jnp.float32)
        .astype(jnp.bfloat16)
        .reshape(latents.shape)
    )
    own_buckets = jnp.sum(jnp.where(pick_hits, flat_code[None, :] - 1, 0), axis=1).astype(jnp.int32)
    own_full, own_half = width_masks(own_buckets, tile_side)
    student_down, student_up = gather_pair(w_down, w_up, dp_count, fsdp_count)
    student, cached = network(own_noisy, own_full, own_half, student_down, student_up)
    target, _ = network(own_noisy, own_full, own_half, teacher_down, teacher_up)
    loss_scale = jnp.float32(1.0 / (tile_count * dp_count * fsdp_count))
    flipped = flip_kernel(student_up)
    d_out, d_hidden = cotangents(
        student, target, adv_grad, own_full, own_half, flipped, cached, loss_scale
    )
    local_down = kernel_grad(cached[0], d_hidden, 2)
    local_up = kernel_grad(cached[5], d_out, 1)
    grad_down, grad_up = reduce_gradients(local_down, local_up, dp_count, fsdp_count)
    return (student, grad_down, grad_up)


def solution(mesh):
    return jax.shard_map(
        on_device,
        mesh=mesh,
        in_specs=(
            P(("dp", "fsdp"), None, None, None),
            P(("dp", "fsdp"), None, None, None),
            P(("dp", "fsdp")),
            P(("dp", "fsdp")),
            P(("dp", "fsdp")),
            P(("dp", "fsdp"), None, None, None),
            P("fsdp", None),
            P("fsdp", None),
            P("fsdp", None),
            P("fsdp", None),
        ),
        out_specs=(P(("dp", "fsdp"), None, None, None), P("fsdp", None), P("fsdp", None)),
        check_vma=False,
    )
```

```python
import jax
import jax.numpy as jnp
from jax import lax
from jax.sharding import PartitionSpec as P

GROUPS = 32
TSTEPS = 1000


distill_weight = 2.5
norm_epsilon = 1e-05


def conv_forward(volume, kernel_rows, stride):
    in_chan = volume.shape[3]
    kernel = kernel_rows.reshape(3, 3, in_chan, kernel_rows.shape[1])
    return lax.conv_general_dilated(
        volume,
        kernel,
        (stride, stride),
        ((1, 1), (1, 1)),
        dimension_numbers=("NHWC", "HWIO", "NHWC"),
        preferred_element_type=jnp.float32,
    )


def kernel_grad(volume, cotangent, stride):
    pad_upper = 1 if stride == 1 else 0
    result_grad = lax.conv_general_dilated(
        volume,
        cotangent,
        (1, 1),
        ((1, pad_upper), (1, pad_upper)),
        rhs_dilation=(stride, stride),
        dimension_numbers=("CHWN", "IHWO", "HWNC"),
        preferred_element_type=jnp.float32,
    )
    return result_grad.reshape(9 * volume.shape[3], cotangent.shape[3])


def width_masks(buckets, tile_side):
    half_side = tile_side // 2
    tile_count = buckets.shape[0]
    columns = jnp.arange(tile_side, dtype=jnp.int32)
    full_mask = (
        columns[None, None, :, None] < (tile_side - 2 * buckets)[:, None, None, None]
    ).astype(jnp.float32)
    full_mask = jnp.broadcast_to(full_mask, (tile_count, tile_side, tile_side, 1))
    half_cols = jnp.arange(half_side, dtype=jnp.int32)
    half_mask = (
        half_cols[None, None, :, None] < (half_side - buckets)[:, None, None, None]
    ).astype(jnp.float32)
    half_mask = jnp.broadcast_to(half_mask, (tile_count, half_side, half_side, 1))
    return (full_mask, half_mask)


def group_stats(hidden, half_mask):
    tile_count, height, breadth, channels = hidden.shape
    grouped = hidden.reshape(tile_count, height * breadth, GROUPS, channels // GROUPS)
    live_weight = half_mask.reshape(tile_count, height * breadth, 1, 1)
    population = jnp.sum(live_weight, axis=(1, 3), keepdims=True) * (channels // GROUPS)
    center = jnp.sum(grouped * live_weight, axis=(1, 3), keepdims=True) / population
    spread = (
        jnp.sum(jnp.square(grouped - center) * live_weight, axis=(1, 3), keepdims=True) / population
    )
    inverse = lax.rsqrt(spread + norm_epsilon)
    normed = ((grouped - center) * inverse).reshape(hidden.shape)
    return (normed, inverse, population)


def group_back(d_norm, normed, inverse, population, half_mask):
    tile_count, height, breadth, channels = d_norm.shape
    grouped_d = d_norm.reshape(tile_count, height * breadth, GROUPS, channels // GROUPS)
    grouped_n = normed.reshape(tile_count, height * breadth, GROUPS, channels // GROUPS)
    live_weight = half_mask.reshape(tile_count, height * breadth, 1, 1)
    mean_first = jnp.sum(grouped_d, axis=(1, 3), keepdims=True) / population
    mean_second = jnp.sum(grouped_d * grouped_n, axis=(1, 3), keepdims=True) / population
    result = live_weight * inverse * (grouped_d - mean_first - grouped_n * mean_second)
    return result.reshape(d_norm.shape)


def upsample(activated):
    return jnp.repeat(jnp.repeat(activated, 2, axis=1), 2, axis=2)


def network(noisy, full_mask, half_mask, down_weight, up_weight):
    hidden = conv_forward(noisy, down_weight, 2)
    normed, inverse, population = group_stats(hidden, half_mask)
    activated = (half_mask * jax.nn.silu(normed)).astype(jnp.bfloat16)
    enlarged = upsample(activated)
    output = conv_forward(enlarged, up_weight, 1)
    student = (full_mask * (noisy.astype(jnp.float32) + output)).astype(jnp.bfloat16)
    return (student, (noisy, normed, inverse, population, activated, enlarged))


def flip_kernel(up_weight):
    up_chan = up_weight.shape[0] // 9
    out_chan = up_weight.shape[1]
    return (
        up_weight.reshape(3, 3, up_chan, out_chan)[::-1, ::-1]
        .transpose(0, 1, 3, 2)
        .reshape(9 * out_chan, up_chan)
    )


def cotangents(student, target, adversarial, full_mask, half_mask, flipped, cached, loss_scale):
    source_in, normed, inverse, population, activated, enlarged = cached
    tile_count, tile_side = (student.shape[0], student.shape[1])
    half_side = tile_side // 2
    d_out = (
        full_mask
        * (
            distill_weight * (student.astype(jnp.float32) - target.astype(jnp.float32))
            + adversarial.astype(jnp.float32)
        )
        * loss_scale
    ).astype(jnp.bfloat16)
    d_up = conv_forward(d_out, flipped, 1)
    d_up = d_up.reshape(tile_count, half_side, 2, half_side, 2, flipped.shape[1])
    d_act = jnp.sum(d_up, axis=(2, 4))
    sigmoid_n = jax.nn.sigmoid(normed)
    d_norm = half_mask * d_act * sigmoid_n * (1.0 + normed * (1.0 - sigmoid_n))
    d_hidden = group_back(d_norm, normed, inverse, population, half_mask).astype(jnp.bfloat16)
    return (d_out, d_hidden)


def ring_gather(shards, dp_count, fsdp_count):
    fsdp_at = lax.axis_index("fsdp")
    core = lax.axis_index("dp") % 2
    step = 1 - 2 * core

    def lin(d, f):
        return d * fsdp_count + f

    ring_pairs = []
    for d in range(dp_count):
        toward = -1 if d % 2 == 0 else 1
        for f in range(fsdp_count):
            ring_pairs.append((lin(d, f), lin(d, (f + toward) % fsdp_count)))
    first = lax.ppermute(shards, ("dp", "fsdp"), ring_pairs)
    halves = tuple(
        lax.dynamic_slice_in_dim(piece, core * (piece.shape[0] // 2), piece.shape[0] // 2, axis=0)
        for piece in first
    )
    second = lax.ppermute(halves, ("dp", "fsdp"), ring_pairs)
    swap_pairs = [(d, d ^ 1) for d in range(dp_count)]
    other_first, other_second = lax.ppermute((first, second), "dp", swap_pairs)
    near = (fsdp_at + step + fsdp_count) % fsdp_count
    behind = (fsdp_at - step + fsdp_count) % fsdp_count
    far = (fsdp_at + 2) % fsdp_count
    gathered = []
    for own, got, got_other, half, half_other in zip(shards, first, other_first, second, other_second):
        rows = own.shape[0]
        full = jnp.zeros((fsdp_count * rows,) + own.shape[1:], own.dtype)
        full = lax.dynamic_update_slice_in_dim(full, own, fsdp_at * rows, axis=0)
        full = lax.dynamic_update_slice_in_dim(full, got, near * rows, axis=0)
        full = lax.dynamic_update_slice_in_dim(full, got_other, behind * rows, axis=0)
        full = lax.dynamic_update_slice_in_dim(full, half, far * rows + core * (rows // 2), axis=0)
        full = lax.dynamic_update_slice_in_dim(
            full, half_other, far * rows + (1 - core) * (rows // 2), axis=0
        )
        gathered.append(full)
    return tuple(gathered)


def gather_pair(down_rows, up_rows, dp_count, fsdp_count):
    if fsdp_count != 4 or dp_count % 2 or down_rows.shape[0] % 2 or up_rows.shape[0] % 2:
        return (
            lax.all_gather(down_rows, "fsdp", axis=0, tiled=True),
            lax.all_gather(up_rows, "fsdp", axis=0, tiled=True),
        )
    return ring_gather((down_rows, up_rows), dp_count, fsdp_count)


def coordinate_pairs(dp_count, fsdp_count, moved, shift):
    sizes = {"x": dp_count // 8, "z": 4, "core": 2, "y": fsdp_count}
    pairs = []
    for d in range(dp_count):
        for f in range(fsdp_count):
            place = {"x": d // 8, "z": (d // 2) % 4, "core": d % 2, "y": f}
            place[moved] = (place[moved] + shift) % sizes[moved]
            target = (place["x"] * 8 + place["z"] * 2 + place["core"]) * fsdp_count + place["y"]
            pairs.append((d * fsdp_count + f, target))
    return pairs


def scatter_sum(parts, at, count, pairs_of, axis=0):
    total = lax.dynamic_index_in_dim(parts, at, axis=axis, keepdims=False)
    for k in range(1, count):
        sent = lax.dynamic_index_in_dim(parts, (at + k) % count, axis=axis, keepdims=False)
        got = lax.ppermute(sent.astype(jnp.bfloat16), ("dp", "fsdp"), pairs_of(k))
        total = total + got.astype(jnp.float32)
    return total


def gather_blocks(block, at, count, pairs_of):
    full = jnp.zeros((count,) + block.shape, block.dtype)
    full = lax.dynamic_update_index_in_dim(full, block, at, axis=0)
    for k in range(1, count):
        got = lax.ppermute(block, ("dp", "fsdp"), pairs_of(k))
        full = lax.dynamic_update_index_in_dim(full, got, (at - k + count) % count, axis=0)
    return full


def reduce_gradients(local_down, local_up, dp_count, fsdp_count):
    d = lax.axis_index("dp")
    at = {"x": d // 8, "z": (d // 2) % 4, "core": d % 2, "y": lax.axis_index("fsdp")}
    sizes = {"x": dp_count // 8, "z": 4, "core": 2, "y": fsdp_count}
    down_size = local_down.size // fsdp_count
    chunk = 2 * down_size // (2 * sizes["x"] * sizes["z"])
    if dp_count != 32 or fsdp_count != 4 or chunk % 2:
        shard_down = lax.psum_scatter(local_down.astype(jnp.bfloat16), "fsdp", scatter_dimension=0, tiled=True)
        shard_up = lax.psum_scatter(local_up.astype(jnp.bfloat16), "fsdp", scatter_dimension=0, tiled=True)
        return (
            lax.psum(shard_down, "dp").astype(jnp.float32),
            lax.psum(shard_up, "dp").astype(jnp.float32),
        )
    table = jnp.concatenate(
        [local_down.reshape(fsdp_count, down_size), local_up.reshape(fsdp_count, down_size)], axis=1
    ).reshape(fsdp_count, 2, sizes["x"], sizes["z"], chunk)

    def pairs(moved):
        return lambda k: coordinate_pairs(dp_count, fsdp_count, moved, k)

    halves = jnp.moveaxis(table, 1, 0)
    part = scatter_sum(halves, at["core"], 2, pairs("core"))
    colour = chunk // 2
    done = []
    for c, order in enumerate((("y", "x"), ("x", "y"))):
        piece = part[..., c * colour:(c + 1) * colour]
        left = ["y", "x", "z"]
        for name in order:
            piece = scatter_sum(piece, at[name], sizes[name], pairs(name), axis=left.index(name))
            left.remove(name)
        done.append(piece)
    part = jnp.concatenate(done, axis=-1)
    part = scatter_sum(part, at["z"], sizes["z"], pairs("z"))
    part = gather_blocks(part.astype(jnp.bfloat16), at["z"], sizes["z"], pairs("z"))
    part = gather_blocks(part, at["x"], sizes["x"], pairs("x"))
    part = gather_blocks(part, at["core"], 2, pairs("core"))
    flat = part.reshape(-1).astype(jnp.float32)
    return (
        flat[:down_size].reshape(local_down.shape[0] // fsdp_count, local_down.shape[1]),
        flat[down_size:].reshape(local_up.shape[0] // fsdp_count, local_up.shape[1]),
    )


def on_device(
    latents, noise_draw, timesteps, buckets, owners, adv_grad, w_down, w_up, t_down, t_up
):
    tile_count, tile_side = (latents.shape[0], latents.shape[1])
    dp_count = lax.axis_size("dp")
    fsdp_count = lax.axis_size("fsdp")
    full_mask, half_mask = width_masks(buckets, tile_side)
    alpha_bar = jnp.square(jnp.cos(0.5 * jnp.pi * (timesteps.astype(jnp.float32) + 0.5) / TSTEPS))
    noisy = (
        full_mask
        * (
            jnp.sqrt(alpha_bar)[:, None, None, None] * latents.astype(jnp.float32)
            + jnp.sqrt(1.0 - alpha_bar)[:, None, None, None] * noise_draw.astype(jnp.float32)
        )
    ).astype(jnp.bfloat16)
    peer_cap = max(2, (tile_count + dp_count - 1) // dp_count)
    slot_count = dp_count * peer_cap
    hit_table = (owners[:, None] == jnp.arange(dp_count, dtype=jnp.int32)[None, :]).astype(
        jnp.int32
    )
    before = jnp.cumsum(hit_table, axis=0) - hit_table
    slot_of = owners * peer_cap + jnp.sum(before * hit_table, axis=1)
    slot_hits = slot_of[None, :] == jnp.arange(slot_count, dtype=jnp.int32)[:, None]
    spread_matrix = slot_hits.astype(jnp.bfloat16)
    send_noisy = (
        jnp.dot(spread_matrix, noisy.reshape(tile_count, -1), preferred_element_type=jnp.float32)
        .astype(jnp.bfloat16)
        .reshape(dp_count, peer_cap, -1)
    )
    send_code = jnp.sum(jnp.where(slot_hits, buckets[None, :] + 1, 0), axis=1).reshape(
        dp_count, peer_cap
    )
    teacher_down, teacher_up = gather_pair(t_down, t_up, dp_count, fsdp_count)
    recv_noisy, recv_code = (
        lax.all_to_all(send_noisy, "dp", split_axis=0, concat_axis=0, tiled=True),
        lax.all_to_all(send_code, "dp", split_axis=0, concat_axis=0, tiled=True),
    )
    flat_code = recv_code.reshape(slot_count)
    live_slot = (flat_code > 0).astype(jnp.int32)
    position = jnp.cumsum(live_slot) - live_slot
    pick_hits = (live_slot[None, :] == 1) & (
        position[None, :] == jnp.arange(tile_count, dtype=jnp.int32)[:, None]
    )
    pick_matrix = pick_hits.astype(jnp.bfloat16)
    own_noisy = (
        jnp.dot(pick_matrix, recv_noisy.reshape(slot_count, -1), preferred_element_type=jnp.float32)
        .astype(jnp.bfloat16)
        .reshape(latents.shape)
    )
    own_buckets = jnp.sum(jnp.where(pick_hits, flat_code[None, :] - 1, 0), axis=1).astype(jnp.int32)
    own_full, own_half = width_masks(own_buckets, tile_side)
    student_down, student_up = gather_pair(w_down, w_up, dp_count, fsdp_count)
    student, cached = network(own_noisy, own_full, own_half, student_down, student_up)
    target, _ = network(own_noisy, own_full, own_half, teacher_down, teacher_up)
    loss_scale = jnp.float32(1.0 / (tile_count * dp_count * fsdp_count))
    flipped = flip_kernel(student_up)
    d_out, d_hidden = cotangents(
        student, target, adv_grad, own_full, own_half, flipped, cached, loss_scale
    )
    local_down = kernel_grad(cached[0], d_hidden, 2)
    local_up = kernel_grad(cached[5], d_out, 1)
    grad_down, grad_up = reduce_gradients(local_down, local_up, dp_count, fsdp_count)
    return (student, grad_down, grad_up)


def solution(mesh):
    return jax.shard_map(
        on_device,
        mesh=mesh,
        in_specs=(
            P(("dp", "fsdp"), None, None, None),
            P(("dp", "fsdp"), None, None, None),
            P(("dp", "fsdp")),
            P(("dp", "fsdp")),
            P(("dp", "fsdp")),
            P(("dp", "fsdp"), None, None, None),
            P("fsdp", None),
            P("fsdp", None),
            P("fsdp", None),
            P("fsdp", None),
        ),
        out_specs=(P(("dp", "fsdp"), None, None, None), P("fsdp", None), P("fsdp", None)),
        check_vma=False,
    )
```

```python
import jax
import jax.numpy as jnp
from jax import lax
from jax.sharding import PartitionSpec as P

GROUPS = 32
TSTEPS = 1000


distill_weight = 2.5
norm_epsilon = 1e-05


def conv_forward(volume, kernel_rows, stride):
    in_chan = volume.shape[3]
    kernel = kernel_rows.reshape(3, 3, in_chan, kernel_rows.shape[1])
    return lax.conv_general_dilated(
        volume,
        kernel,
        (stride, stride),
        ((1, 1), (1, 1)),
        dimension_numbers=("NHWC", "HWIO", "NHWC"),
        preferred_element_type=jnp.float32,
    )


def kernel_grad(volume, cotangent, stride):
    pad_upper = 1 if stride == 1 else 0
    result_grad = lax.conv_general_dilated(
        volume,
        cotangent,
        (1, 1),
        ((1, pad_upper), (1, pad_upper)),
        rhs_dilation=(stride, stride),
        dimension_numbers=("CHWN", "IHWO", "HWNC"),
        preferred_element_type=jnp.float32,
    )
    return result_grad.reshape(9 * volume.shape[3], cotangent.shape[3])


def width_masks(buckets, tile_side):
    half_side = tile_side // 2
    tile_count = buckets.shape[0]
    columns = jnp.arange(tile_side, dtype=jnp.int32)
    full_mask = (
        columns[None, None, :, None] < (tile_side - 2 * buckets)[:, None, None, None]
    ).astype(jnp.float32)
    full_mask = jnp.broadcast_to(full_mask, (tile_count, tile_side, tile_side, 1))
    half_cols = jnp.arange(half_side, dtype=jnp.int32)
    half_mask = (
        half_cols[None, None, :, None] < (half_side - buckets)[:, None, None, None]
    ).astype(jnp.float32)
    half_mask = jnp.broadcast_to(half_mask, (tile_count, half_side, half_side, 1))
    return (full_mask, half_mask)


def group_stats(hidden, half_mask):
    tile_count, height, breadth, channels = hidden.shape
    grouped = hidden.reshape(tile_count, height * breadth, GROUPS, channels // GROUPS)
    live_weight = half_mask.reshape(tile_count, height * breadth, 1, 1)
    population = jnp.sum(live_weight, axis=(1, 3), keepdims=True) * (channels // GROUPS)
    center = jnp.sum(grouped * live_weight, axis=(1, 3), keepdims=True) / population
    spread = (
        jnp.sum(jnp.square(grouped - center) * live_weight, axis=(1, 3), keepdims=True) / population
    )
    inverse = lax.rsqrt(spread + norm_epsilon)
    normed = ((grouped - center) * inverse).reshape(hidden.shape)
    return (normed, inverse, population)


def group_back(d_norm, normed, inverse, population, half_mask):
    tile_count, height, breadth, channels = d_norm.shape
    grouped_d = d_norm.reshape(tile_count, height * breadth, GROUPS, channels // GROUPS)
    grouped_n = normed.reshape(tile_count, height * breadth, GROUPS, channels // GROUPS)
    live_weight = half_mask.reshape(tile_count, height * breadth, 1, 1)
    mean_first = jnp.sum(grouped_d, axis=(1, 3), keepdims=True) / population
    mean_second = jnp.sum(grouped_d * grouped_n, axis=(1, 3), keepdims=True) / population
    result = live_weight * inverse * (grouped_d - mean_first - grouped_n * mean_second)
    return result.reshape(d_norm.shape)


def upsample(activated):
    return jnp.repeat(jnp.repeat(activated, 2, axis=1), 2, axis=2)


def network(noisy, full_mask, half_mask, down_weight, up_weight):
    hidden = conv_forward(noisy, down_weight, 2)
    normed, inverse, population = group_stats(hidden, half_mask)
    activated = (half_mask * jax.nn.silu(normed)).astype(jnp.bfloat16)
    enlarged = upsample(activated)
    output = conv_forward(enlarged, up_weight, 1)
    student = (full_mask * (noisy.astype(jnp.float32) + output)).astype(jnp.bfloat16)
    return (student, (noisy, normed, inverse, population, activated, enlarged))


def flip_kernel(up_weight):
    up_chan = up_weight.shape[0] // 9
    out_chan = up_weight.shape[1]
    return (
        up_weight.reshape(3, 3, up_chan, out_chan)[::-1, ::-1]
        .transpose(0, 1, 3, 2)
        .reshape(9 * out_chan, up_chan)
    )


def cotangents(student, target, adversarial, full_mask, half_mask, flipped, cached, loss_scale):
    source_in, normed, inverse, population, activated, enlarged = cached
    tile_count, tile_side = (student.shape[0], student.shape[1])
    half_side = tile_side // 2
    d_out = (
        full_mask
        * (
            distill_weight * (student.astype(jnp.float32) - target.astype(jnp.float32))
            + adversarial.astype(jnp.float32)
        )
        * loss_scale
    ).astype(jnp.bfloat16)
    d_up = conv_forward(d_out, flipped, 1)
    d_up = d_up.reshape(tile_count, half_side, 2, half_side, 2, flipped.shape[1])
    d_act = jnp.sum(d_up, axis=(2, 4))
    sigmoid_n = jax.nn.sigmoid(normed)
    d_norm = half_mask * d_act * sigmoid_n * (1.0 + normed * (1.0 - sigmoid_n))
    d_hidden = group_back(d_norm, normed, inverse, population, half_mask).astype(jnp.bfloat16)
    return (d_out, d_hidden)


def ring_gather(shards, dp_count, fsdp_count):
    fsdp_at = lax.axis_index("fsdp")
    core = lax.axis_index("dp") % 2
    step = 1 - 2 * core

    def lin(d, f):
        return d * fsdp_count + f

    ring_pairs = []
    for d in range(dp_count):
        toward = -1 if d % 2 == 0 else 1
        for f in range(fsdp_count):
            ring_pairs.append((lin(d, f), lin(d, (f + toward) % fsdp_count)))
    first = lax.ppermute(shards, ("dp", "fsdp"), ring_pairs)
    halves = tuple(
        lax.dynamic_slice_in_dim(piece, core * (piece.shape[0] // 2), piece.shape[0] // 2, axis=0)
        for piece in first
    )
    second = lax.ppermute(halves, ("dp", "fsdp"), ring_pairs)
    swap_pairs = [(d, d ^ 1) for d in range(dp_count)]
    other_first, other_second = lax.ppermute((first, second), "dp", swap_pairs)
    is_even = core == 0
    gathered = []
    for own, got, got_other, half, half_other in zip(shards, first, other_first, second, other_second):
        rows = own.shape[0]
        far = jnp.where(
            is_even, jnp.concatenate([half, half_other]), jnp.concatenate([half_other, half])
        )
        relative = jnp.concatenate(
            [own, jnp.where(is_even, got, got_other), far, jnp.where(is_even, got_other, got)]
        )
        doubled = jnp.concatenate([relative, relative])
        gathered.append(
            lax.dynamic_slice_in_dim(doubled, (fsdp_count - fsdp_at) * rows, fsdp_count * rows, axis=0)
        )
    return tuple(gathered)


def gather_pair(down_rows, up_rows, dp_count, fsdp_count):
    if fsdp_count != 4 or dp_count % 2 or down_rows.shape[0] % 2 or up_rows.shape[0] % 2:
        return (
            lax.all_gather(down_rows, "fsdp", axis=0, tiled=True),
            lax.all_gather(up_rows, "fsdp", axis=0, tiled=True),
        )
    return ring_gather((down_rows, up_rows), dp_count, fsdp_count)


def coordinate_pairs(dp_count, fsdp_count, moved, shift):
    sizes = {"x": dp_count // 8, "z": 4, "core": 2, "y": fsdp_count}
    pairs = []
    for d in range(dp_count):
        for f in range(fsdp_count):
            place = {"x": d // 8, "z": (d // 2) % 4, "core": d % 2, "y": f}
            place[moved] = (place[moved] + shift) % sizes[moved]
            target = (place["x"] * 8 + place["z"] * 2 + place["core"]) * fsdp_count + place["y"]
            pairs.append((d * fsdp_count + f, target))
    return pairs


def scatter_sum(parts, at, count, pairs_of, axis=0):
    total = lax.dynamic_index_in_dim(parts, at, axis=axis, keepdims=False)
    for k in range(1, count):
        sent = lax.dynamic_index_in_dim(parts, (at + k) % count, axis=axis, keepdims=False)
        got = lax.ppermute(sent.astype(jnp.bfloat16), ("dp", "fsdp"), pairs_of(k))
        total = total + got.astype(jnp.float32)
    return total


def gather_blocks(block, at, count, pairs_of):
    full = jnp.zeros((count,) + block.shape, block.dtype)
    full = lax.dynamic_update_index_in_dim(full, block, at, axis=0)
    for k in range(1, count):
        got = lax.ppermute(block, ("dp", "fsdp"), pairs_of(k))
        full = lax.dynamic_update_index_in_dim(full, got, (at - k + count) % count, axis=0)
    return full


def reduce_gradients(local_down, local_up, dp_count, fsdp_count):
    d = lax.axis_index("dp")
    at = {"x": d // 8, "z": (d // 2) % 4, "core": d % 2, "y": lax.axis_index("fsdp")}
    sizes = {"x": dp_count // 8, "z": 4, "core": 2, "y": fsdp_count}
    down_size = local_down.size // fsdp_count
    chunk = 2 * down_size // (2 * sizes["x"] * sizes["z"])
    if dp_count != 32 or fsdp_count != 4 or chunk % 2:
        shard_down = lax.psum_scatter(local_down.astype(jnp.bfloat16), "fsdp", scatter_dimension=0, tiled=True)
        shard_up = lax.psum_scatter(local_up.astype(jnp.bfloat16), "fsdp", scatter_dimension=0, tiled=True)
        return (
            lax.psum(shard_down, "dp").astype(jnp.float32),
            lax.psum(shard_up, "dp").astype(jnp.float32),
        )
    table = jnp.concatenate(
        [local_down.reshape(fsdp_count, down_size), local_up.reshape(fsdp_count, down_size)], axis=1
    ).reshape(fsdp_count, 2, sizes["x"], sizes["z"], chunk)

    def pairs(moved):
        return lambda k: coordinate_pairs(dp_count, fsdp_count, moved, k)

    halves = jnp.moveaxis(table, 1, 0)
    part = scatter_sum(halves, at["core"], 2, pairs("core"))
    colour = chunk // 2
    done = []
    for c, order in enumerate((("y", "x"), ("x", "y"))):
        piece = part[..., c * colour:(c + 1) * colour]
        left = ["y", "x", "z"]
        for name in order:
            piece = scatter_sum(piece, at[name], sizes[name], pairs(name), axis=left.index(name))
            left.remove(name)
        done.append(piece)
    part = jnp.concatenate(done, axis=-1)
    part = scatter_sum(part, at["z"], sizes["z"], pairs("z"))
    part = gather_blocks(part.astype(jnp.bfloat16), at["z"], sizes["z"], pairs("z"))
    part = gather_blocks(part, at["x"], sizes["x"], pairs("x"))
    part = gather_blocks(part, at["core"], 2, pairs("core"))
    flat = part.reshape(-1).astype(jnp.float32)
    return (
        flat[:down_size].reshape(local_down.shape[0] // fsdp_count, local_down.shape[1]),
        flat[down_size:].reshape(local_up.shape[0] // fsdp_count, local_up.shape[1]),
    )


def on_device(
    latents, noise_draw, timesteps, buckets, owners, adv_grad, w_down, w_up, t_down, t_up
):
    tile_count, tile_side = (latents.shape[0], latents.shape[1])
    dp_count = lax.axis_size("dp")
    fsdp_count = lax.axis_size("fsdp")
    full_mask, half_mask = width_masks(buckets, tile_side)
    alpha_bar = jnp.square(jnp.cos(0.5 * jnp.pi * (timesteps.astype(jnp.float32) + 0.5) / TSTEPS))
    noisy = (
        full_mask
        * (
            jnp.sqrt(alpha_bar)[:, None, None, None] * latents.astype(jnp.float32)
            + jnp.sqrt(1.0 - alpha_bar)[:, None, None, None] * noise_draw.astype(jnp.float32)
        )
    ).astype(jnp.bfloat16)
    peer_cap = max(2, (tile_count + dp_count - 1) // dp_count)
    slot_count = dp_count * peer_cap
    hit_table = (owners[:, None] == jnp.arange(dp_count, dtype=jnp.int32)[None, :]).astype(
        jnp.int32
    )
    before = jnp.cumsum(hit_table, axis=0) - hit_table
    slot_of = owners * peer_cap + jnp.sum(before * hit_table, axis=1)
    slot_hits = slot_of[None, :] == jnp.arange(slot_count, dtype=jnp.int32)[:, None]
    spread_matrix = slot_hits.astype(jnp.bfloat16)
    send_noisy = (
        jnp.dot(spread_matrix, noisy.reshape(tile_count, -1), preferred_element_type=jnp.float32)
        .astype(jnp.bfloat16)
        .reshape(dp_count, peer_cap, -1)
    )
    send_code = jnp.sum(jnp.where(slot_hits, buckets[None, :] + 1, 0), axis=1).reshape(
        dp_count, peer_cap
    )
    teacher_down, teacher_up = gather_pair(t_down, t_up, dp_count, fsdp_count)
    recv_noisy, recv_code = (
        lax.all_to_all(send_noisy, "dp", split_axis=0, concat_axis=0, tiled=True),
        lax.all_to_all(send_code, "dp", split_axis=0, concat_axis=0, tiled=True),
    )
    flat_code = recv_code.reshape(slot_count)
    live_slot = (flat_code > 0).astype(jnp.int32)
    position = jnp.cumsum(live_slot) - live_slot
    pick_hits = (live_slot[None, :] == 1) & (
        position[None, :] == jnp.arange(tile_count, dtype=jnp.int32)[:, None]
    )
    pick_matrix = pick_hits.astype(jnp.bfloat16)
    own_noisy = (
        jnp.dot(pick_matrix, recv_noisy.reshape(slot_count, -1), preferred_element_type=jnp.float32)
        .astype(jnp.bfloat16)
        .reshape(latents.shape)
    )
    own_buckets = jnp.sum(jnp.where(pick_hits, flat_code[None, :] - 1, 0), axis=1).astype(jnp.int32)
    own_full, own_half = width_masks(own_buckets, tile_side)
    student_down, student_up = gather_pair(w_down, w_up, dp_count, fsdp_count)
    student, cached = network(own_noisy, own_full, own_half, student_down, student_up)
    target, _ = network(own_noisy, own_full, own_half, teacher_down, teacher_up)
    loss_scale = jnp.float32(1.0 / (tile_count * dp_count * fsdp_count))
    flipped = flip_kernel(student_up)
    d_out, d_hidden = cotangents(
        student, target, adv_grad, own_full, own_half, flipped, cached, loss_scale
    )
    local_down = kernel_grad(cached[0], d_hidden, 2)
    local_up = kernel_grad(cached[5], d_out, 1)
    grad_down, grad_up = reduce_gradients(local_down, local_up, dp_count, fsdp_count)
    return (student, grad_down, grad_up)


def solution(mesh):
    return jax.shard_map(
        on_device,
        mesh=mesh,
        in_specs=(
            P(("dp", "fsdp"), None, None, None),
            P(("dp", "fsdp"), None, None, None),
            P(("dp", "fsdp")),
            P(("dp", "fsdp")),
            P(("dp", "fsdp")),
            P(("dp", "fsdp"), None, None, None),
            P("fsdp", None),
            P("fsdp", None),
            P("fsdp", None),
            P("fsdp", None),
        ),
        out_specs=(P(("dp", "fsdp"), None, None, None), P("fsdp", None), P("fsdp", None)),
        check_vma=False,
    )
```

```python
import functools

import jax
import jax.numpy as jnp
from jax import lax
from jax.sharding import PartitionSpec as P

GROUPS = 32
TSTEPS = 1000


distill_weight = 2.5
norm_epsilon = 1e-05


def conv_forward(volume, kernel_rows, stride):
    in_chan = volume.shape[3]
    kernel = kernel_rows.reshape(3, 3, in_chan, kernel_rows.shape[1])
    return lax.conv_general_dilated(
        volume,
        kernel,
        (stride, stride),
        ((1, 1), (1, 1)),
        dimension_numbers=("NHWC", "HWIO", "NHWC"),
        preferred_element_type=jnp.float32,
    )


def kernel_grad(volume, cotangent, stride):
    pad_upper = 1 if stride == 1 else 0
    result_grad = lax.conv_general_dilated(
        volume,
        cotangent,
        (1, 1),
        ((1, pad_upper), (1, pad_upper)),
        rhs_dilation=(stride, stride),
        dimension_numbers=("CHWN", "IHWO", "HWNC"),
        preferred_element_type=jnp.float32,
    )
    return result_grad.reshape(9 * volume.shape[3], cotangent.shape[3])


def width_masks(buckets, tile_side):
    half_side = tile_side // 2
    tile_count = buckets.shape[0]
    columns = jnp.arange(tile_side, dtype=jnp.int32)
    full_mask = (
        columns[None, None, :, None] < (tile_side - 2 * buckets)[:, None, None, None]
    ).astype(jnp.float32)
    full_mask = jnp.broadcast_to(full_mask, (tile_count, tile_side, tile_side, 1))
    half_cols = jnp.arange(half_side, dtype=jnp.int32)
    half_mask = (
        half_cols[None, None, :, None] < (half_side - buckets)[:, None, None, None]
    ).astype(jnp.float32)
    half_mask = jnp.broadcast_to(half_mask, (tile_count, half_side, half_side, 1))
    return (full_mask, half_mask)


def group_stats(hidden, half_mask):
    tile_count, height, breadth, channels = hidden.shape
    grouped = hidden.reshape(tile_count, height * breadth, GROUPS, channels // GROUPS)
    live_weight = half_mask.reshape(tile_count, height * breadth, 1, 1)
    population = jnp.sum(live_weight, axis=(1, 3), keepdims=True) * (channels // GROUPS)
    center = jnp.sum(grouped * live_weight, axis=(1, 3), keepdims=True) / population
    spread = (
        jnp.sum(jnp.square(grouped - center) * live_weight, axis=(1, 3), keepdims=True) / population
    )
    inverse = lax.rsqrt(spread + norm_epsilon)
    normed = ((grouped - center) * inverse).reshape(hidden.shape)
    return (normed, inverse, population)


def group_back(d_norm, normed, inverse, population, half_mask):
    tile_count, height, breadth, channels = d_norm.shape
    grouped_d = d_norm.reshape(tile_count, height * breadth, GROUPS, channels // GROUPS)
    grouped_n = normed.reshape(tile_count, height * breadth, GROUPS, channels // GROUPS)
    live_weight = half_mask.reshape(tile_count, height * breadth, 1, 1)
    mean_first = jnp.sum(grouped_d, axis=(1, 3), keepdims=True) / population
    mean_second = jnp.sum(grouped_d * grouped_n, axis=(1, 3), keepdims=True) / population
    result = live_weight * inverse * (grouped_d - mean_first - grouped_n * mean_second)
    return result.reshape(d_norm.shape)


def upsample(activated):
    return jnp.repeat(jnp.repeat(activated, 2, axis=1), 2, axis=2)


def network(noisy, full_mask, half_mask, down_weight, up_weight):
    hidden = conv_forward(noisy, down_weight, 2)
    normed, inverse, population = group_stats(hidden, half_mask)
    activated = (half_mask * jax.nn.silu(normed)).astype(jnp.bfloat16)
    enlarged = upsample(activated)
    output = conv_forward(enlarged, up_weight, 1)
    student = (full_mask * (noisy.astype(jnp.float32) + output)).astype(jnp.bfloat16)
    return (student, (noisy, normed, inverse, population, activated, enlarged))


def flip_kernel(up_weight):
    up_chan = up_weight.shape[0] // 9
    out_chan = up_weight.shape[1]
    return (
        up_weight.reshape(3, 3, up_chan, out_chan)[::-1, ::-1]
        .transpose(0, 1, 3, 2)
        .reshape(9 * out_chan, up_chan)
    )


def cotangents(student, target, adversarial, full_mask, half_mask, flipped, cached, loss_scale):
    source_in, normed, inverse, population, activated, enlarged = cached
    tile_count, tile_side = (student.shape[0], student.shape[1])
    half_side = tile_side // 2
    d_out = (
        full_mask
        * (
            distill_weight * (student.astype(jnp.float32) - target.astype(jnp.float32))
            + adversarial.astype(jnp.float32)
        )
        * loss_scale
    ).astype(jnp.bfloat16)
    d_up = conv_forward(d_out, flipped, 1)
    d_up = d_up.reshape(tile_count, half_side, 2, half_side, 2, flipped.shape[1])
    d_act = jnp.sum(d_up, axis=(2, 4))
    sigmoid_n = jax.nn.sigmoid(normed)
    d_norm = half_mask * d_act * sigmoid_n * (1.0 + normed * (1.0 - sigmoid_n))
    d_hidden = group_back(d_norm, normed, inverse, population, half_mask).astype(jnp.bfloat16)
    return (d_out, d_hidden)


def ring_gather(shards, dp_count, fsdp_count):
    fsdp_at = lax.axis_index("fsdp")
    core = lax.axis_index("dp") % 2
    step = 1 - 2 * core

    def lin(d, f):
        return d * fsdp_count + f

    ring_pairs = []
    for d in range(dp_count):
        toward = -1 if d % 2 == 0 else 1
        for f in range(fsdp_count):
            ring_pairs.append((lin(d, f), lin(d, (f + toward) % fsdp_count)))
    first = lax.ppermute(shards, ("dp", "fsdp"), ring_pairs)
    halves = tuple(
        lax.dynamic_slice_in_dim(piece, core * (piece.shape[0] // 2), piece.shape[0] // 2, axis=0)
        for piece in first
    )
    second = lax.ppermute(halves, ("dp", "fsdp"), ring_pairs)
    swap_pairs = [(d, d ^ 1) for d in range(dp_count)]
    other_first, other_second = lax.ppermute((first, second), "dp", swap_pairs)

    def place(at_y, at_core, pieces):
        toward = 1 - 2 * at_core
        gathered = []
        for own, got, got_other, half, half_other in pieces:
            far = jnp.concatenate([half, half_other] if at_core == 0 else [half_other, half])
            blocks = {
                at_y: own,
                (at_y + toward) % fsdp_count: got,
                (at_y - toward) % fsdp_count: got_other,
                (at_y + 2) % fsdp_count: far,
            }
            gathered.append(jnp.concatenate([blocks[f] for f in range(fsdp_count)]))
        return tuple(gathered)

    pieces = tuple(zip(shards, first, other_first, second, other_second))
    branches = [
        functools.partial(place, at_y, at_core) for at_y in range(fsdp_count) for at_core in range(2)
    ]
    gathered = lax.switch(fsdp_at * 2 + core, branches, pieces)
    return tuple(gathered)


def gather_pair(down_rows, up_rows, dp_count, fsdp_count):
    if fsdp_count != 4 or dp_count % 2 or down_rows.shape[0] % 2 or up_rows.shape[0] % 2:
        return (
            lax.all_gather(down_rows, "fsdp", axis=0, tiled=True),
            lax.all_gather(up_rows, "fsdp", axis=0, tiled=True),
        )
    return ring_gather((down_rows, up_rows), dp_count, fsdp_count)


def coordinate_pairs(dp_count, fsdp_count, moved, shift):
    sizes = {"x": dp_count // 8, "z": 4, "core": 2, "y": fsdp_count}
    pairs = []
    for d in range(dp_count):
        for f in range(fsdp_count):
            place = {"x": d // 8, "z": (d // 2) % 4, "core": d % 2, "y": f}
            place[moved] = (place[moved] + shift) % sizes[moved]
            target = (place["x"] * 8 + place["z"] * 2 + place["core"]) * fsdp_count + place["y"]
            pairs.append((d * fsdp_count + f, target))
    return pairs


def scatter_sum(parts, at, count, pairs_of, axis=0):
    total = lax.dynamic_index_in_dim(parts, at, axis=axis, keepdims=False)
    for k in range(1, count):
        sent = lax.dynamic_index_in_dim(parts, (at + k) % count, axis=axis, keepdims=False)
        got = lax.ppermute(sent.astype(jnp.bfloat16), ("dp", "fsdp"), pairs_of(k))
        total = total + got.astype(jnp.float32)
    return total


def gather_blocks(block, at, count, pairs_of):
    full = jnp.zeros((count,) + block.shape, block.dtype)
    full = lax.dynamic_update_index_in_dim(full, block, at, axis=0)
    for k in range(1, count):
        got = lax.ppermute(block, ("dp", "fsdp"), pairs_of(k))
        full = lax.dynamic_update_index_in_dim(full, got, (at - k + count) % count, axis=0)
    return full


def reduce_gradients(local_down, local_up, dp_count, fsdp_count):
    d = lax.axis_index("dp")
    at = {"x": d // 8, "z": (d // 2) % 4, "core": d % 2, "y": lax.axis_index("fsdp")}
    sizes = {"x": dp_count // 8, "z": 4, "core": 2, "y": fsdp_count}
    down_size = local_down.size // fsdp_count
    chunk = 2 * down_size // (2 * sizes["x"] * sizes["z"])
    if dp_count != 32 or fsdp_count != 4 or chunk % 2:
        shard_down = lax.psum_scatter(local_down.astype(jnp.bfloat16), "fsdp", scatter_dimension=0, tiled=True)
        shard_up = lax.psum_scatter(local_up.astype(jnp.bfloat16), "fsdp", scatter_dimension=0, tiled=True)
        return (
            lax.psum(shard_down, "dp").astype(jnp.float32),
            lax.psum(shard_up, "dp").astype(jnp.float32),
        )
    table = jnp.concatenate(
        [local_down.reshape(fsdp_count, down_size), local_up.reshape(fsdp_count, down_size)], axis=1
    ).reshape(fsdp_count, 2, sizes["x"], sizes["z"], chunk)

    def pairs(moved):
        return lambda k: coordinate_pairs(dp_count, fsdp_count, moved, k)

    halves = jnp.moveaxis(table, 1, 0)
    part = scatter_sum(halves, at["core"], 2, pairs("core"))
    colour = chunk // 2
    done = []
    for c, order in enumerate((("y", "x"), ("x", "y"))):
        piece = part[..., c * colour:(c + 1) * colour]
        left = ["y", "x", "z"]
        for name in order:
            piece = scatter_sum(piece, at[name], sizes[name], pairs(name), axis=left.index(name))
            left.remove(name)
        done.append(piece)
    part = jnp.concatenate(done, axis=-1)
    part = scatter_sum(part, at["z"], sizes["z"], pairs("z"))
    part = gather_blocks(part.astype(jnp.bfloat16), at["z"], sizes["z"], pairs("z"))
    part = gather_blocks(part, at["x"], sizes["x"], pairs("x"))
    part = gather_blocks(part, at["core"], 2, pairs("core"))
    flat = part.reshape(-1).astype(jnp.float32)
    return (
        flat[:down_size].reshape(local_down.shape[0] // fsdp_count, local_down.shape[1]),
        flat[down_size:].reshape(local_up.shape[0] // fsdp_count, local_up.shape[1]),
    )


def on_device(
    latents, noise_draw, timesteps, buckets, owners, adv_grad, w_down, w_up, t_down, t_up
):
    tile_count, tile_side = (latents.shape[0], latents.shape[1])
    dp_count = lax.axis_size("dp")
    fsdp_count = lax.axis_size("fsdp")
    full_mask, half_mask = width_masks(buckets, tile_side)
    alpha_bar = jnp.square(jnp.cos(0.5 * jnp.pi * (timesteps.astype(jnp.float32) + 0.5) / TSTEPS))
    noisy = (
        full_mask
        * (
            jnp.sqrt(alpha_bar)[:, None, None, None] * latents.astype(jnp.float32)
            + jnp.sqrt(1.0 - alpha_bar)[:, None, None, None] * noise_draw.astype(jnp.float32)
        )
    ).astype(jnp.bfloat16)
    peer_cap = max(2, (tile_count + dp_count - 1) // dp_count)
    slot_count = dp_count * peer_cap
    hit_table = (owners[:, None] == jnp.arange(dp_count, dtype=jnp.int32)[None, :]).astype(
        jnp.int32
    )
    before = jnp.cumsum(hit_table, axis=0) - hit_table
    slot_of = owners * peer_cap + jnp.sum(before * hit_table, axis=1)
    slot_hits = slot_of[None, :] == jnp.arange(slot_count, dtype=jnp.int32)[:, None]
    spread_matrix = slot_hits.astype(jnp.bfloat16)
    send_noisy = (
        jnp.dot(spread_matrix, noisy.reshape(tile_count, -1), preferred_element_type=jnp.float32)
        .astype(jnp.bfloat16)
        .reshape(dp_count, peer_cap, -1)
    )
    send_code = jnp.sum(jnp.where(slot_hits, buckets[None, :] + 1, 0), axis=1).reshape(
        dp_count, peer_cap
    )
    teacher_down, teacher_up = gather_pair(t_down, t_up, dp_count, fsdp_count)
    recv_noisy, recv_code = (
        lax.all_to_all(send_noisy, "dp", split_axis=0, concat_axis=0, tiled=True),
        lax.all_to_all(send_code, "dp", split_axis=0, concat_axis=0, tiled=True),
    )
    flat_code = recv_code.reshape(slot_count)
    live_slot = (flat_code > 0).astype(jnp.int32)
    position = jnp.cumsum(live_slot) - live_slot
    pick_hits = (live_slot[None, :] == 1) & (
        position[None, :] == jnp.arange(tile_count, dtype=jnp.int32)[:, None]
    )
    pick_matrix = pick_hits.astype(jnp.bfloat16)
    own_noisy = (
        jnp.dot(pick_matrix, recv_noisy.reshape(slot_count, -1), preferred_element_type=jnp.float32)
        .astype(jnp.bfloat16)
        .reshape(latents.shape)
    )
    own_buckets = jnp.sum(jnp.where(pick_hits, flat_code[None, :] - 1, 0), axis=1).astype(jnp.int32)
    own_full, own_half = width_masks(own_buckets, tile_side)
    student_down, student_up = gather_pair(w_down, w_up, dp_count, fsdp_count)
    student, cached = network(own_noisy, own_full, own_half, student_down, student_up)
    target, _ = network(own_noisy, own_full, own_half, teacher_down, teacher_up)
    loss_scale = jnp.float32(1.0 / (tile_count * dp_count * fsdp_count))
    flipped = flip_kernel(student_up)
    d_out, d_hidden = cotangents(
        student, target, adv_grad, own_full, own_half, flipped, cached, loss_scale
    )
    local_down = kernel_grad(cached[0], d_hidden, 2)
    local_up = kernel_grad(cached[5], d_out, 1)
    grad_down, grad_up = reduce_gradients(local_down, local_up, dp_count, fsdp_count)
    return (student, grad_down, grad_up)


def solution(mesh):
    return jax.shard_map(
        on_device,
        mesh=mesh,
        in_specs=(
            P(("dp", "fsdp"), None, None, None),
            P(("dp", "fsdp"), None, None, None),
            P(("dp", "fsdp")),
            P(("dp", "fsdp")),
            P(("dp", "fsdp")),
            P(("dp", "fsdp"), None, None, None),
            P("fsdp", None),
            P("fsdp", None),
            P("fsdp", None),
            P("fsdp", None),
        ),
        out_specs=(P(("dp", "fsdp"), None, None, None), P("fsdp", None), P("fsdp", None)),
        check_vma=False,
    )
```

```python
import jax
import jax.numpy as jnp
from jax import lax
from jax.sharding import PartitionSpec as P

GROUPS = 32
TSTEPS = 1000


distill_weight = 2.5
norm_epsilon = 1e-05


def conv_forward(volume, kernel_rows, stride):
    in_chan = volume.shape[3]
    kernel = kernel_rows.reshape(3, 3, in_chan, kernel_rows.shape[1])
    return lax.conv_general_dilated(
        volume,
        kernel,
        (stride, stride),
        ((1, 1), (1, 1)),
        dimension_numbers=("NHWC", "HWIO", "NHWC"),
        preferred_element_type=jnp.float32,
    )


def kernel_grad(volume, cotangent, stride):
    pad_upper = 1 if stride == 1 else 0
    result_grad = lax.conv_general_dilated(
        volume,
        cotangent,
        (1, 1),
        ((1, pad_upper), (1, pad_upper)),
        rhs_dilation=(stride, stride),
        dimension_numbers=("CHWN", "IHWO", "HWNC"),
        preferred_element_type=jnp.float32,
    )
    return result_grad.reshape(9 * volume.shape[3], cotangent.shape[3])


def width_masks(buckets, tile_side):
    half_side = tile_side // 2
    tile_count = buckets.shape[0]
    columns = jnp.arange(tile_side, dtype=jnp.int32)
    full_mask = (
        columns[None, None, :, None] < (tile_side - 2 * buckets)[:, None, None, None]
    ).astype(jnp.float32)
    full_mask = jnp.broadcast_to(full_mask, (tile_count, tile_side, tile_side, 1))
    half_cols = jnp.arange(half_side, dtype=jnp.int32)
    half_mask = (
        half_cols[None, None, :, None] < (half_side - buckets)[:, None, None, None]
    ).astype(jnp.float32)
    half_mask = jnp.broadcast_to(half_mask, (tile_count, half_side, half_side, 1))
    return (full_mask, half_mask)


def group_stats(hidden, half_mask):
    tile_count, height, breadth, channels = hidden.shape
    grouped = hidden.reshape(tile_count, height * breadth, GROUPS, channels // GROUPS)
    live_weight = half_mask.reshape(tile_count, height * breadth, 1, 1)
    population = jnp.sum(live_weight, axis=(1, 3), keepdims=True) * (channels // GROUPS)
    center = jnp.sum(grouped * live_weight, axis=(1, 3), keepdims=True) / population
    spread = (
        jnp.sum(jnp.square(grouped - center) * live_weight, axis=(1, 3), keepdims=True) / population
    )
    inverse = lax.rsqrt(spread + norm_epsilon)
    normed = ((grouped - center) * inverse).reshape(hidden.shape)
    return (normed, inverse, population)


def group_back(d_norm, normed, inverse, population, half_mask):
    tile_count, height, breadth, channels = d_norm.shape
    grouped_d = d_norm.reshape(tile_count, height * breadth, GROUPS, channels // GROUPS)
    grouped_n = normed.reshape(tile_count, height * breadth, GROUPS, channels // GROUPS)
    live_weight = half_mask.reshape(tile_count, height * breadth, 1, 1)
    mean_first = jnp.sum(grouped_d, axis=(1, 3), keepdims=True) / population
    mean_second = jnp.sum(grouped_d * grouped_n, axis=(1, 3), keepdims=True) / population
    result = live_weight * inverse * (grouped_d - mean_first - grouped_n * mean_second)
    return result.reshape(d_norm.shape)


def upsample(activated):
    return jnp.repeat(jnp.repeat(activated, 2, axis=1), 2, axis=2)


def network(noisy, full_mask, half_mask, down_weight, up_weight):
    hidden = conv_forward(noisy, down_weight, 2)
    normed, inverse, population = group_stats(hidden, half_mask)
    activated = (half_mask * jax.nn.silu(normed)).astype(jnp.bfloat16)
    enlarged = upsample(activated)
    output = conv_forward(enlarged, up_weight, 1)
    student = (full_mask * (noisy.astype(jnp.float32) + output)).astype(jnp.bfloat16)
    return (student, (noisy, normed, inverse, population, activated, enlarged))


def flip_kernel(up_weight):
    up_chan = up_weight.shape[0] // 9
    out_chan = up_weight.shape[1]
    return (
        up_weight.reshape(3, 3, up_chan, out_chan)[::-1, ::-1]
        .transpose(0, 1, 3, 2)
        .reshape(9 * out_chan, up_chan)
    )


def cotangents(student, target, adversarial, full_mask, half_mask, flipped, cached, loss_scale):
    source_in, normed, inverse, population, activated, enlarged = cached
    tile_count, tile_side = (student.shape[0], student.shape[1])
    half_side = tile_side // 2
    d_out = (
        full_mask
        * (
            distill_weight * (student.astype(jnp.float32) - target.astype(jnp.float32))
            + adversarial.astype(jnp.float32)
        )
        * loss_scale
    ).astype(jnp.bfloat16)
    d_up = conv_forward(d_out, flipped, 1)
    d_up = d_up.reshape(tile_count, half_side, 2, half_side, 2, flipped.shape[1])
    d_act = jnp.sum(d_up, axis=(2, 4))
    sigmoid_n = jax.nn.sigmoid(normed)
    d_norm = half_mask * d_act * sigmoid_n * (1.0 + normed * (1.0 - sigmoid_n))
    d_hidden = group_back(d_norm, normed, inverse, population, half_mask).astype(jnp.bfloat16)
    return (d_out, d_hidden)


def ring_gather(shards, dp_count, fsdp_count):
    fsdp_at = lax.axis_index("fsdp")
    core = lax.axis_index("dp") % 2
    step = 1 - 2 * core

    def lin(d, f):
        return d * fsdp_count + f

    ring_pairs = []
    for d in range(dp_count):
        toward = -1 if d % 2 == 0 else 1
        for f in range(fsdp_count):
            ring_pairs.append((lin(d, f), lin(d, (f + toward) % fsdp_count)))
    first = lax.ppermute(shards, ("dp", "fsdp"), ring_pairs)
    halves = tuple(
        lax.dynamic_slice_in_dim(piece, core * (piece.shape[0] // 2), piece.shape[0] // 2, axis=0)
        for piece in first
    )
    second = lax.ppermute(halves, ("dp", "fsdp"), ring_pairs)
    swap_pairs = [(d, d ^ 1) for d in range(dp_count)]
    other_first, other_second = lax.ppermute((first, second), "dp", swap_pairs)
    near = (fsdp_at + step + fsdp_count) % fsdp_count
    behind = (fsdp_at - step + fsdp_count) % fsdp_count
    far = (fsdp_at + 2) % fsdp_count
    gathered = []
    for own, got, got_other, half, half_other in zip(shards, first, other_first, second, other_second):
        rows = own.shape[0]
        full = jnp.zeros((fsdp_count * rows,) + own.shape[1:], own.dtype)
        full = lax.dynamic_update_slice_in_dim(full, own, fsdp_at * rows, axis=0)
        full = lax.dynamic_update_slice_in_dim(full, got, near * rows, axis=0)
        full = lax.dynamic_update_slice_in_dim(full, got_other, behind * rows, axis=0)
        full = lax.dynamic_update_slice_in_dim(full, half, far * rows + core * (rows // 2), axis=0)
        full = lax.dynamic_update_slice_in_dim(
            full, half_other, far * rows + (1 - core) * (rows // 2), axis=0
        )
        gathered.append(full)
    return tuple(gathered)


def gather_pair(down_rows, up_rows, dp_count, fsdp_count):
    if fsdp_count != 4 or dp_count % 2 or down_rows.shape[0] % 2 or up_rows.shape[0] % 2:
        return (
            lax.all_gather(down_rows, "fsdp", axis=0, tiled=True),
            lax.all_gather(up_rows, "fsdp", axis=0, tiled=True),
        )
    return ring_gather((down_rows, up_rows), dp_count, fsdp_count)


def coordinate_pairs(dp_count, fsdp_count, moved, shift):
    sizes = {"x": dp_count // 8, "z": 4, "core": 2, "y": fsdp_count}
    pairs = []
    for d in range(dp_count):
        for f in range(fsdp_count):
            place = {"x": d // 8, "z": (d // 2) % 4, "core": d % 2, "y": f}
            place[moved] = (place[moved] + shift) % sizes[moved]
            target = (place["x"] * 8 + place["z"] * 2 + place["core"]) * fsdp_count + place["y"]
            pairs.append((d * fsdp_count + f, target))
    return pairs


def scatter_sum(parts, at, count, pairs_of, axis=0):
    total = lax.dynamic_index_in_dim(parts, at, axis=axis, keepdims=False)
    for k in range(1, count):
        sent = lax.dynamic_index_in_dim(parts, (at + k) % count, axis=axis, keepdims=False)
        got = lax.ppermute(sent.astype(jnp.bfloat16), ("dp", "fsdp"), pairs_of(k))
        total = total + got.astype(jnp.float32)
    return total


def gather_blocks(block, at, count, pairs_of):
    full = jnp.zeros((count,) + block.shape, block.dtype)
    full = lax.dynamic_update_index_in_dim(full, block, at, axis=0)
    for k in range(1, count):
        got = lax.ppermute(block, ("dp", "fsdp"), pairs_of(k))
        full = lax.dynamic_update_index_in_dim(full, got, (at - k + count) % count, axis=0)
    return full


def reduce_gradients(local_down, local_up, dp_count, fsdp_count):
    d = lax.axis_index("dp")
    at = {"x": d // 8, "z": (d // 2) % 4, "core": d % 2, "y": lax.axis_index("fsdp")}
    sizes = {"x": dp_count // 8, "z": 4, "core": 2, "y": fsdp_count}
    down_size = local_down.size // fsdp_count
    chunk = 2 * down_size // (2 * sizes["x"] * sizes["z"])
    if dp_count != 32 or fsdp_count != 4 or chunk % 2:
        shard_down = lax.psum_scatter(local_down.astype(jnp.bfloat16), "fsdp", scatter_dimension=0, tiled=True)
        shard_up = lax.psum_scatter(local_up.astype(jnp.bfloat16), "fsdp", scatter_dimension=0, tiled=True)
        return (
            lax.psum(shard_down, "dp").astype(jnp.float32),
            lax.psum(shard_up, "dp").astype(jnp.float32),
        )
    table = jnp.concatenate(
        [local_down.reshape(fsdp_count, down_size), local_up.reshape(fsdp_count, down_size)], axis=1
    ).reshape(fsdp_count, 2, sizes["x"], sizes["z"], chunk)

    def pairs(moved):
        return lambda k: coordinate_pairs(dp_count, fsdp_count, moved, k)

    halves = jnp.moveaxis(table, 1, 0)
    part = scatter_sum(halves, at["core"], 2, pairs("core"))
    colour = chunk // 2
    done = []
    for c, order in enumerate((("y", "x"), ("x", "y"))):
        piece = part[..., c * colour:(c + 1) * colour]
        left = ["y", "x", "z"]
        for name in order:
            piece = scatter_sum(piece, at[name], sizes[name], pairs(name), axis=left.index(name))
            left.remove(name)
        done.append(piece)
    part = jnp.concatenate(done, axis=-1)
    part = scatter_sum(part, at["z"], sizes["z"], pairs("z"))
    part = gather_blocks(part.astype(jnp.bfloat16), at["z"], sizes["z"], pairs("z"))
    part = gather_blocks(part, at["x"], sizes["x"], pairs("x"))
    part = gather_blocks(part, at["core"], 2, pairs("core"))
    flat = part.reshape(-1).astype(jnp.float32)
    return (
        flat[:down_size].reshape(local_down.shape[0] // fsdp_count, local_down.shape[1]),
        flat[down_size:].reshape(local_up.shape[0] // fsdp_count, local_up.shape[1]),
    )


def on_device(
    latents, noise_draw, timesteps, buckets, owners, adv_grad, w_down, w_up, t_down, t_up
):
    tile_count, tile_side = (latents.shape[0], latents.shape[1])
    dp_count = lax.axis_size("dp")
    fsdp_count = lax.axis_size("fsdp")
    full_mask, half_mask = width_masks(buckets, tile_side)
    alpha_bar = jnp.square(jnp.cos(0.5 * jnp.pi * (timesteps.astype(jnp.float32) + 0.5) / TSTEPS))
    noisy = (
        full_mask
        * (
            jnp.sqrt(alpha_bar)[:, None, None, None] * latents.astype(jnp.float32)
            + jnp.sqrt(1.0 - alpha_bar)[:, None, None, None] * noise_draw.astype(jnp.float32)
        )
    ).astype(jnp.bfloat16)
    peer_cap = max(2, (tile_count + dp_count - 1) // dp_count)
    slot_count = dp_count * peer_cap
    hit_table = (owners[:, None] == jnp.arange(dp_count, dtype=jnp.int32)[None, :]).astype(
        jnp.int32
    )
    before = jnp.cumsum(hit_table, axis=0) - hit_table
    slot_of = owners * peer_cap + jnp.sum(before * hit_table, axis=1)
    slot_hits = slot_of[None, :] == jnp.arange(slot_count, dtype=jnp.int32)[:, None]
    spread_matrix = slot_hits.astype(jnp.bfloat16)
    send_noisy = (
        jnp.dot(spread_matrix, noisy.reshape(tile_count, -1), preferred_element_type=jnp.float32)
        .astype(jnp.bfloat16)
        .reshape(dp_count, peer_cap, -1)
    )
    send_code = jnp.sum(jnp.where(slot_hits, buckets[None, :] + 1, 0), axis=1).reshape(
        dp_count, peer_cap
    )
    recv_noisy, recv_code = (
        lax.all_to_all(send_noisy, "dp", split_axis=0, concat_axis=0, tiled=True),
        lax.all_to_all(send_code, "dp", split_axis=0, concat_axis=0, tiled=True),
    )
    flat_code = recv_code.reshape(slot_count)
    live_slot = (flat_code > 0).astype(jnp.int32)
    position = jnp.cumsum(live_slot) - live_slot
    pick_hits = (live_slot[None, :] == 1) & (
        position[None, :] == jnp.arange(tile_count, dtype=jnp.int32)[:, None]
    )
    pick_matrix = pick_hits.astype(jnp.bfloat16)
    own_noisy = (
        jnp.dot(pick_matrix, recv_noisy.reshape(slot_count, -1), preferred_element_type=jnp.float32)
        .astype(jnp.bfloat16)
        .reshape(latents.shape)
    )
    own_buckets = jnp.sum(jnp.where(pick_hits, flat_code[None, :] - 1, 0), axis=1).astype(jnp.int32)
    own_full, own_half = width_masks(own_buckets, tile_side)
    student_down, student_up = gather_pair(w_down, w_up, dp_count, fsdp_count)
    t_down, t_up, _, _ = lax.optimization_barrier((t_down, t_up, student_down, student_up))
    teacher_down, teacher_up = gather_pair(t_down, t_up, dp_count, fsdp_count)
    student, cached = network(own_noisy, own_full, own_half, student_down, student_up)
    target, _ = network(own_noisy, own_full, own_half, teacher_down, teacher_up)
    loss_scale = jnp.float32(1.0 / (tile_count * dp_count * fsdp_count))
    flipped = flip_kernel(student_up)
    d_out, d_hidden = cotangents(
        student, target, adv_grad, own_full, own_half, flipped, cached, loss_scale
    )
    local_down = kernel_grad(cached[0], d_hidden, 2)
    local_up = kernel_grad(cached[5], d_out, 1)
    grad_down, grad_up = reduce_gradients(local_down, local_up, dp_count, fsdp_count)
    return (student, grad_down, grad_up)


def solution(mesh):
    return jax.shard_map(
        on_device,
        mesh=mesh,
        in_specs=(
            P(("dp", "fsdp"), None, None, None),
            P(("dp", "fsdp"), None, None, None),
            P(("dp", "fsdp")),
            P(("dp", "fsdp")),
            P(("dp", "fsdp")),
            P(("dp", "fsdp"), None, None, None),
            P("fsdp", None),
            P("fsdp", None),
            P("fsdp", None),
            P("fsdp", None),
        ),
        out_specs=(P(("dp", "fsdp"), None, None, None), P("fsdp", None), P("fsdp", None)),
        check_vma=False,
    )
```

```python
import jax
import jax.numpy as jnp
from jax import lax
from jax.sharding import PartitionSpec as P

GROUPS = 32
TSTEPS = 1000


distill_weight = 2.5
norm_epsilon = 1e-05


def conv_forward(volume, kernel_rows, stride):
    in_chan = volume.shape[3]
    kernel = kernel_rows.reshape(3, 3, in_chan, kernel_rows.shape[1])
    return lax.conv_general_dilated(
        volume,
        kernel,
        (stride, stride),
        ((1, 1), (1, 1)),
        dimension_numbers=("NHWC", "HWIO", "NHWC"),
        preferred_element_type=jnp.float32,
    )


def kernel_grad(volume, cotangent, stride):
    pad_upper = 1 if stride == 1 else 0
    result_grad = lax.conv_general_dilated(
        volume,
        cotangent,
        (1, 1),
        ((1, pad_upper), (1, pad_upper)),
        rhs_dilation=(stride, stride),
        dimension_numbers=("CHWN", "IHWO", "HWNC"),
        preferred_element_type=jnp.float32,
    )
    return result_grad.reshape(9 * volume.shape[3], cotangent.shape[3])


def width_masks(buckets, tile_side):
    half_side = tile_side // 2
    tile_count = buckets.shape[0]
    columns = jnp.arange(tile_side, dtype=jnp.int32)
    full_mask = (
        columns[None, None, :, None] < (tile_side - 2 * buckets)[:, None, None, None]
    ).astype(jnp.float32)
    full_mask = jnp.broadcast_to(full_mask, (tile_count, tile_side, tile_side, 1))
    half_cols = jnp.arange(half_side, dtype=jnp.int32)
    half_mask = (
        half_cols[None, None, :, None] < (half_side - buckets)[:, None, None, None]
    ).astype(jnp.float32)
    half_mask = jnp.broadcast_to(half_mask, (tile_count, half_side, half_side, 1))
    return (full_mask, half_mask)


def group_stats(hidden, half_mask):
    tile_count, height, breadth, channels = hidden.shape
    grouped = hidden.reshape(tile_count, height * breadth, GROUPS, channels // GROUPS)
    live_weight = half_mask.reshape(tile_count, height * breadth, 1, 1)
    population = jnp.sum(live_weight, axis=(1, 3), keepdims=True) * (channels // GROUPS)
    center = jnp.sum(grouped * live_weight, axis=(1, 3), keepdims=True) / population
    spread = (
        jnp.sum(jnp.square(grouped - center) * live_weight, axis=(1, 3), keepdims=True) / population
    )
    inverse = lax.rsqrt(spread + norm_epsilon)
    normed = ((grouped - center) * inverse).reshape(hidden.shape)
    return (normed, inverse, population)


def group_back(d_norm, normed, inverse, population, half_mask):
    tile_count, height, breadth, channels = d_norm.shape
    grouped_d = d_norm.reshape(tile_count, height * breadth, GROUPS, channels // GROUPS)
    grouped_n = normed.reshape(tile_count, height * breadth, GROUPS, channels // GROUPS)
    live_weight = half_mask.reshape(tile_count, height * breadth, 1, 1)
    mean_first = jnp.sum(grouped_d, axis=(1, 3), keepdims=True) / population
    mean_second = jnp.sum(grouped_d * grouped_n, axis=(1, 3), keepdims=True) / population
    result = live_weight * inverse * (grouped_d - mean_first - grouped_n * mean_second)
    return result.reshape(d_norm.shape)


def upsample(activated):
    return jnp.repeat(jnp.repeat(activated, 2, axis=1), 2, axis=2)


def network(noisy, full_mask, half_mask, down_weight, up_weight):
    hidden = conv_forward(noisy, down_weight, 2)
    normed, inverse, population = group_stats(hidden, half_mask)
    activated = (half_mask * jax.nn.silu(normed)).astype(jnp.bfloat16)
    enlarged = upsample(activated)
    output = conv_forward(enlarged, up_weight, 1)
    student = (full_mask * (noisy.astype(jnp.float32) + output)).astype(jnp.bfloat16)
    return (student, (noisy, normed, inverse, population, activated, enlarged))


def flip_kernel(up_weight):
    up_chan = up_weight.shape[0] // 9
    out_chan = up_weight.shape[1]
    return (
        up_weight.reshape(3, 3, up_chan, out_chan)[::-1, ::-1]
        .transpose(0, 1, 3, 2)
        .reshape(9 * out_chan, up_chan)
    )


def cotangents(student, target, adversarial, full_mask, half_mask, flipped, cached, loss_scale):
    source_in, normed, inverse, population, activated, enlarged = cached
    tile_count, tile_side = (student.shape[0], student.shape[1])
    half_side = tile_side // 2
    d_out = (
        full_mask
        * (
            distill_weight * (student.astype(jnp.float32) - target.astype(jnp.float32))
            + adversarial.astype(jnp.float32)
        )
        * loss_scale
    ).astype(jnp.bfloat16)
    d_up = conv_forward(d_out, flipped, 1)
    d_up = d_up.reshape(tile_count, half_side, 2, half_side, 2, flipped.shape[1])
    d_act = jnp.sum(d_up, axis=(2, 4))
    sigmoid_n = jax.nn.sigmoid(normed)
    d_norm = half_mask * d_act * sigmoid_n * (1.0 + normed * (1.0 - sigmoid_n))
    d_hidden = group_back(d_norm, normed, inverse, population, half_mask).astype(jnp.bfloat16)
    return (d_out, d_hidden)


def ring_gather(shards, dp_count, fsdp_count):
    fsdp_at = lax.axis_index("fsdp")
    core = lax.axis_index("dp") % 2
    step = 1 - 2 * core

    def lin(d, f):
        return d * fsdp_count + f

    ring_pairs = []
    for d in range(dp_count):
        toward = -1 if d % 2 == 0 else 1
        for f in range(fsdp_count):
            ring_pairs.append((lin(d, f), lin(d, (f + toward) % fsdp_count)))
    first = lax.ppermute(shards, ("dp", "fsdp"), ring_pairs)
    halves = tuple(
        lax.dynamic_slice_in_dim(piece, core * (piece.shape[0] // 2), piece.shape[0] // 2, axis=0)
        for piece in first
    )
    second = lax.ppermute(halves, ("dp", "fsdp"), ring_pairs)
    swap_pairs = [(d, d ^ 1) for d in range(dp_count)]
    other_first, other_second = lax.ppermute((first, second), "dp", swap_pairs)
    near = (fsdp_at + step + fsdp_count) % fsdp_count
    behind = (fsdp_at - step + fsdp_count) % fsdp_count
    far = (fsdp_at + 2) % fsdp_count
    gathered = []
    for own, got, got_other, half, half_other in zip(shards, first, other_first, second, other_second):
        rows = own.shape[0]
        full = jnp.zeros((fsdp_count * rows,) + own.shape[1:], own.dtype)
        full = lax.dynamic_update_slice_in_dim(full, own, fsdp_at * rows, axis=0)
        full = lax.dynamic_update_slice_in_dim(full, got, near * rows, axis=0)
        full = lax.dynamic_update_slice_in_dim(full, got_other, behind * rows, axis=0)
        full = lax.dynamic_update_slice_in_dim(full, half, far * rows + core * (rows // 2), axis=0)
        full = lax.dynamic_update_slice_in_dim(
            full, half_other, far * rows + (1 - core) * (rows // 2), axis=0
        )
        gathered.append(full)
    return tuple(gathered)


def gather_pair(down_rows, up_rows, dp_count, fsdp_count):
    if fsdp_count != 4 or dp_count % 2 or down_rows.shape[0] % 2 or up_rows.shape[0] % 2:
        return (
            lax.all_gather(down_rows, "fsdp", axis=0, tiled=True),
            lax.all_gather(up_rows, "fsdp", axis=0, tiled=True),
        )
    return ring_gather((down_rows, up_rows), dp_count, fsdp_count)


def coordinate_pairs(dp_count, fsdp_count, moved, shift):
    sizes = {"x": dp_count // 8, "z": 4, "core": 2, "y": fsdp_count}
    pairs = []
    for d in range(dp_count):
        for f in range(fsdp_count):
            place = {"x": d // 8, "z": (d // 2) % 4, "core": d % 2, "y": f}
            place[moved] = (place[moved] + shift) % sizes[moved]
            target = (place["x"] * 8 + place["z"] * 2 + place["core"]) * fsdp_count + place["y"]
            pairs.append((d * fsdp_count + f, target))
    return pairs


def scatter_sum(parts, at, count, pairs_of, axis=0):
    total = lax.dynamic_index_in_dim(parts, at, axis=axis, keepdims=False)
    for k in range(1, count):
        sent = lax.dynamic_index_in_dim(parts, (at + k) % count, axis=axis, keepdims=False)
        got = lax.ppermute(sent.astype(jnp.bfloat16), ("dp", "fsdp"), pairs_of(k))
        total = total + got.astype(jnp.float32)
    return total


def gather_blocks(block, at, count, pairs_of):
    full = jnp.zeros((count,) + block.shape, block.dtype)
    full = lax.dynamic_update_index_in_dim(full, block, at, axis=0)
    for k in range(1, count):
        got = lax.ppermute(block, ("dp", "fsdp"), pairs_of(k))
        full = lax.dynamic_update_index_in_dim(full, got, (at - k + count) % count, axis=0)
    return full


def reduce_gradients(local_down, local_up, dp_count, fsdp_count):
    d = lax.axis_index("dp")
    at = {"x": d // 8, "z": (d // 2) % 4, "core": d % 2, "y": lax.axis_index("fsdp")}
    sizes = {"x": dp_count // 8, "z": 4, "core": 2, "y": fsdp_count}
    down_size = local_down.size // fsdp_count
    chunk = 2 * down_size // (2 * sizes["x"] * sizes["z"])
    if dp_count != 32 or fsdp_count != 4 or chunk % 2:
        shard_down = lax.psum_scatter(local_down.astype(jnp.bfloat16), "fsdp", scatter_dimension=0, tiled=True)
        shard_up = lax.psum_scatter(local_up.astype(jnp.bfloat16), "fsdp", scatter_dimension=0, tiled=True)
        return (
            lax.psum(shard_down, "dp").astype(jnp.float32),
            lax.psum(shard_up, "dp").astype(jnp.float32),
        )
    table = jnp.concatenate(
        [local_down.reshape(fsdp_count, down_size), local_up.reshape(fsdp_count, down_size)], axis=1
    ).reshape(fsdp_count, 2, sizes["x"], sizes["z"], chunk)

    def pairs(moved):
        return lambda k: coordinate_pairs(dp_count, fsdp_count, moved, k)

    halves = jnp.moveaxis(table, 1, 0)
    part = scatter_sum(halves, at["core"], 2, pairs("core"))
    colour = chunk // 2
    done = []
    for c, order in enumerate((("y", "x"), ("x", "y"))):
        piece = part[..., c * colour:(c + 1) * colour]
        left = ["y", "x", "z"]
        for name in order:
            piece = scatter_sum(piece, at[name], sizes[name], pairs(name), axis=left.index(name))
            left.remove(name)
        done.append(piece)
    part = jnp.concatenate(done, axis=-1)
    part = scatter_sum(part, at["z"], sizes["z"], pairs("z"))
    part = gather_blocks(part.astype(jnp.bfloat16), at["z"], sizes["z"], pairs("z"))
    part = gather_blocks(part, at["x"], sizes["x"], pairs("x"))
    part = gather_blocks(part, at["core"], 2, pairs("core"))
    flat = part.reshape(-1).astype(jnp.float32)
    return (
        flat[:down_size].reshape(local_down.shape[0] // fsdp_count, local_down.shape[1]),
        flat[down_size:].reshape(local_up.shape[0] // fsdp_count, local_up.shape[1]),
    )


def gather_first(rows, later, dp_count, fsdp_count):
    if fsdp_count != 4 or dp_count % 2 or rows.shape[0] % 2:
        full = lax.all_gather(rows, "fsdp", axis=0, tiled=True)
    else:
        (full,) = ring_gather((rows,), dp_count, fsdp_count)
    later, _ = lax.optimization_barrier((later, full))
    return (full, later)


def on_device(
    latents, noise_draw, timesteps, buckets, owners, adv_grad, w_down, w_up, t_down, t_up
):
    tile_count, tile_side = (latents.shape[0], latents.shape[1])
    dp_count = lax.axis_size("dp")
    fsdp_count = lax.axis_size("fsdp")
    full_mask, half_mask = width_masks(buckets, tile_side)
    alpha_bar = jnp.square(jnp.cos(0.5 * jnp.pi * (timesteps.astype(jnp.float32) + 0.5) / TSTEPS))
    noisy = (
        full_mask
        * (
            jnp.sqrt(alpha_bar)[:, None, None, None] * latents.astype(jnp.float32)
            + jnp.sqrt(1.0 - alpha_bar)[:, None, None, None] * noise_draw.astype(jnp.float32)
        )
    ).astype(jnp.bfloat16)
    peer_cap = max(2, (tile_count + dp_count - 1) // dp_count)
    slot_count = dp_count * peer_cap
    hit_table = (owners[:, None] == jnp.arange(dp_count, dtype=jnp.int32)[None, :]).astype(
        jnp.int32
    )
    before = jnp.cumsum(hit_table, axis=0) - hit_table
    slot_of = owners * peer_cap + jnp.sum(before * hit_table, axis=1)
    slot_hits = slot_of[None, :] == jnp.arange(slot_count, dtype=jnp.int32)[:, None]
    spread_matrix = slot_hits.astype(jnp.bfloat16)
    send_noisy = (
        jnp.dot(spread_matrix, noisy.reshape(tile_count, -1), preferred_element_type=jnp.float32)
        .astype(jnp.bfloat16)
        .reshape(dp_count, peer_cap, -1)
    )
    send_code = jnp.sum(jnp.where(slot_hits, buckets[None, :] + 1, 0), axis=1).reshape(
        dp_count, peer_cap
    )
    recv_noisy, recv_code = (
        lax.all_to_all(send_noisy, "dp", split_axis=0, concat_axis=0, tiled=True),
        lax.all_to_all(send_code, "dp", split_axis=0, concat_axis=0, tiled=True),
    )
    flat_code = recv_code.reshape(slot_count)
    live_slot = (flat_code > 0).astype(jnp.int32)
    position = jnp.cumsum(live_slot) - live_slot
    pick_hits = (live_slot[None, :] == 1) & (
        position[None, :] == jnp.arange(tile_count, dtype=jnp.int32)[:, None]
    )
    pick_matrix = pick_hits.astype(jnp.bfloat16)
    own_noisy = (
        jnp.dot(pick_matrix, recv_noisy.reshape(slot_count, -1), preferred_element_type=jnp.float32)
        .astype(jnp.bfloat16)
        .reshape(latents.shape)
    )
    own_buckets = jnp.sum(jnp.where(pick_hits, flat_code[None, :] - 1, 0), axis=1).astype(jnp.int32)
    own_full, own_half = width_masks(own_buckets, tile_side)
    student_down, w_up = gather_first(w_down, w_up, dp_count, fsdp_count)
    student_up, t_down = gather_first(w_up, t_down, dp_count, fsdp_count)
    t_down, t_up, _, _ = lax.optimization_barrier((t_down, t_up, student_down, student_up))
    teacher_down, teacher_up = gather_pair(t_down, t_up, dp_count, fsdp_count)
    student, cached = network(own_noisy, own_full, own_half, student_down, student_up)
    target, _ = network(own_noisy, own_full, own_half, teacher_down, teacher_up)
    loss_scale = jnp.float32(1.0 / (tile_count * dp_count * fsdp_count))
    flipped = flip_kernel(student_up)
    d_out, d_hidden = cotangents(
        student, target, adv_grad, own_full, own_half, flipped, cached, loss_scale
    )
    local_down = kernel_grad(cached[0], d_hidden, 2)
    local_up = kernel_grad(cached[5], d_out, 1)
    grad_down, grad_up = reduce_gradients(local_down, local_up, dp_count, fsdp_count)
    return (student, grad_down, grad_up)


def solution(mesh):
    return jax.shard_map(
        on_device,
        mesh=mesh,
        in_specs=(
            P(("dp", "fsdp"), None, None, None),
            P(("dp", "fsdp"), None, None, None),
            P(("dp", "fsdp")),
            P(("dp", "fsdp")),
            P(("dp", "fsdp")),
            P(("dp", "fsdp"), None, None, None),
            P("fsdp", None),
            P("fsdp", None),
            P("fsdp", None),
            P("fsdp", None),
        ),
        out_specs=(P(("dp", "fsdp"), None, None, None), P("fsdp", None), P("fsdp", None)),
        check_vma=False,
    )
```

```python
import jax
import jax.numpy as jnp
from jax import lax
from jax.sharding import PartitionSpec as P

GROUPS = 32
TSTEPS = 1000


distill_weight = 2.5
norm_epsilon = 1e-05


def conv_forward(volume, kernel_rows, stride):
    in_chan = volume.shape[3]
    kernel = kernel_rows.reshape(3, 3, in_chan, kernel_rows.shape[1])
    return lax.conv_general_dilated(
        volume,
        kernel,
        (stride, stride),
        ((1, 1), (1, 1)),
        dimension_numbers=("NHWC", "HWIO", "NHWC"),
        preferred_element_type=jnp.float32,
    )


def kernel_grad(volume, cotangent, stride):
    pad_upper = 1 if stride == 1 else 0
    result_grad = lax.conv_general_dilated(
        volume,
        cotangent,
        (1, 1),
        ((1, pad_upper), (1, pad_upper)),
        rhs_dilation=(stride, stride),
        dimension_numbers=("CHWN", "IHWO", "HWNC"),
        preferred_element_type=jnp.float32,
    )
    return result_grad.reshape(9 * volume.shape[3], cotangent.shape[3])


def width_masks(buckets, tile_side):
    half_side = tile_side // 2
    tile_count = buckets.shape[0]
    columns = jnp.arange(tile_side, dtype=jnp.int32)
    full_mask = (
        columns[None, None, :, None] < (tile_side - 2 * buckets)[:, None, None, None]
    ).astype(jnp.float32)
    full_mask = jnp.broadcast_to(full_mask, (tile_count, tile_side, tile_side, 1))
    half_cols = jnp.arange(half_side, dtype=jnp.int32)
    half_mask = (
        half_cols[None, None, :, None] < (half_side - buckets)[:, None, None, None]
    ).astype(jnp.float32)
    half_mask = jnp.broadcast_to(half_mask, (tile_count, half_side, half_side, 1))
    return (full_mask, half_mask)


def group_stats(hidden, half_mask):
    tile_count, height, breadth, channels = hidden.shape
    grouped = hidden.reshape(tile_count, height * breadth, GROUPS, channels // GROUPS)
    live_weight = half_mask.reshape(tile_count, height * breadth, 1, 1)
    population = jnp.sum(live_weight, axis=(1, 3), keepdims=True) * (channels // GROUPS)
    center = jnp.sum(grouped * live_weight, axis=(1, 3), keepdims=True) / population
    spread = (
        jnp.sum(jnp.square(grouped - center) * live_weight, axis=(1, 3), keepdims=True) / population
    )
    inverse = lax.rsqrt(spread + norm_epsilon)
    normed = ((grouped - center) * inverse).reshape(hidden.shape)
    return (normed, inverse, population)


def group_back(d_norm, normed, inverse, population, half_mask):
    tile_count, height, breadth, channels = d_norm.shape
    grouped_d = d_norm.reshape(tile_count, height * breadth, GROUPS, channels // GROUPS)
    grouped_n = normed.reshape(tile_count, height * breadth, GROUPS, channels // GROUPS)
    live_weight = half_mask.reshape(tile_count, height * breadth, 1, 1)
    mean_first = jnp.sum(grouped_d, axis=(1, 3), keepdims=True) / population
    mean_second = jnp.sum(grouped_d * grouped_n, axis=(1, 3), keepdims=True) / population
    result = live_weight * inverse * (grouped_d - mean_first - grouped_n * mean_second)
    return result.reshape(d_norm.shape)


def upsample(activated):
    return jnp.repeat(jnp.repeat(activated, 2, axis=1), 2, axis=2)


def network(noisy, full_mask, half_mask, down_weight, up_weight):
    hidden = conv_forward(noisy, down_weight, 2)
    normed, inverse, population = group_stats(hidden, half_mask)
    activated = (half_mask * jax.nn.silu(normed)).astype(jnp.bfloat16)
    enlarged = upsample(activated)
    output = conv_forward(enlarged, up_weight, 1)
    student = (full_mask * (noisy.astype(jnp.float32) + output)).astype(jnp.bfloat16)
    return (student, (noisy, normed, inverse, population, activated, enlarged))


def flip_kernel(up_weight):
    up_chan = up_weight.shape[0] // 9
    out_chan = up_weight.shape[1]
    return (
        up_weight.reshape(3, 3, up_chan, out_chan)[::-1, ::-1]
        .transpose(0, 1, 3, 2)
        .reshape(9 * out_chan, up_chan)
    )


def cotangents(student, target, adversarial, full_mask, half_mask, flipped, cached, loss_scale):
    source_in, normed, inverse, population, activated, enlarged = cached
    tile_count, tile_side = (student.shape[0], student.shape[1])
    half_side = tile_side // 2
    d_out = (
        full_mask
        * (
            distill_weight * (student.astype(jnp.float32) - target.astype(jnp.float32))
            + adversarial.astype(jnp.float32)
        )
        * loss_scale
    ).astype(jnp.bfloat16)
    d_up = conv_forward(d_out, flipped, 1)
    d_up = d_up.reshape(tile_count, half_side, 2, half_side, 2, flipped.shape[1])
    d_act = jnp.sum(d_up, axis=(2, 4))
    sigmoid_n = jax.nn.sigmoid(normed)
    d_norm = half_mask * d_act * sigmoid_n * (1.0 + normed * (1.0 - sigmoid_n))
    d_hidden = group_back(d_norm, normed, inverse, population, half_mask).astype(jnp.bfloat16)
    return (d_out, d_hidden)


def ring_gather(shards, dp_count, fsdp_count):
    fsdp_at = lax.axis_index("fsdp")
    core = lax.axis_index("dp") % 2
    step = 1 - 2 * core

    def lin(d, f):
        return d * fsdp_count + f

    ring_pairs = []
    for d in range(dp_count):
        toward = -1 if d % 2 == 0 else 1
        for f in range(fsdp_count):
            ring_pairs.append((lin(d, f), lin(d, (f + toward) % fsdp_count)))
    first = lax.ppermute(shards, ("dp", "fsdp"), ring_pairs)
    halves = tuple(
        lax.dynamic_slice_in_dim(piece, core * (piece.shape[0] // 2), piece.shape[0] // 2, axis=0)
        for piece in first
    )
    second = lax.ppermute(halves, ("dp", "fsdp"), ring_pairs)
    swap_pairs = [(d, d ^ 1) for d in range(dp_count)]
    other_first, other_second = lax.ppermute((first, second), "dp", swap_pairs)
    near = (fsdp_at + step + fsdp_count) % fsdp_count
    behind = (fsdp_at - step + fsdp_count) % fsdp_count
    far = (fsdp_at + 2) % fsdp_count
    gathered = []
    for own, got, got_other, half, half_other in zip(shards, first, other_first, second, other_second):
        rows = own.shape[0]
        full = jnp.zeros((fsdp_count * rows,) + own.shape[1:], own.dtype)
        full = lax.dynamic_update_slice_in_dim(full, own, fsdp_at * rows, axis=0)
        full = lax.dynamic_update_slice_in_dim(full, got, near * rows, axis=0)
        full = lax.dynamic_update_slice_in_dim(full, got_other, behind * rows, axis=0)
        full = lax.dynamic_update_slice_in_dim(full, half, far * rows + core * (rows // 2), axis=0)
        full = lax.dynamic_update_slice_in_dim(
            full, half_other, far * rows + (1 - core) * (rows // 2), axis=0
        )
        gathered.append(full)
    return (tuple(gathered), second)


def gather_pair(down_rows, up_rows, dp_count, fsdp_count):
    if fsdp_count != 4 or dp_count % 2 or down_rows.shape[0] % 2 or up_rows.shape[0] % 2:
        return (
            lax.all_gather(down_rows, "fsdp", axis=0, tiled=True),
            lax.all_gather(up_rows, "fsdp", axis=0, tiled=True),
            (down_rows, up_rows),
        )
    gathered, last_hop = ring_gather((down_rows, up_rows), dp_count, fsdp_count)
    return gathered + (last_hop,)


def coordinate_pairs(dp_count, fsdp_count, moved, shift):
    sizes = {"x": dp_count // 8, "z": 4, "core": 2, "y": fsdp_count}
    pairs = []
    for d in range(dp_count):
        for f in range(fsdp_count):
            place = {"x": d // 8, "z": (d // 2) % 4, "core": d % 2, "y": f}
            place[moved] = (place[moved] + shift) % sizes[moved]
            target = (place["x"] * 8 + place["z"] * 2 + place["core"]) * fsdp_count + place["y"]
            pairs.append((d * fsdp_count + f, target))
    return pairs


def scatter_sum(parts, at, count, pairs_of, axis=0):
    total = lax.dynamic_index_in_dim(parts, at, axis=axis, keepdims=False)
    for k in range(1, count):
        sent = lax.dynamic_index_in_dim(parts, (at + k) % count, axis=axis, keepdims=False)
        got = lax.ppermute(sent.astype(jnp.bfloat16), ("dp", "fsdp"), pairs_of(k))
        total = total + got.astype(jnp.float32)
    return total


def gather_blocks(block, at, count, pairs_of):
    full = jnp.zeros((count,) + block.shape, block.dtype)
    full = lax.dynamic_update_index_in_dim(full, block, at, axis=0)
    for k in range(1, count):
        got = lax.ppermute(block, ("dp", "fsdp"), pairs_of(k))
        full = lax.dynamic_update_index_in_dim(full, got, (at - k + count) % count, axis=0)
    return full


def reduce_gradients(local_down, local_up, dp_count, fsdp_count):
    d = lax.axis_index("dp")
    at = {"x": d // 8, "z": (d // 2) % 4, "core": d % 2, "y": lax.axis_index("fsdp")}
    sizes = {"x": dp_count // 8, "z": 4, "core": 2, "y": fsdp_count}
    down_size = local_down.size // fsdp_count
    chunk = 2 * down_size // (2 * sizes["x"] * sizes["z"])
    if dp_count != 32 or fsdp_count != 4 or chunk % 2:
        shard_down = lax.psum_scatter(local_down.astype(jnp.bfloat16), "fsdp", scatter_dimension=0, tiled=True)
        shard_up = lax.psum_scatter(local_up.astype(jnp.bfloat16), "fsdp", scatter_dimension=0, tiled=True)
        return (
            lax.psum(shard_down, "dp").astype(jnp.float32),
            lax.psum(shard_up, "dp").astype(jnp.float32),
        )
    table = jnp.concatenate(
        [local_down.reshape(fsdp_count, down_size), local_up.reshape(fsdp_count, down_size)], axis=1
    ).reshape(fsdp_count, 2, sizes["x"], sizes["z"], chunk)

    def pairs(moved):
        return lambda k: coordinate_pairs(dp_count, fsdp_count, moved, k)

    halves = jnp.moveaxis(table, 1, 0)
    part = scatter_sum(halves, at["core"], 2, pairs("core"))
    colour = chunk // 2
    done = []
    for c, order in enumerate((("y", "x"), ("x", "y"))):
        piece = part[..., c * colour:(c + 1) * colour]
        left = ["y", "x", "z"]
        for name in order:
            piece = scatter_sum(piece, at[name], sizes[name], pairs(name), axis=left.index(name))
            left.remove(name)
        done.append(piece)
    part = jnp.concatenate(done, axis=-1)
    part = scatter_sum(part, at["z"], sizes["z"], pairs("z"))
    part = gather_blocks(part.astype(jnp.bfloat16), at["z"], sizes["z"], pairs("z"))
    part = gather_blocks(part, at["x"], sizes["x"], pairs("x"))
    part = gather_blocks(part, at["core"], 2, pairs("core"))
    flat = part.reshape(-1).astype(jnp.float32)
    return (
        flat[:down_size].reshape(local_down.shape[0] // fsdp_count, local_down.shape[1]),
        flat[down_size:].reshape(local_up.shape[0] // fsdp_count, local_up.shape[1]),
    )


def on_device(
    latents, noise_draw, timesteps, buckets, owners, adv_grad, w_down, w_up, t_down, t_up
):
    tile_count, tile_side = (latents.shape[0], latents.shape[1])
    dp_count = lax.axis_size("dp")
    fsdp_count = lax.axis_size("fsdp")
    full_mask, half_mask = width_masks(buckets, tile_side)
    alpha_bar = jnp.square(jnp.cos(0.5 * jnp.pi * (timesteps.astype(jnp.float32) + 0.5) / TSTEPS))
    noisy = (
        full_mask
        * (
            jnp.sqrt(alpha_bar)[:, None, None, None] * latents.astype(jnp.float32)
            + jnp.sqrt(1.0 - alpha_bar)[:, None, None, None] * noise_draw.astype(jnp.float32)
        )
    ).astype(jnp.bfloat16)
    peer_cap = max(2, (tile_count + dp_count - 1) // dp_count)
    slot_count = dp_count * peer_cap
    hit_table = (owners[:, None] == jnp.arange(dp_count, dtype=jnp.int32)[None, :]).astype(
        jnp.int32
    )
    before = jnp.cumsum(hit_table, axis=0) - hit_table
    slot_of = owners * peer_cap + jnp.sum(before * hit_table, axis=1)
    slot_hits = slot_of[None, :] == jnp.arange(slot_count, dtype=jnp.int32)[:, None]
    spread_matrix = slot_hits.astype(jnp.bfloat16)
    send_noisy = (
        jnp.dot(spread_matrix, noisy.reshape(tile_count, -1), preferred_element_type=jnp.float32)
        .astype(jnp.bfloat16)
        .reshape(dp_count, peer_cap, -1)
    )
    send_code = jnp.sum(jnp.where(slot_hits, buckets[None, :] + 1, 0), axis=1).reshape(
        dp_count, peer_cap
    )
    recv_noisy, recv_code = (
        lax.all_to_all(send_noisy, "dp", split_axis=0, concat_axis=0, tiled=True),
        lax.all_to_all(send_code, "dp", split_axis=0, concat_axis=0, tiled=True),
    )
    flat_code = recv_code.reshape(slot_count)
    live_slot = (flat_code > 0).astype(jnp.int32)
    position = jnp.cumsum(live_slot) - live_slot
    pick_hits = (live_slot[None, :] == 1) & (
        position[None, :] == jnp.arange(tile_count, dtype=jnp.int32)[:, None]
    )
    pick_matrix = pick_hits.astype(jnp.bfloat16)
    own_noisy = (
        jnp.dot(pick_matrix, recv_noisy.reshape(slot_count, -1), preferred_element_type=jnp.float32)
        .astype(jnp.bfloat16)
        .reshape(latents.shape)
    )
    own_buckets = jnp.sum(jnp.where(pick_hits, flat_code[None, :] - 1, 0), axis=1).astype(jnp.int32)
    own_full, own_half = width_masks(own_buckets, tile_side)
    student_down, student_up, student_hop = gather_pair(w_down, w_up, dp_count, fsdp_count)
    t_down, t_up, _ = lax.optimization_barrier((t_down, t_up, student_hop))
    teacher_down, teacher_up, _ = gather_pair(t_down, t_up, dp_count, fsdp_count)
    student, cached = network(own_noisy, own_full, own_half, student_down, student_up)
    target, _ = network(own_noisy, own_full, own_half, teacher_down, teacher_up)
    loss_scale = jnp.float32(1.0 / (tile_count * dp_count * fsdp_count))
    flipped = flip_kernel(student_up)
    d_out, d_hidden = cotangents(
        student, target, adv_grad, own_full, own_half, flipped, cached, loss_scale
    )
    local_down = kernel_grad(cached[0], d_hidden, 2)
    local_up = kernel_grad(cached[5], d_out, 1)
    grad_down, grad_up = reduce_gradients(local_down, local_up, dp_count, fsdp_count)
    return (student, grad_down, grad_up)


def solution(mesh):
    return jax.shard_map(
        on_device,
        mesh=mesh,
        in_specs=(
            P(("dp", "fsdp"), None, None, None),
            P(("dp", "fsdp"), None, None, None),
            P(("dp", "fsdp")),
            P(("dp", "fsdp")),
            P(("dp", "fsdp")),
            P(("dp", "fsdp"), None, None, None),
            P("fsdp", None),
            P("fsdp", None),
            P("fsdp", None),
            P("fsdp", None),
        ),
        out_specs=(P(("dp", "fsdp"), None, None, None), P("fsdp", None), P("fsdp", None)),
        check_vma=False,
    )
```

```python
import jax
import jax.numpy as jnp
from jax import lax
from jax.sharding import PartitionSpec as P

GROUPS = 32
TSTEPS = 1000


distill_weight = 2.5
norm_epsilon = 1e-05


def conv_forward(volume, kernel_rows, stride):
    in_chan = volume.shape[3]
    kernel = kernel_rows.reshape(3, 3, in_chan, kernel_rows.shape[1])
    return lax.conv_general_dilated(
        volume,
        kernel,
        (stride, stride),
        ((1, 1), (1, 1)),
        dimension_numbers=("NHWC", "HWIO", "NHWC"),
        preferred_element_type=jnp.float32,
    )


def kernel_grad(volume, cotangent, stride):
    pad_upper = 1 if stride == 1 else 0
    result_grad = lax.conv_general_dilated(
        volume,
        cotangent,
        (1, 1),
        ((1, pad_upper), (1, pad_upper)),
        rhs_dilation=(stride, stride),
        dimension_numbers=("CHWN", "IHWO", "HWNC"),
        preferred_element_type=jnp.float32,
    )
    return result_grad.reshape(9 * volume.shape[3], cotangent.shape[3])


def width_masks(buckets, tile_side):
    half_side = tile_side // 2
    tile_count = buckets.shape[0]
    columns = jnp.arange(tile_side, dtype=jnp.int32)
    full_mask = (
        columns[None, None, :, None] < (tile_side - 2 * buckets)[:, None, None, None]
    ).astype(jnp.float32)
    full_mask = jnp.broadcast_to(full_mask, (tile_count, tile_side, tile_side, 1))
    half_cols = jnp.arange(half_side, dtype=jnp.int32)
    half_mask = (
        half_cols[None, None, :, None] < (half_side - buckets)[:, None, None, None]
    ).astype(jnp.float32)
    half_mask = jnp.broadcast_to(half_mask, (tile_count, half_side, half_side, 1))
    return (full_mask, half_mask)


def group_stats(hidden, half_mask):
    tile_count, height, breadth, channels = hidden.shape
    grouped = hidden.reshape(tile_count, height * breadth, GROUPS, channels // GROUPS)
    live_weight = half_mask.reshape(tile_count, height * breadth, 1, 1)
    population = jnp.sum(live_weight, axis=(1, 3), keepdims=True) * (channels // GROUPS)
    center = jnp.sum(grouped * live_weight, axis=(1, 3), keepdims=True) / population
    spread = (
        jnp.sum(jnp.square(grouped - center) * live_weight, axis=(1, 3), keepdims=True) / population
    )
    inverse = lax.rsqrt(spread + norm_epsilon)
    normed = ((grouped - center) * inverse).reshape(hidden.shape)
    return (normed, inverse, population)


def group_back(d_norm, normed, inverse, population, half_mask):
    tile_count, height, breadth, channels = d_norm.shape
    grouped_d = d_norm.reshape(tile_count, height * breadth, GROUPS, channels // GROUPS)
    grouped_n = normed.reshape(tile_count, height * breadth, GROUPS, channels // GROUPS)
    live_weight = half_mask.reshape(tile_count, height * breadth, 1, 1)
    mean_first = jnp.sum(grouped_d, axis=(1, 3), keepdims=True) / population
    mean_second = jnp.sum(grouped_d * grouped_n, axis=(1, 3), keepdims=True) / population
    result = live_weight * inverse * (grouped_d - mean_first - grouped_n * mean_second)
    return result.reshape(d_norm.shape)


def upsample(activated):
    return jnp.repeat(jnp.repeat(activated, 2, axis=1), 2, axis=2)


def network(noisy, full_mask, half_mask, down_weight, up_weight):
    hidden = conv_forward(noisy, down_weight, 2)
    normed, inverse, population = group_stats(hidden, half_mask)
    activated = (half_mask * jax.nn.silu(normed)).astype(jnp.bfloat16)
    enlarged = upsample(activated)
    output = conv_forward(enlarged, up_weight, 1)
    student = (full_mask * (noisy.astype(jnp.float32) + output)).astype(jnp.bfloat16)
    return (student, (noisy, normed, inverse, population, activated, enlarged))


def flip_kernel(up_weight):
    up_chan = up_weight.shape[0] // 9
    out_chan = up_weight.shape[1]
    return (
        up_weight.reshape(3, 3, up_chan, out_chan)[::-1, ::-1]
        .transpose(0, 1, 3, 2)
        .reshape(9 * out_chan, up_chan)
    )


def cotangents(student, target, adversarial, full_mask, half_mask, flipped, cached, loss_scale):
    source_in, normed, inverse, population, activated, enlarged = cached
    tile_count, tile_side = (student.shape[0], student.shape[1])
    half_side = tile_side // 2
    d_out = (
        full_mask
        * (
            distill_weight * (student.astype(jnp.float32) - target.astype(jnp.float32))
            + adversarial.astype(jnp.float32)
        )
        * loss_scale
    ).astype(jnp.bfloat16)
    d_up = conv_forward(d_out, flipped, 1)
    d_up = d_up.reshape(tile_count, half_side, 2, half_side, 2, flipped.shape[1])
    d_act = jnp.sum(d_up, axis=(2, 4))
    sigmoid_n = jax.nn.sigmoid(normed)
    d_norm = half_mask * d_act * sigmoid_n * (1.0 + normed * (1.0 - sigmoid_n))
    d_hidden = group_back(d_norm, normed, inverse, population, half_mask).astype(jnp.bfloat16)
    return (d_out, d_hidden)


def ring_gather(shards, dp_count, fsdp_count):
    fsdp_at = lax.axis_index("fsdp")
    core = lax.axis_index("dp") % 2
    step = 1 - 2 * core

    def lin(d, f):
        return d * fsdp_count + f

    ring_pairs = []
    for d in range(dp_count):
        toward = -1 if d % 2 == 0 else 1
        for f in range(fsdp_count):
            ring_pairs.append((lin(d, f), lin(d, (f + toward) % fsdp_count)))
    first = lax.ppermute(shards, ("dp", "fsdp"), ring_pairs)
    halves = tuple(
        lax.dynamic_slice_in_dim(piece, core * (piece.shape[0] // 2), piece.shape[0] // 2, axis=0)
        for piece in first
    )
    second = lax.ppermute(halves, ("dp", "fsdp"), ring_pairs)
    swap_pairs = [(d, d ^ 1) for d in range(dp_count)]
    other_first, other_second = lax.ppermute((first, second), "dp", swap_pairs)
    near = (fsdp_at + step + fsdp_count) % fsdp_count
    behind = (fsdp_at - step + fsdp_count) % fsdp_count
    far = (fsdp_at + 2) % fsdp_count
    gathered = []
    for own, got, got_other, half, half_other in zip(shards, first, other_first, second, other_second):
        rows = own.shape[0]
        full = jnp.zeros((fsdp_count * rows,) + own.shape[1:], own.dtype)
        full = lax.dynamic_update_slice_in_dim(full, own, fsdp_at * rows, axis=0)
        full = lax.dynamic_update_slice_in_dim(full, got, near * rows, axis=0)
        full = lax.dynamic_update_slice_in_dim(full, got_other, behind * rows, axis=0)
        full = lax.dynamic_update_slice_in_dim(full, half, far * rows + core * (rows // 2), axis=0)
        full = lax.dynamic_update_slice_in_dim(
            full, half_other, far * rows + (1 - core) * (rows // 2), axis=0
        )
        gathered.append(full)
    return tuple(gathered)


def gather_pair(down_rows, up_rows, dp_count, fsdp_count):
    if fsdp_count != 4 or dp_count % 2 or down_rows.shape[0] % 2 or up_rows.shape[0] % 2:
        return (
            lax.all_gather(down_rows, "fsdp", axis=0, tiled=True),
            lax.all_gather(up_rows, "fsdp", axis=0, tiled=True),
        )
    return ring_gather((down_rows, up_rows), dp_count, fsdp_count)


def coordinate_pairs(dp_count, fsdp_count, moved, shift):
    sizes = {"x": dp_count // 8, "z": 4, "core": 2, "y": fsdp_count}
    pairs = []
    for d in range(dp_count):
        for f in range(fsdp_count):
            place = {"x": d // 8, "z": (d // 2) % 4, "core": d % 2, "y": f}
            place[moved] = (place[moved] + shift) % sizes[moved]
            target = (place["x"] * 8 + place["z"] * 2 + place["core"]) * fsdp_count + place["y"]
            pairs.append((d * fsdp_count + f, target))
    return pairs


def scatter_sum(parts, at, count, pairs_of, axis=0):
    total = lax.dynamic_index_in_dim(parts, at, axis=axis, keepdims=False).astype(jnp.float32)
    for k in range(1, count):
        sent = lax.dynamic_index_in_dim(parts, (at + k) % count, axis=axis, keepdims=False)
        got = lax.ppermute(sent.astype(jnp.bfloat16), ("dp", "fsdp"), pairs_of(k))
        total = total + got.astype(jnp.float32)
    return total


def gather_blocks(block, at, count, pairs_of):
    full = jnp.zeros((count,) + block.shape, block.dtype)
    full = lax.dynamic_update_index_in_dim(full, block, at, axis=0)
    for k in range(1, count):
        got = lax.ppermute(block, ("dp", "fsdp"), pairs_of(k))
        full = lax.dynamic_update_index_in_dim(full, got, (at - k + count) % count, axis=0)
    return full


def reduce_gradients(local_down, local_up, dp_count, fsdp_count):
    d = lax.axis_index("dp")
    at = {"x": d // 8, "z": (d // 2) % 4, "core": d % 2, "y": lax.axis_index("fsdp")}
    sizes = {"x": dp_count // 8, "z": 4, "core": 2, "y": fsdp_count}
    down_size = local_down.size // fsdp_count
    chunk = 2 * down_size // (2 * sizes["x"] * sizes["z"])
    if dp_count != 32 or fsdp_count != 4 or chunk % 2:
        shard_down = lax.psum_scatter(local_down.astype(jnp.bfloat16), "fsdp", scatter_dimension=0, tiled=True)
        shard_up = lax.psum_scatter(local_up.astype(jnp.bfloat16), "fsdp", scatter_dimension=0, tiled=True)
        return (
            lax.psum(shard_down, "dp").astype(jnp.float32),
            lax.psum(shard_up, "dp").astype(jnp.float32),
        )
    table = jnp.concatenate(
        [
            local_down.astype(jnp.bfloat16).reshape(fsdp_count, down_size),
            local_up.astype(jnp.bfloat16).reshape(fsdp_count, down_size),
        ],
        axis=1,
    ).reshape(fsdp_count, 2, sizes["x"], sizes["z"], chunk)

    def pairs(moved):
        return lambda k: coordinate_pairs(dp_count, fsdp_count, moved, k)

    halves = jnp.moveaxis(table, 1, 0)
    part = scatter_sum(halves, at["core"], 2, pairs("core"))
    colour = chunk // 2
    done = []
    for c, order in enumerate((("y", "x"), ("x", "y"))):
        piece = part[..., c * colour:(c + 1) * colour]
        left = ["y", "x", "z"]
        for name in order:
            piece = scatter_sum(piece, at[name], sizes[name], pairs(name), axis=left.index(name))
            left.remove(name)
        done.append(piece)
    part = jnp.concatenate(done, axis=-1)
    part = scatter_sum(part, at["z"], sizes["z"], pairs("z"))
    part = gather_blocks(part.astype(jnp.bfloat16), at["z"], sizes["z"], pairs("z"))
    part = gather_blocks(part, at["x"], sizes["x"], pairs("x"))
    part = gather_blocks(part, at["core"], 2, pairs("core"))
    flat = part.reshape(-1).astype(jnp.float32)
    return (
        flat[:down_size].reshape(local_down.shape[0] // fsdp_count, local_down.shape[1]),
        flat[down_size:].reshape(local_up.shape[0] // fsdp_count, local_up.shape[1]),
    )


def on_device(
    latents, noise_draw, timesteps, buckets, owners, adv_grad, w_down, w_up, t_down, t_up
):
    tile_count, tile_side = (latents.shape[0], latents.shape[1])
    dp_count = lax.axis_size("dp")
    fsdp_count = lax.axis_size("fsdp")
    full_mask, half_mask = width_masks(buckets, tile_side)
    alpha_bar = jnp.square(jnp.cos(0.5 * jnp.pi * (timesteps.astype(jnp.float32) + 0.5) / TSTEPS))
    noisy = (
        full_mask
        * (
            jnp.sqrt(alpha_bar)[:, None, None, None] * latents.astype(jnp.float32)
            + jnp.sqrt(1.0 - alpha_bar)[:, None, None, None] * noise_draw.astype(jnp.float32)
        )
    ).astype(jnp.bfloat16)
    peer_cap = max(2, (tile_count + dp_count - 1) // dp_count)
    slot_count = dp_count * peer_cap
    hit_table = (owners[:, None] == jnp.arange(dp_count, dtype=jnp.int32)[None, :]).astype(
        jnp.int32
    )
    before = jnp.cumsum(hit_table, axis=0) - hit_table
    slot_of = owners * peer_cap + jnp.sum(before * hit_table, axis=1)
    slot_hits = slot_of[None, :] == jnp.arange(slot_count, dtype=jnp.int32)[:, None]
    spread_matrix = slot_hits.astype(jnp.bfloat16)
    send_noisy = (
        jnp.dot(spread_matrix, noisy.reshape(tile_count, -1), preferred_element_type=jnp.float32)
        .astype(jnp.bfloat16)
        .reshape(dp_count, peer_cap, -1)
    )
    send_code = jnp.sum(jnp.where(slot_hits, buckets[None, :] + 1, 0), axis=1).reshape(
        dp_count, peer_cap
    )
    recv_noisy, recv_code = (
        lax.all_to_all(send_noisy, "dp", split_axis=0, concat_axis=0, tiled=True),
        lax.all_to_all(send_code, "dp", split_axis=0, concat_axis=0, tiled=True),
    )
    flat_code = recv_code.reshape(slot_count)
    live_slot = (flat_code > 0).astype(jnp.int32)
    position = jnp.cumsum(live_slot) - live_slot
    pick_hits = (live_slot[None, :] == 1) & (
        position[None, :] == jnp.arange(tile_count, dtype=jnp.int32)[:, None]
    )
    pick_matrix = pick_hits.astype(jnp.bfloat16)
    own_noisy = (
        jnp.dot(pick_matrix, recv_noisy.reshape(slot_count, -1), preferred_element_type=jnp.float32)
        .astype(jnp.bfloat16)
        .reshape(latents.shape)
    )
    own_buckets = jnp.sum(jnp.where(pick_hits, flat_code[None, :] - 1, 0), axis=1).astype(jnp.int32)
    own_full, own_half = width_masks(own_buckets, tile_side)
    student_down, student_up = gather_pair(w_down, w_up, dp_count, fsdp_count)
    t_down, t_up, _, _ = lax.optimization_barrier((t_down, t_up, student_down, student_up))
    teacher_down, teacher_up = gather_pair(t_down, t_up, dp_count, fsdp_count)
    student, cached = network(own_noisy, own_full, own_half, student_down, student_up)
    target, _ = network(own_noisy, own_full, own_half, teacher_down, teacher_up)
    loss_scale = jnp.float32(1.0 / (tile_count * dp_count * fsdp_count))
    flipped = flip_kernel(student_up)
    d_out, d_hidden = cotangents(
        student, target, adv_grad, own_full, own_half, flipped, cached, loss_scale
    )
    local_down = kernel_grad(cached[0], d_hidden, 2)
    local_up = kernel_grad(cached[5], d_out, 1)
    grad_down, grad_up = reduce_gradients(local_down, local_up, dp_count, fsdp_count)
    return (student, grad_down, grad_up)


def solution(mesh):
    return jax.shard_map(
        on_device,
        mesh=mesh,
        in_specs=(
            P(("dp", "fsdp"), None, None, None),
            P(("dp", "fsdp"), None, None, None),
            P(("dp", "fsdp")),
            P(("dp", "fsdp")),
            P(("dp", "fsdp")),
            P(("dp", "fsdp"), None, None, None),
            P("fsdp", None),
            P("fsdp", None),
            P("fsdp", None),
            P("fsdp", None),
        ),
        out_specs=(P(("dp", "fsdp"), None, None, None), P("fsdp", None), P("fsdp", None)),
        check_vma=False,
    )
```

```python
import jax
import jax.numpy as jnp
from jax import lax
from jax.sharding import PartitionSpec as P

GROUPS = 32
TSTEPS = 1000


distill_weight = 2.5
norm_epsilon = 1e-05


def conv_forward(volume, kernel_rows, stride):
    in_chan = volume.shape[3]
    kernel = kernel_rows.reshape(3, 3, in_chan, kernel_rows.shape[1])
    return lax.conv_general_dilated(
        volume,
        kernel,
        (stride, stride),
        ((1, 1), (1, 1)),
        dimension_numbers=("NHWC", "HWIO", "NHWC"),
        preferred_element_type=jnp.float32,
    )


def kernel_grad(volume, cotangent, stride):
    pad_upper = 1 if stride == 1 else 0
    result_grad = lax.conv_general_dilated(
        volume,
        cotangent,
        (1, 1),
        ((1, pad_upper), (1, pad_upper)),
        rhs_dilation=(stride, stride),
        dimension_numbers=("CHWN", "IHWO", "HWNC"),
        preferred_element_type=jnp.float32,
    )
    return result_grad.reshape(9 * volume.shape[3], cotangent.shape[3])


def width_masks(buckets, tile_side):
    half_side = tile_side // 2
    tile_count = buckets.shape[0]
    columns = jnp.arange(tile_side, dtype=jnp.int32)
    full_mask = (
        columns[None, None, :, None] < (tile_side - 2 * buckets)[:, None, None, None]
    ).astype(jnp.float32)
    full_mask = jnp.broadcast_to(full_mask, (tile_count, tile_side, tile_side, 1))
    half_cols = jnp.arange(half_side, dtype=jnp.int32)
    half_mask = (
        half_cols[None, None, :, None] < (half_side - buckets)[:, None, None, None]
    ).astype(jnp.float32)
    half_mask = jnp.broadcast_to(half_mask, (tile_count, half_side, half_side, 1))
    return (full_mask, half_mask)


def group_stats(hidden, half_mask):
    tile_count, height, breadth, channels = hidden.shape
    grouped = hidden.reshape(tile_count, height * breadth, GROUPS, channels // GROUPS)
    live_weight = half_mask.reshape(tile_count, height * breadth, 1, 1)
    population = jnp.sum(live_weight, axis=(1, 3), keepdims=True) * (channels // GROUPS)
    center = jnp.sum(grouped * live_weight, axis=(1, 3), keepdims=True) / population
    spread = (
        jnp.sum(jnp.square(grouped - center) * live_weight, axis=(1, 3), keepdims=True) / population
    )
    inverse = lax.rsqrt(spread + norm_epsilon)
    normed = ((grouped - center) * inverse).reshape(hidden.shape)
    return (normed, inverse, population)


def group_back(d_norm, normed, inverse, population, half_mask):
    tile_count, height, breadth, channels = d_norm.shape
    grouped_d = d_norm.reshape(tile_count, height * breadth, GROUPS, channels // GROUPS)
    grouped_n = normed.reshape(tile_count, height * breadth, GROUPS, channels // GROUPS)
    live_weight = half_mask.reshape(tile_count, height * breadth, 1, 1)
    mean_first = jnp.sum(grouped_d, axis=(1, 3), keepdims=True) / population
    mean_second = jnp.sum(grouped_d * grouped_n, axis=(1, 3), keepdims=True) / population
    result = live_weight * inverse * (grouped_d - mean_first - grouped_n * mean_second)
    return result.reshape(d_norm.shape)


def upsample(activated):
    return jnp.repeat(jnp.repeat(activated, 2, axis=1), 2, axis=2)


def network(noisy, full_mask, half_mask, down_weight, up_weight):
    hidden = conv_forward(noisy, down_weight, 2)
    normed, inverse, population = group_stats(hidden, half_mask)
    activated = (half_mask * jax.nn.silu(normed)).astype(jnp.bfloat16)
    enlarged = upsample(activated)
    output = conv_forward(enlarged, up_weight, 1)
    student = (full_mask * (noisy.astype(jnp.float32) + output)).astype(jnp.bfloat16)
    return (student, (noisy, normed, inverse, population, activated, enlarged))


def flip_kernel(up_weight):
    up_chan = up_weight.shape[0] // 9
    out_chan = up_weight.shape[1]
    return (
        up_weight.reshape(3, 3, up_chan, out_chan)[::-1, ::-1]
        .transpose(0, 1, 3, 2)
        .reshape(9 * out_chan, up_chan)
    )


def cotangents(student, target, adversarial, full_mask, half_mask, flipped, cached, loss_scale):
    source_in, normed, inverse, population, activated, enlarged = cached
    tile_count, tile_side = (student.shape[0], student.shape[1])
    half_side = tile_side // 2
    d_out = (
        full_mask
        * (
            distill_weight * (student.astype(jnp.float32) - target.astype(jnp.float32))
            + adversarial.astype(jnp.float32)
        )
        * loss_scale
    ).astype(jnp.bfloat16)
    d_up = conv_forward(d_out, flipped, 1)
    d_up = d_up.reshape(tile_count, half_side, 2, half_side, 2, flipped.shape[1])
    d_act = jnp.sum(d_up, axis=(2, 4))
    sigmoid_n = jax.nn.sigmoid(normed)
    d_norm = half_mask * d_act * sigmoid_n * (1.0 + normed * (1.0 - sigmoid_n))
    d_hidden = group_back(d_norm, normed, inverse, population, half_mask).astype(jnp.bfloat16)
    return (d_out, d_hidden)


def ring_gather(shards, dp_count, fsdp_count):
    fsdp_at = lax.axis_index("fsdp")
    core = lax.axis_index("dp") % 2
    step = 1 - 2 * core

    def lin(d, f):
        return d * fsdp_count + f

    ring_pairs = []
    for d in range(dp_count):
        toward = -1 if d % 2 == 0 else 1
        for f in range(fsdp_count):
            ring_pairs.append((lin(d, f), lin(d, (f + toward) % fsdp_count)))
    first = lax.ppermute(shards, ("dp", "fsdp"), ring_pairs)
    halves = tuple(
        lax.dynamic_slice_in_dim(piece, core * (piece.shape[0] // 2), piece.shape[0] // 2, axis=0)
        for piece in first
    )
    second = lax.ppermute(halves, ("dp", "fsdp"), ring_pairs)
    swap_pairs = [(d, d ^ 1) for d in range(dp_count)]
    other_first, other_second = lax.ppermute((first, second), "dp", swap_pairs)
    near = (fsdp_at + step + fsdp_count) % fsdp_count
    behind = (fsdp_at - step + fsdp_count) % fsdp_count
    far = (fsdp_at + 2) % fsdp_count
    gathered = []
    for own, got, got_other, half, half_other in zip(shards, first, other_first, second, other_second):
        rows = own.shape[0]
        full = jnp.zeros((fsdp_count * rows,) + own.shape[1:], own.dtype)
        full = lax.dynamic_update_slice_in_dim(full, own, fsdp_at * rows, axis=0)
        full = lax.dynamic_update_slice_in_dim(full, got, near * rows, axis=0)
        full = lax.dynamic_update_slice_in_dim(full, got_other, behind * rows, axis=0)
        full = lax.dynamic_update_slice_in_dim(full, half, far * rows + core * (rows // 2), axis=0)
        full = lax.dynamic_update_slice_in_dim(
            full, half_other, far * rows + (1 - core) * (rows // 2), axis=0
        )
        gathered.append(full)
    return tuple(gathered)


def gather_pair(down_rows, up_rows, dp_count, fsdp_count):
    if fsdp_count != 4 or dp_count % 2 or down_rows.shape[0] % 2 or up_rows.shape[0] % 2:
        return (
            lax.all_gather(down_rows, "fsdp", axis=0, tiled=True),
            lax.all_gather(up_rows, "fsdp", axis=0, tiled=True),
        )
    return ring_gather((down_rows, up_rows), dp_count, fsdp_count)


def coordinate_pairs(dp_count, fsdp_count, moved, shift):
    sizes = {"x": dp_count // 8, "z": 4, "core": 2, "y": fsdp_count}
    pairs = []
    for d in range(dp_count):
        for f in range(fsdp_count):
            place = {"x": d // 8, "z": (d // 2) % 4, "core": d % 2, "y": f}
            place[moved] = (place[moved] + shift) % sizes[moved]
            target = (place["x"] * 8 + place["z"] * 2 + place["core"]) * fsdp_count + place["y"]
            pairs.append((d * fsdp_count + f, target))
    return pairs


def scatter_sum(parts, at, count, pairs_of, axis=0):
    total = lax.dynamic_index_in_dim(parts, at, axis=axis, keepdims=False).astype(jnp.float32)
    for k in range(1, count):
        sent = lax.dynamic_index_in_dim(parts, (at + k) % count, axis=axis, keepdims=False)
        got = lax.ppermute(sent.astype(jnp.bfloat16), ("dp", "fsdp"), pairs_of(k))
        total = total + got.astype(jnp.float32)
    return total.astype(jnp.bfloat16)


def gather_blocks(block, at, count, pairs_of):
    full = jnp.zeros((count,) + block.shape, block.dtype)
    full = lax.dynamic_update_index_in_dim(full, block, at, axis=0)
    for k in range(1, count):
        got = lax.ppermute(block, ("dp", "fsdp"), pairs_of(k))
        full = lax.dynamic_update_index_in_dim(full, got, (at - k + count) % count, axis=0)
    return full


def reduce_gradients(local_down, local_up, dp_count, fsdp_count):
    d = lax.axis_index("dp")
    at = {"x": d // 8, "z": (d // 2) % 4, "core": d % 2, "y": lax.axis_index("fsdp")}
    sizes = {"x": dp_count // 8, "z": 4, "core": 2, "y": fsdp_count}
    down_size = local_down.size // fsdp_count
    chunk = 2 * down_size // (2 * sizes["x"] * sizes["z"])
    if dp_count != 32 or fsdp_count != 4 or chunk % 2:
        shard_down = lax.psum_scatter(local_down.astype(jnp.bfloat16), "fsdp", scatter_dimension=0, tiled=True)
        shard_up = lax.psum_scatter(local_up.astype(jnp.bfloat16), "fsdp", scatter_dimension=0, tiled=True)
        return (
            lax.psum(shard_down, "dp").astype(jnp.float32),
            lax.psum(shard_up, "dp").astype(jnp.float32),
        )
    table = jnp.concatenate(
        [
            local_down.astype(jnp.bfloat16).reshape(fsdp_count, down_size),
            local_up.astype(jnp.bfloat16).reshape(fsdp_count, down_size),
        ],
        axis=1,
    ).reshape(fsdp_count, 2, sizes["x"], sizes["z"], chunk)

    def pairs(moved):
        return lambda k: coordinate_pairs(dp_count, fsdp_count, moved, k)

    halves = jnp.moveaxis(table, 1, 0)
    part = scatter_sum(halves, at["core"], 2, pairs("core"))
    colour = chunk // 2
    done = []
    for c, order in enumerate((("y", "x"), ("x", "y"))):
        piece = part[..., c * colour:(c + 1) * colour]
        left = ["y", "x", "z"]
        for name in order:
            piece = scatter_sum(piece, at[name], sizes[name], pairs(name), axis=left.index(name))
            left.remove(name)
        done.append(piece)
    part = jnp.concatenate(done, axis=-1)
    part = scatter_sum(part, at["z"], sizes["z"], pairs("z"))
    part = gather_blocks(part.astype(jnp.bfloat16), at["z"], sizes["z"], pairs("z"))
    part = gather_blocks(part, at["x"], sizes["x"], pairs("x"))
    part = gather_blocks(part, at["core"], 2, pairs("core"))
    flat = part.reshape(-1).astype(jnp.float32)
    return (
        flat[:down_size].reshape(local_down.shape[0] // fsdp_count, local_down.shape[1]),
        flat[down_size:].reshape(local_up.shape[0] // fsdp_count, local_up.shape[1]),
    )


def on_device(
    latents, noise_draw, timesteps, buckets, owners, adv_grad, w_down, w_up, t_down, t_up
):
    tile_count, tile_side = (latents.shape[0], latents.shape[1])
    dp_count = lax.axis_size("dp")
    fsdp_count = lax.axis_size("fsdp")
    full_mask, half_mask = width_masks(buckets, tile_side)
    alpha_bar = jnp.square(jnp.cos(0.5 * jnp.pi * (timesteps.astype(jnp.float32) + 0.5) / TSTEPS))
    noisy = (
        full_mask
        * (
            jnp.sqrt(alpha_bar)[:, None, None, None] * latents.astype(jnp.float32)
            + jnp.sqrt(1.0 - alpha_bar)[:, None, None, None] * noise_draw.astype(jnp.float32)
        )
    ).astype(jnp.bfloat16)
    peer_cap = max(2, (tile_count + dp_count - 1) // dp_count)
    slot_count = dp_count * peer_cap
    hit_table = (owners[:, None] == jnp.arange(dp_count, dtype=jnp.int32)[None, :]).astype(
        jnp.int32
    )
    before = jnp.cumsum(hit_table, axis=0) - hit_table
    slot_of = owners * peer_cap + jnp.sum(before * hit_table, axis=1)
    slot_hits = slot_of[None, :] == jnp.arange(slot_count, dtype=jnp.int32)[:, None]
    spread_matrix = slot_hits.astype(jnp.bfloat16)
    send_noisy = (
        jnp.dot(spread_matrix, noisy.reshape(tile_count, -1), preferred_element_type=jnp.float32)
        .astype(jnp.bfloat16)
        .reshape(dp_count, peer_cap, -1)
    )
    send_code = jnp.sum(jnp.where(slot_hits, buckets[None, :] + 1, 0), axis=1).reshape(
        dp_count, peer_cap
    )
    recv_noisy, recv_code = (
        lax.all_to_all(send_noisy, "dp", split_axis=0, concat_axis=0, tiled=True),
        lax.all_to_all(send_code, "dp", split_axis=0, concat_axis=0, tiled=True),
    )
    flat_code = recv_code.reshape(slot_count)
    live_slot = (flat_code > 0).astype(jnp.int32)
    position = jnp.cumsum(live_slot) - live_slot
    pick_hits = (live_slot[None, :] == 1) & (
        position[None, :] == jnp.arange(tile_count, dtype=jnp.int32)[:, None]
    )
    pick_matrix = pick_hits.astype(jnp.bfloat16)
    own_noisy = (
        jnp.dot(pick_matrix, recv_noisy.reshape(slot_count, -1), preferred_element_type=jnp.float32)
        .astype(jnp.bfloat16)
        .reshape(latents.shape)
    )
    own_buckets = jnp.sum(jnp.where(pick_hits, flat_code[None, :] - 1, 0), axis=1).astype(jnp.int32)
    own_full, own_half = width_masks(own_buckets, tile_side)
    student_down, student_up = gather_pair(w_down, w_up, dp_count, fsdp_count)
    t_down, t_up, _, _ = lax.optimization_barrier((t_down, t_up, student_down, student_up))
    teacher_down, teacher_up = gather_pair(t_down, t_up, dp_count, fsdp_count)
    student, cached = network(own_noisy, own_full, own_half, student_down, student_up)
    target, _ = network(own_noisy, own_full, own_half, teacher_down, teacher_up)
    loss_scale = jnp.float32(1.0 / (tile_count * dp_count * fsdp_count))
    flipped = flip_kernel(student_up)
    d_out, d_hidden = cotangents(
        student, target, adv_grad, own_full, own_half, flipped, cached, loss_scale
    )
    local_down = kernel_grad(cached[0], d_hidden, 2)
    local_up = kernel_grad(cached[5], d_out, 1)
    grad_down, grad_up = reduce_gradients(local_down, local_up, dp_count, fsdp_count)
    return (student, grad_down, grad_up)


def solution(mesh):
    return jax.shard_map(
        on_device,
        mesh=mesh,
        in_specs=(
            P(("dp", "fsdp"), None, None, None),
            P(("dp", "fsdp"), None, None, None),
            P(("dp", "fsdp")),
            P(("dp", "fsdp")),
            P(("dp", "fsdp")),
            P(("dp", "fsdp"), None, None, None),
            P("fsdp", None),
            P("fsdp", None),
            P("fsdp", None),
            P("fsdp", None),
        ),
        out_specs=(P(("dp", "fsdp"), None, None, None), P("fsdp", None), P("fsdp", None)),
        check_vma=False,
    )
```

```python
import jax
import jax.numpy as jnp
from jax import lax
from jax.sharding import PartitionSpec as P

GROUPS = 32
TSTEPS = 1000


distill_weight = 2.5
norm_epsilon = 1e-05


def conv_forward(volume, kernel_rows, stride):
    in_chan = volume.shape[3]
    kernel = kernel_rows.reshape(3, 3, in_chan, kernel_rows.shape[1])
    return lax.conv_general_dilated(
        volume,
        kernel,
        (stride, stride),
        ((1, 1), (1, 1)),
        dimension_numbers=("NHWC", "HWIO", "NHWC"),
        preferred_element_type=jnp.float32,
    )


def kernel_grad(volume, cotangent, stride):
    pad_upper = 1 if stride == 1 else 0
    result_grad = lax.conv_general_dilated(
        volume,
        cotangent,
        (1, 1),
        ((1, pad_upper), (1, pad_upper)),
        rhs_dilation=(stride, stride),
        dimension_numbers=("CHWN", "IHWO", "HWNC"),
        preferred_element_type=jnp.float32,
    )
    return result_grad.reshape(9 * volume.shape[3], cotangent.shape[3])


def width_masks(buckets, tile_side):
    half_side = tile_side // 2
    tile_count = buckets.shape[0]
    columns = jnp.arange(tile_side, dtype=jnp.int32)
    full_mask = (
        columns[None, None, :, None] < (tile_side - 2 * buckets)[:, None, None, None]
    ).astype(jnp.float32)
    full_mask = jnp.broadcast_to(full_mask, (tile_count, tile_side, tile_side, 1))
    half_cols = jnp.arange(half_side, dtype=jnp.int32)
    half_mask = (
        half_cols[None, None, :, None] < (half_side - buckets)[:, None, None, None]
    ).astype(jnp.float32)
    half_mask = jnp.broadcast_to(half_mask, (tile_count, half_side, half_side, 1))
    return (full_mask, half_mask)


def group_stats(hidden, half_mask):
    tile_count, height, breadth, channels = hidden.shape
    grouped = hidden.reshape(tile_count, height * breadth, GROUPS, channels // GROUPS)
    live_weight = half_mask.reshape(tile_count, height * breadth, 1, 1)
    population = jnp.sum(live_weight, axis=(1, 3), keepdims=True) * (channels // GROUPS)
    center = jnp.sum(grouped * live_weight, axis=(1, 3), keepdims=True) / population
    spread = (
        jnp.sum(jnp.square(grouped - center) * live_weight, axis=(1, 3), keepdims=True) / population
    )
    inverse = lax.rsqrt(spread + norm_epsilon)
    normed = ((grouped - center) * inverse).reshape(hidden.shape)
    return (normed, inverse, population)


def group_back(d_norm, normed, inverse, population, half_mask):
    tile_count, height, breadth, channels = d_norm.shape
    grouped_d = d_norm.reshape(tile_count, height * breadth, GROUPS, channels // GROUPS)
    grouped_n = normed.reshape(tile_count, height * breadth, GROUPS, channels // GROUPS)
    live_weight = half_mask.reshape(tile_count, height * breadth, 1, 1)
    mean_first = jnp.sum(grouped_d, axis=(1, 3), keepdims=True) / population
    mean_second = jnp.sum(grouped_d * grouped_n, axis=(1, 3), keepdims=True) / population
    result = live_weight * inverse * (grouped_d - mean_first - grouped_n * mean_second)
    return result.reshape(d_norm.shape)


def upsample(activated):
    return jnp.repeat(jnp.repeat(activated, 2, axis=1), 2, axis=2)


def network(noisy, full_mask, half_mask, down_weight, up_weight):
    hidden = conv_forward(noisy, down_weight, 2)
    normed, inverse, population = group_stats(hidden, half_mask)
    activated = (half_mask * jax.nn.silu(normed)).astype(jnp.bfloat16)
    enlarged = upsample(activated)
    output = conv_forward(enlarged, up_weight, 1)
    student = (full_mask * (noisy.astype(jnp.float32) + output)).astype(jnp.bfloat16)
    return (student, (noisy, normed, inverse, population, activated, enlarged))


def flip_kernel(up_weight):
    up_chan = up_weight.shape[0] // 9
    out_chan = up_weight.shape[1]
    return (
        up_weight.reshape(3, 3, up_chan, out_chan)[::-1, ::-1]
        .transpose(0, 1, 3, 2)
        .reshape(9 * out_chan, up_chan)
    )


def cotangents(student, target, adversarial, full_mask, half_mask, flipped, cached, loss_scale):
    source_in, normed, inverse, population, activated, enlarged = cached
    tile_count, tile_side = (student.shape[0], student.shape[1])
    half_side = tile_side // 2
    d_out = (
        full_mask
        * (
            distill_weight * (student.astype(jnp.float32) - target.astype(jnp.float32))
            + adversarial.astype(jnp.float32)
        )
        * loss_scale
    ).astype(jnp.bfloat16)
    d_up = conv_forward(d_out, flipped, 1)
    d_up = d_up.reshape(tile_count, half_side, 2, half_side, 2, flipped.shape[1])
    d_act = jnp.sum(d_up, axis=(2, 4))
    sigmoid_n = jax.nn.sigmoid(normed)
    d_norm = half_mask * d_act * sigmoid_n * (1.0 + normed * (1.0 - sigmoid_n))
    d_hidden = group_back(d_norm, normed, inverse, population, half_mask).astype(jnp.bfloat16)
    return (d_out, d_hidden)


def ring_gather(shards, dp_count, fsdp_count):
    fsdp_at = lax.axis_index("fsdp")
    core = lax.axis_index("dp") % 2
    step = 1 - 2 * core

    def lin(d, f):
        return d * fsdp_count + f

    ring_pairs = []
    for d in range(dp_count):
        toward = -1 if d % 2 == 0 else 1
        for f in range(fsdp_count):
            ring_pairs.append((lin(d, f), lin(d, (f + toward) % fsdp_count)))
    first = lax.ppermute(shards, ("dp", "fsdp"), ring_pairs)
    halves = tuple(
        lax.dynamic_slice_in_dim(piece, core * (piece.shape[0] // 2), piece.shape[0] // 2, axis=0)
        for piece in first
    )
    second = lax.ppermute(halves, ("dp", "fsdp"), ring_pairs)
    swap_pairs = [(d, d ^ 1) for d in range(dp_count)]
    other_first, other_second = lax.ppermute((first, second), "dp", swap_pairs)
    near = (fsdp_at + step + fsdp_count) % fsdp_count
    behind = (fsdp_at - step + fsdp_count) % fsdp_count
    far = (fsdp_at + 2) % fsdp_count
    gathered = []
    for own, got, got_other, half, half_other in zip(shards, first, other_first, second, other_second):
        rows = own.shape[0]
        full = jnp.zeros((fsdp_count * rows,) + own.shape[1:], own.dtype)
        full = lax.dynamic_update_slice_in_dim(full, own, fsdp_at * rows, axis=0)
        full = lax.dynamic_update_slice_in_dim(full, got, near * rows, axis=0)
        full = lax.dynamic_update_slice_in_dim(full, got_other, behind * rows, axis=0)
        full = lax.dynamic_update_slice_in_dim(full, half, far * rows + core * (rows // 2), axis=0)
        full = lax.dynamic_update_slice_in_dim(
            full, half_other, far * rows + (1 - core) * (rows // 2), axis=0
        )
        gathered.append(full)
    return tuple(gathered)


def gather_pair(down_rows, up_rows, dp_count, fsdp_count):
    if fsdp_count != 4 or dp_count % 2 or down_rows.shape[0] % 2 or up_rows.shape[0] % 2:
        return (
            lax.all_gather(down_rows, "fsdp", axis=0, tiled=True),
            lax.all_gather(up_rows, "fsdp", axis=0, tiled=True),
        )
    return ring_gather((down_rows, up_rows), dp_count, fsdp_count)


def coordinate_pairs(dp_count, fsdp_count, moved, shift):
    sizes = {"x": dp_count // 8, "z": 4, "core": 2, "y": fsdp_count}
    pairs = []
    for d in range(dp_count):
        for f in range(fsdp_count):
            place = {"x": d // 8, "z": (d // 2) % 4, "core": d % 2, "y": f}
            place[moved] = (place[moved] + shift) % sizes[moved]
            target = (place["x"] * 8 + place["z"] * 2 + place["core"]) * fsdp_count + place["y"]
            pairs.append((d * fsdp_count + f, target))
    return pairs


def scatter_sum(parts, at, count, pairs_of, axis=0):
    total = lax.dynamic_index_in_dim(parts, at, axis=axis, keepdims=False).astype(jnp.float32)
    for k in range(1, count):
        sent = lax.dynamic_index_in_dim(parts, (at + k) % count, axis=axis, keepdims=False)
        got = lax.ppermute(sent.astype(jnp.bfloat16), ("dp", "fsdp"), pairs_of(k))
        total = total + got.astype(jnp.float32)
    return total


def gather_blocks(block, at, count, pairs_of):
    full = jnp.zeros((count,) + block.shape, block.dtype)
    full = lax.dynamic_update_index_in_dim(full, block, at, axis=0)
    for k in range(1, count):
        got = lax.ppermute(block, ("dp", "fsdp"), pairs_of(k))
        full = lax.dynamic_update_index_in_dim(full, got, (at - k + count) % count, axis=0)
    return full


def reduce_gradients(local_down, local_up, dp_count, fsdp_count):
    d = lax.axis_index("dp")
    at = {"x": d // 8, "z": (d // 2) % 4, "core": d % 2, "y": lax.axis_index("fsdp")}
    sizes = {"x": dp_count // 8, "z": 4, "core": 2, "y": fsdp_count}
    down_size = local_down.size // fsdp_count
    chunk = 2 * down_size // (2 * sizes["x"] * sizes["z"])
    if dp_count != 32 or fsdp_count != 4 or chunk % 2:
        shard_down = lax.psum_scatter(local_down.astype(jnp.bfloat16), "fsdp", scatter_dimension=0, tiled=True)
        shard_up = lax.psum_scatter(local_up.astype(jnp.bfloat16), "fsdp", scatter_dimension=0, tiled=True)
        return (
            lax.psum(shard_down, "dp").astype(jnp.float32),
            lax.psum(shard_up, "dp").astype(jnp.float32),
        )
    table = jnp.concatenate(
        [
            local_down.astype(jnp.bfloat16).reshape(fsdp_count, down_size),
            local_up.astype(jnp.bfloat16).reshape(fsdp_count, down_size),
        ],
        axis=1,
    ).reshape(fsdp_count, 2, sizes["x"], sizes["z"], chunk)

    def pairs(moved):
        return lambda k: coordinate_pairs(dp_count, fsdp_count, moved, k)

    halves = jnp.moveaxis(table, 1, 0)
    part = scatter_sum(halves, at["core"], 2, pairs("core"))
    colour = chunk // 2
    done = []
    for c, order in enumerate((("y", "x"), ("x", "y"))):
        piece = part[..., c * colour:(c + 1) * colour]
        left = ["y", "x", "z"]
        for name in order:
            piece = scatter_sum(piece, at[name], sizes[name], pairs(name), axis=left.index(name))
            left.remove(name)
        done.append(piece)
    part = jnp.concatenate(done, axis=-1)
    part = scatter_sum(part, at["z"], sizes["z"], pairs("z"))
    part = gather_blocks(part.astype(jnp.bfloat16), at["z"], sizes["z"], pairs("z"))
    part = gather_blocks(part, at["x"], sizes["x"], pairs("x"))
    part = gather_blocks(part, at["core"], 2, pairs("core"))
    flat = part.reshape(-1).astype(jnp.float32)
    return (
        flat[:down_size].reshape(local_down.shape[0] // fsdp_count, local_down.shape[1]),
        flat[down_size:].reshape(local_up.shape[0] // fsdp_count, local_up.shape[1]),
    )


def on_device(
    latents, noise_draw, timesteps, buckets, owners, adv_grad, w_down, w_up, t_down, t_up
):
    tile_count, tile_side = (latents.shape[0], latents.shape[1])
    dp_count = lax.axis_size("dp")
    fsdp_count = lax.axis_size("fsdp")
    full_mask, half_mask = width_masks(buckets, tile_side)
    alpha_bar = jnp.square(jnp.cos(0.5 * jnp.pi * (timesteps.astype(jnp.float32) + 0.5) / TSTEPS))
    noisy = (
        full_mask
        * (
            jnp.sqrt(alpha_bar)[:, None, None, None] * latents.astype(jnp.float32)
            + jnp.sqrt(1.0 - alpha_bar)[:, None, None, None] * noise_draw.astype(jnp.float32)
        )
    ).astype(jnp.bfloat16)
    peer_cap = max(2, (tile_count + dp_count - 1) // dp_count)
    slot_count = dp_count * peer_cap
    hit_table = (owners[:, None] == jnp.arange(dp_count, dtype=jnp.int32)[None, :]).astype(
        jnp.int32
    )
    before = jnp.cumsum(hit_table, axis=0) - hit_table
    slot_of = owners * peer_cap + jnp.sum(before * hit_table, axis=1)
    slot_hits = slot_of[None, :] == jnp.arange(slot_count, dtype=jnp.int32)[:, None]
    spread_matrix = slot_hits.astype(jnp.bfloat16)
    send_noisy = (
        jnp.dot(spread_matrix, noisy.reshape(tile_count, -1), preferred_element_type=jnp.float32)
        .astype(jnp.bfloat16)
        .reshape(dp_count, peer_cap, -1)
    )
    send_code = jnp.sum(jnp.where(slot_hits, buckets[None, :] + 1, 0), axis=1).reshape(
        dp_count, peer_cap
    )
    packed = jnp.concatenate(
        [send_noisy, jnp.broadcast_to(send_code[..., None], send_code.shape + (128,)).astype(jnp.bfloat16)],
        axis=-1,
    )
    received = lax.all_to_all(packed, "dp", split_axis=0, concat_axis=0, tiled=True)
    recv_noisy = received[..., :-128]
    recv_code = received[..., -1].astype(jnp.int32)
    flat_code = recv_code.reshape(slot_count)
    live_slot = (flat_code > 0).astype(jnp.int32)
    position = jnp.cumsum(live_slot) - live_slot
    pick_hits = (live_slot[None, :] == 1) & (
        position[None, :] == jnp.arange(tile_count, dtype=jnp.int32)[:, None]
    )
    pick_matrix = pick_hits.astype(jnp.bfloat16)
    own_noisy = (
        jnp.dot(pick_matrix, recv_noisy.reshape(slot_count, -1), preferred_element_type=jnp.float32)
        .astype(jnp.bfloat16)
        .reshape(latents.shape)
    )
    own_buckets = jnp.sum(jnp.where(pick_hits, flat_code[None, :] - 1, 0), axis=1).astype(jnp.int32)
    own_full, own_half = width_masks(own_buckets, tile_side)
    student_down, student_up = gather_pair(w_down, w_up, dp_count, fsdp_count)
    t_down, t_up, _, _ = lax.optimization_barrier((t_down, t_up, student_down, student_up))
    teacher_down, teacher_up = gather_pair(t_down, t_up, dp_count, fsdp_count)
    student, cached = network(own_noisy, own_full, own_half, student_down, student_up)
    target, _ = network(own_noisy, own_full, own_half, teacher_down, teacher_up)
    loss_scale = jnp.float32(1.0 / (tile_count * dp_count * fsdp_count))
    flipped = flip_kernel(student_up)
    d_out, d_hidden = cotangents(
        student, target, adv_grad, own_full, own_half, flipped, cached, loss_scale
    )
    local_down = kernel_grad(cached[0], d_hidden, 2)
    local_up = kernel_grad(cached[5], d_out, 1)
    grad_down, grad_up = reduce_gradients(local_down, local_up, dp_count, fsdp_count)
    return (student, grad_down, grad_up)


def solution(mesh):
    return jax.shard_map(
        on_device,
        mesh=mesh,
        in_specs=(
            P(("dp", "fsdp"), None, None, None),
            P(("dp", "fsdp"), None, None, None),
            P(("dp", "fsdp")),
            P(("dp", "fsdp")),
            P(("dp", "fsdp")),
            P(("dp", "fsdp"), None, None, None),
            P("fsdp", None),
            P("fsdp", None),
            P("fsdp", None),
            P("fsdp", None),
        ),
        out_specs=(P(("dp", "fsdp"), None, None, None), P("fsdp", None), P("fsdp", None)),
        check_vma=False,
    )
```
